32 devices in a mesh: ang: 8 (over z, core), row: 4 (over y, x).
Axes of the slice: x: 2, y: 2, z: 4, core: 2. Of those that a mesh axis runs over, the one named last changes fastest.
Arguments:
- panels: bfloat16 [4, 32, 64, 2, 128], P('row', None, 'ang'), may hold values from -6 to 6
- panel_slot: int32 [4, 32], P('row'), may hold values from 0 to 15
- panel_cell: int32 [4, 32, 2], P('row'), may hold values from 0 to 15
- bloch_k: float32 [8, 2], replicated, may hold values from -3.140625 to 3.140625
- leaf_inverse: bfloat16 [8, 2, 8192, 256], P('ang', None, 'row'), may hold values from -0.25 to 0.25
- level_left: bfloat16 [8, 3, 2, 32, 8192], P('ang', None, None, None, 'row'), may hold values from -0.75 to 0.75
- level_right: bfloat16 [8, 3, 2, 32, 8192], P('ang', None, None, None, 'row'), may hold values from -0.125 to 0.125
- block_left: bfloat16 [8, 2, 32, 8192], P('ang', None, None, 'row'), may hold values from -0.75 to 0.75
- block_right: bfloat16 [8, 2, 32, 8192], P('ang', None, None, 'row'), may hold values from -0.09375 to 0.09375
- block_coupling: bfloat16 [8, 4, 2, 32, 128], P('ang', 'row'), may hold values from -0.375 to 0.375
- rank_count: int32 [8, 4], P('ang', 'row'), may hold values from 16 to 32
- quad_weight: float32 [8, 2], P('ang'), may hold values from -2 to 2
Outputs:
- response: float32 [64, 2, 8192], P('ang', None, 'row')
The draws below stay inside these ranges and needn't reach their ends.
All inputs are finite; a program needn't handle non-finite values.
Results may differ from the reference program's by a relative error of at most 0.0045.
Values may be sent and summed in bfloat16 or wider, within the bound.
No kernel may reach another device: no remote copies, remote signals or barrier semaphores. Data moves between devices by JAX's collectives and lax.ppermute only.
A program may use at most 64 MiB of HBM per device.

```python
import jax
import jax.numpy as jnp
from jax import lax

LEAF = 256
LOCAL_LEVELS = 3
ROWS_DEV = 2048
BLOCKS = 4
ORDER = 8192
PANEL = 128
SLOTS = 16
PANELS_B = 32
NSRC = 64
RL = 32
RC = 32
SIDE = 16
ANGLES = 8


def with_ends(drawn, key, low, high):
    place = [jax.random.randint(jax.random.fold_in(key, axis), (), 0, length) for axis, length in enumerate(drawn.shape)]
    main_axis = drawn.shape.index(max(drawn.shape))
    beside = place[:main_axis] + [(place[main_axis] + 1) % drawn.shape[main_axis]] + place[main_axis + 1:]
    return drawn.at[tuple(place)].set(low).at[tuple(beside)].set(high)


def block_scale(key, extent, shards, low, top_value):
    factor_of = 1.0
    for dim, blocks in shards:
        heights = jax.random.uniform(jax.random.fold_in(jax.random.fold_in(key, 6), dim), (blocks,), jnp.float32, low / len(shards), top_value / len(shards))
        factor_of = factor_of * jnp.repeat(jnp.exp(heights), extent[dim] // blocks).reshape((-1,) + (1,) * (len(extent) - 1 - dim))
    return factor_of


def normal_values(rng, extent, spread, most, pieces=(), kind=jnp.bfloat16):
    entries = spread * jax.random.normal(rng, extent, jnp.float32)
    if pieces:
        entries = entries * block_scale(rng, extent, pieces, -0.22, 0.18)
    return jnp.clip(entries, -most, most).astype(kind)


def setup_inputs(seed: int = 0) -> dict:
    key_of = jax.random.split(jax.random.key(seed), 13)
    return {
        "panels": normal_values(key_of[0], (BLOCKS, PANELS_B, NSRC, 2, PANEL), 1.0, 6.0, ((0, 4), (2, 8))),
        "panel_slot": with_ends(jax.random.randint(key_of[1], (BLOCKS, PANELS_B), 0, SLOTS), jax.random.fold_in(key_of[1], 1), 0, SLOTS - 1).astype(jnp.int32),
        "panel_cell": with_ends(jax.random.randint(key_of[2], (BLOCKS, PANELS_B, 2), 0, SIDE), jax.random.fold_in(key_of[2], 1), 0, SIDE - 1).astype(jnp.int32),
        "bloch_k": jnp.clip(jax.random.uniform(key_of[3], (ANGLES, 2), jnp.float32, -3.140625, 3.140625), -3.140625, 3.140625),
        "leaf_inverse": normal_values(key_of[4], (ANGLES, 2, ORDER, LEAF), (2 * LEAF) ** -0.5, 0.25, ((0, 8), (2, 4))),
        "level_left": normal_values(key_of[5], (ANGLES, LOCAL_LEVELS, 2, RL, ORDER), (2 * RL) ** -0.5, 0.75, ((0, 8), (4, 4))),
        "level_right": normal_values(key_of[6], (ANGLES, LOCAL_LEVELS, 2, RL, ORDER), ROWS_DEV ** -0.5, 0.125, ((0, 8), (4, 4))),
        "block_left": normal_values(key_of[7], (ANGLES, 2, RC, ORDER), (2 * RC) ** -0.5, 0.75, ((0, 8), (3, 4))),
        "block_right": normal_values(key_of[8], (ANGLES, 2, RC, ORDER), (2 * ROWS_DEV) ** -0.5, 0.09375, ((0, 8), (3, 4))),
        "block_coupling": normal_values(key_of[9], (ANGLES, BLOCKS, 2, RC, BLOCKS * RC), (2 * BLOCKS * RC) ** -0.5, 0.375, ((0, 8), (1, 4))),
        "rank_count": with_ends(jax.random.randint(key_of[10], (ANGLES, BLOCKS), RC // 2, RC + 1), jax.random.fold_in(key_of[10], 1), RC // 2, RC).astype(jnp.int32),
        "quad_weight": normal_values(key_of[11], (ANGLES, 2), ANGLES ** -0.5, 2.0, ((0, 8),), jnp.float32),
    }


def complex_product(form, left_real, left_imag, right_real, right_imag):
    def single(first, second):
        return jnp.einsum(form, first.astype(jnp.float32), second.astype(jnp.float32))
    return (single(left_real, right_real) - single(left_imag, right_imag),
            single(left_real, right_imag) + single(left_imag, right_real))


def near_field(excite, leaf_block, right_factors, left_factors):
    source_count = excite.shape[0]
    row_count = excite.shape[2]
    leaf_count = row_count // LEAF
    gathered_groups = excite.reshape(source_count, 2, leaf_count, LEAF)
    real_part, imag_part = complex_product(
        "lwv,slv->slw",
        leaf_block[0].reshape(leaf_count, LEAF, LEAF),
        leaf_block[1].reshape(leaf_count, LEAF, LEAF),
        gathered_groups[:, 0], gathered_groups[:, 1])
    real_part = real_part.reshape(source_count, row_count)
    imag_part = imag_part.reshape(source_count, row_count)
    for tree_level_index in range(LOCAL_LEVELS):
        node_size = ROWS_DEV // 2 ** (tree_level_index + 1)
        groups = row_count // node_size
        node_view = excite.reshape(source_count, 2, groups, node_size)
        right_real = right_factors[tree_level_index, 0].reshape(RL, groups, node_size)
        right_imag = right_factors[tree_level_index, 1].reshape(RL, groups, node_size)
        proj_real, proj_imag = complex_product("rgm,sgm->sgr", right_real, right_imag, node_view[:, 0], node_view[:, 1])
        projected = jnp.stack([proj_real, proj_imag], 1).astype(jnp.bfloat16)
        swapped = projected.reshape(source_count, 2, groups // 2, 2, RL)[:, :, :, ::-1].reshape(source_count, 2, groups, RL)
        left_real = left_factors[tree_level_index, 0].reshape(RL, groups, node_size)
        left_imag = left_factors[tree_level_index, 1].reshape(RL, groups, node_size)
        add_real, add_imag = complex_product("rgm,sgr->sgm", left_real, left_imag, swapped[:, 0], swapped[:, 1])
        real_part = real_part + add_real.reshape(source_count, row_count)
        imag_part = imag_part + add_imag.reshape(source_count, row_count)
    return real_part, imag_part


def reference(panels, panel_slot, panel_cell, bloch_k, leaf_inverse, level_left, level_right, block_left, block_right, block_coupling, rank_count, quad_weight):
    slot_count = ROWS_DEV // PANEL
    onehot = (panel_slot[:, :, None] == jnp.arange(slot_count, dtype=jnp.int32)[None, None, :]).astype(jnp.bfloat16)
    cell_float = panel_cell.astype(jnp.float32)
    panel_real = panels[:, :, :, 0, :].astype(jnp.float32)
    panel_imag = panels[:, :, :, 1, :].astype(jnp.float32)
    block_numbers = jnp.arange(BLOCKS, dtype=jnp.int32)
    keep_other = (block_numbers[:, None] != block_numbers[None, :]).astype(jnp.bfloat16)
    rank_iota = jnp.arange(RC, dtype=jnp.int32)

    def one_angle(summed, angle_index):
        theta = bloch_k[angle_index, 0] * cell_float[:, :, 0] + bloch_k[angle_index, 1] * cell_float[:, :, 1]
        phase_cosine = jnp.cos(theta).astype(jnp.bfloat16)
        phase_sin = jnp.sin(theta).astype(jnp.bfloat16)
        coef_cos = (phase_cosine[:, :, None] * onehot).astype(jnp.float32)
        coef_sin = (phase_sin[:, :, None] * onehot).astype(jnp.float32)

        def assemble(coefficient, entry_values):
            return jnp.einsum("afx,afnl->naxl", coefficient, entry_values)

        real_part = assemble(coef_cos, panel_real) + assemble(coef_sin, panel_imag)
        imag_part = assemble(coef_cos, panel_imag) - assemble(coef_sin, panel_real)
        excite = jnp.stack([real_part, imag_part], 1).reshape(NSRC, 2, ORDER).astype(jnp.bfloat16)
        near_real, near_imag = near_field(excite, leaf_inverse[angle_index], level_right[angle_index], level_left[angle_index])
        rank_mask = (rank_iota[None, :] < rank_count[angle_index][:, None]).astype(jnp.bfloat16)
        right_block = block_right[angle_index].reshape(2, RC, BLOCKS, ROWS_DEV) * rank_mask.T[None, :, :, None]
        block_view = excite.reshape(NSRC, 2, BLOCKS, ROWS_DEV)
        proj_real, proj_imag = complex_product("rjm,sjm->sjr", right_block[0], right_block[1], block_view[:, 0], block_view[:, 1])
        projected = jnp.stack([proj_real, proj_imag], 1).astype(jnp.bfloat16)
        coupling = block_coupling[angle_index].reshape(BLOCKS, 2, RC, BLOCKS, RC) * keep_other[:, None, None, :, None]
        coup_real, coup_imag = complex_product("irjq,sjq->sir", coupling[:, 0], coupling[:, 1], projected[:, 0], projected[:, 1])
        coupled = jnp.stack([coup_real, coup_imag], 1).astype(jnp.bfloat16)
        left_block = block_left[angle_index].reshape(2, RC, BLOCKS, ROWS_DEV) * rank_mask.T[None, :, :, None]
        far_real, far_imag = complex_product("rim,sir->sim", left_block[0], left_block[1], coupled[:, 0], coupled[:, 1])
        field_real = near_real + far_real.reshape(NSRC, ORDER)
        field_imag = near_imag + far_imag.reshape(NSRC, ORDER)
        weight_real = quad_weight[angle_index, 0]
        weight_imag = quad_weight[angle_index, 1]
        term = jnp.stack([weight_real * field_real - weight_imag * field_imag,
                          weight_real * field_imag + weight_imag * field_real], 1)
        return summed + term, None

    start_total = jnp.zeros((NSRC, 2, ORDER), jnp.float32)
    response, unused_out = lax.scan(one_angle, start_total, jnp.arange(ANGLES, dtype=jnp.int32))
    return response
```

```python
import jax
import jax.numpy as jnp
from jax import lax
from jax.experimental import pallas as pl
from jax.experimental.pallas import tpu as pltpu
from jax.sharding import PartitionSpec as P

LEAF = 256

_SMEM = pl.BlockSpec(memory_space=pltpu.MemorySpace.SMEM)
_VMEM = pl.BlockSpec(memory_space=pltpu.MemorySpace.VMEM)


def _nt(a, b):
    return lax.dot_general(a, b, (((1,), (1,)), ((), ())), preferred_element_type=jnp.float32)


def _nn(a, b):
    return lax.dot_general(a, b, (((1,), (0,)), ((), ())), preferred_element_type=jnp.float32)


def _rank_mask(rank_ref, shape):
    return lax.broadcasted_iota(jnp.int32, shape, 0) < rank_ref[0]


def _excite_kernel(slot_ref, cos_ref, sin_ref, rank_ref, g_ref, br_ref, e_ref, bp_ref, acc_re, acc_im):
    panel_count, _, width2 = g_ref.shape
    width = width2 // 2
    slots = acc_re.shape[0]
    acc_re[...] = jnp.zeros(acc_re.shape, jnp.float32)
    acc_im[...] = jnp.zeros(acc_im.shape, jnp.float32)

    def body(q, carry):
        k = slot_ref[q]
        c = cos_ref[q]
        s = sin_ref[q]
        p_re = g_ref[q, :, :width].astype(jnp.float32)
        p_im = g_ref[q, :, width:].astype(jnp.float32)
        acc_re[k] = acc_re[k] + (c * p_re + s * p_im)
        acc_im[k] = acc_im[k] + (c * p_im - s * p_re)
        return carry

    lax.fori_loop(0, panel_count, body, 0)
    for k in range(slots):
        e_ref[0, :, k * width:(k + 1) * width] = acc_re[k].astype(jnp.bfloat16)
        e_ref[1, :, k * width:(k + 1) * width] = acc_im[k].astype(jnp.bfloat16)
    e_re = e_ref[0]
    e_im = e_ref[1]
    keep = _rank_mask(rank_ref, br_ref.shape[1:])
    zero = jnp.zeros(br_ref.shape[1:], jnp.bfloat16)
    r_re = jnp.where(keep, br_ref[0], zero)
    r_im = jnp.where(keep, br_ref[1], zero)
    bp_ref[0] = (_nt(e_re, r_re) - _nt(e_im, r_im)).astype(jnp.bfloat16)
    bp_ref[1] = (_nt(e_re, r_im) + _nt(e_im, r_re)).astype(jnp.bfloat16)


def _field_kernel(qw_ref, rank_ref, me_ref, e_ref, leaf_ref, lr_ref, ll_ref, bl_ref, cp_ref, bpa_ref, out_ref):
    _, source_count, row_count = e_ref.shape
    levels = lr_ref.shape[0]
    rank_width = lr_ref.shape[2]
    blocks = bpa_ref.shape[0]
    coupling_rank = bpa_ref.shape[3]
    e_re = e_ref[0]
    e_im = e_ref[1]

    projections = []
    for j in range(levels):
        node = row_count // 2 ** (j + 1)
        level_proj = []
        for g in range(2 ** (j + 1)):
            cols = slice(g * node, (g + 1) * node)
            a = e_re[:, cols]
            b = e_im[:, cols]
            r_re = lr_ref[j, 0, :, cols]
            r_im = lr_ref[j, 1, :, cols]
            p_re = (_nt(a, r_re) - _nt(b, r_im)).astype(jnp.bfloat16)
            p_im = (_nt(a, r_im) + _nt(b, r_re)).astype(jnp.bfloat16)
            level_proj.append((p_re, p_im))
        projections.append(level_proj)

    me = me_ref[0]
    c_re = jnp.zeros((source_count, rank_width), jnp.float32)
    c_im = jnp.zeros((source_count, rank_width), jnp.float32)
    for u in range(blocks):
        own = me == u
        zero = jnp.zeros((source_count, coupling_rank), jnp.bfloat16)
        b_re = jnp.where(own, zero, bpa_ref[u, 0])
        b_im = jnp.where(own, zero, bpa_ref[u, 1])
        k_re = cp_ref[0, :, u * coupling_rank:(u + 1) * coupling_rank]
        k_im = cp_ref[1, :, u * coupling_rank:(u + 1) * coupling_rank]
        c_re = c_re + (_nt(b_re, k_re) - _nt(b_im, k_im))
        c_im = c_im + (_nt(b_re, k_im) + _nt(b_im, k_re))
    coupled_re = c_re.astype(jnp.bfloat16)
    coupled_im = c_im.astype(jnp.bfloat16)

    w_re = qw_ref[0]
    w_im = qw_ref[1]
    for l in range(row_count // LEAF):
        cols = slice(l * LEAF, (l + 1) * LEAF)
        a = e_re[:, cols]
        b = e_im[:, cols]
        lf_re = leaf_ref[0, cols, :]
        lf_im = leaf_ref[1, cols, :]
        f_re = _nt(a, lf_re) - _nt(b, lf_im)
        f_im = _nt(a, lf_im) + _nt(b, lf_re)
        for j in range(levels):
            node = row_count // 2 ** (j + 1)
            g = (l * LEAF) // node
            p_re, p_im = projections[j][g ^ 1]
            m_re = ll_ref[j, 0, :, cols]
            m_im = ll_ref[j, 1, :, cols]
            f_re = f_re + (_nn(p_re, m_re) - _nn(p_im, m_im))
            f_im = f_im + (_nn(p_re, m_im) + _nn(p_im, m_re))
        keep = _rank_mask(rank_ref, (bl_ref.shape[1], LEAF))
        zero = jnp.zeros((bl_ref.shape[1], LEAF), jnp.bfloat16)
        q_re = jnp.where(keep, bl_ref[0, :, cols], zero)
        q_im = jnp.where(keep, bl_ref[1, :, cols], zero)
        f_re = f_re + (_nn(coupled_re, q_re) - _nn(coupled_im, q_im))
        f_im = f_im + (_nn(coupled_re, q_im) + _nn(coupled_im, q_re))
        out_ref[0, :, cols] = w_re * f_re - w_im * f_im
        out_ref[1, :, cols] = w_re * f_im + w_im * f_re


def shards(
    panels,
    panel_slot,
    panel_cell,
    bloch_k,
    leaf_inverse,
    level_left,
    level_right,
    block_left,
    block_right,
    block_coupling,
    rank_count,
    quad_weight,
):
    local_angles = leaf_inverse.shape[0]
    assert local_angles == 1
    row_count = leaf_inverse.shape[2]
    panel_count = panels.shape[1]
    local_sources = panels.shape[2]
    panel_width = panels.shape[4]
    slot_count = row_count // panel_width
    source_count = local_sources * lax.axis_size("ang")
    rank_width = block_right.shape[2]

    cell_float = panel_cell[0].astype(jnp.float32)
    own_wave = lax.dynamic_slice_in_dim(bloch_k, lax.axis_index("ang") * local_angles, local_angles, 0)
    theta = own_wave[0, 0] * cell_float[:, 0] + own_wave[0, 1] * cell_float[:, 1]
    own_cos = jnp.cos(theta).astype(jnp.bfloat16).astype(jnp.float32)
    own_sin = jnp.sin(theta).astype(jnp.bfloat16).astype(jnp.float32)

    local_panels = panels[0].reshape(panel_count, local_sources, 2 * panel_width)
    gathered = lax.all_gather(local_panels, "ang", axis=1, tiled=True)
    rank = rank_count[0].reshape(1)

    excitation, projected = pl.pallas_call(
        _excite_kernel,
        out_shape=(
            jax.ShapeDtypeStruct((2, source_count, row_count), jnp.bfloat16),
            jax.ShapeDtypeStruct((2, source_count, rank_width), jnp.bfloat16),
        ),
        in_specs=[_SMEM, _SMEM, _SMEM, _SMEM, _VMEM, _VMEM],
        out_specs=(_VMEM, _VMEM),
        scratch_shapes=[
            pltpu.VMEM((slot_count, source_count, panel_width), jnp.float32),
            pltpu.VMEM((slot_count, source_count, panel_width), jnp.float32),
        ],
    )(panel_slot[0], own_cos, own_sin, rank, gathered, block_right[0])

    all_projected = lax.all_gather(projected, "row", axis=0, tiled=False)
    me = lax.axis_index("row").astype(jnp.int32).reshape(1)

    field = pl.pallas_call(
        _field_kernel,
        out_shape=jax.ShapeDtypeStruct((2, source_count, row_count), jnp.float32),
        in_specs=[_SMEM, _SMEM, _SMEM] + [_VMEM] * 7,
        out_specs=_VMEM,
    )(
        quad_weight[0],
        rank,
        me,
        excitation,
        leaf_inverse[0],
        level_right[0],
        level_left[0],
        block_left[0],
        block_coupling[0, 0],
        all_projected,
    )
    summed = lax.psum_scatter(field, "ang", scatter_dimension=1, tiled=True)
    return jnp.transpose(summed, (1, 0, 2))


def solution(mesh):
    placed = (
        P("row", None, "ang", None, None),
        P("row", None),
        P("row", None, None),
        P(),
        P("ang", None, "row", None),
        P("ang", None, None, None, "row"),
        P("ang", None, None, None, "row"),
        P("ang", None, None, "row"),
        P("ang", None, None, "row"),
        P("ang", "row", None, None, None),
        P("ang", "row"),
        P("ang", None),
    )
    return jax.shard_map(
        shards, mesh=mesh, in_specs=placed, out_specs=P("ang", None, "row"), check_vma=False
    )
```

```python
import jax
import jax.numpy as jnp
from jax import lax
from jax.experimental import pallas as pl
from jax.experimental.pallas import tpu as pltpu
from jax.sharding import PartitionSpec as P

LEAF = 256

_SMEM = pl.BlockSpec(memory_space=pltpu.MemorySpace.SMEM)
_VMEM = pl.BlockSpec(memory_space=pltpu.MemorySpace.VMEM)


def _nt(a, b):
    return lax.dot_general(a, b, (((1,), (1,)), ((), ())), preferred_element_type=jnp.float32)


def _nn(a, b):
    return lax.dot_general(a, b, (((1,), (0,)), ((), ())), preferred_element_type=jnp.float32)


def _rank_mask(rank_ref, shape):
    return lax.broadcasted_iota(jnp.int32, shape, 0) < rank_ref[0]


def _excite_kernel(slot_ref, cos_ref, sin_ref, rank_ref, g_ref, br_ref, e_ref, bp_ref, acc_re, acc_im):
    panel_count, _, width2 = g_ref.shape
    width = width2 // 2
    slots = acc_re.shape[0]
    acc_re[...] = jnp.zeros(acc_re.shape, jnp.float32)
    acc_im[...] = jnp.zeros(acc_im.shape, jnp.float32)

    def body(q, carry):
        k = slot_ref[q]
        c = cos_ref[q]
        s = sin_ref[q]
        p_re = g_ref[q, :, :width].astype(jnp.float32)
        p_im = g_ref[q, :, width:].astype(jnp.float32)
        acc_re[k] = acc_re[k] + (c * p_re + s * p_im)
        acc_im[k] = acc_im[k] + (c * p_im - s * p_re)
        return carry

    lax.fori_loop(0, panel_count, body, 0)
    for k in range(slots):
        e_ref[0, :, k * width:(k + 1) * width] = acc_re[k].astype(jnp.bfloat16)
        e_ref[1, :, k * width:(k + 1) * width] = acc_im[k].astype(jnp.bfloat16)
    e_re = e_ref[0]
    e_im = e_ref[1]
    keep = _rank_mask(rank_ref, br_ref.shape[1:])
    zero = jnp.zeros(br_ref.shape[1:], jnp.bfloat16)
    r_re = jnp.where(keep, br_ref[0], zero)
    r_im = jnp.where(keep, br_ref[1], zero)
    bp_ref[0] = (_nt(e_re, r_re) - _nt(e_im, r_im)).astype(jnp.bfloat16)
    bp_ref[1] = (_nt(e_re, r_im) + _nt(e_im, r_re)).astype(jnp.bfloat16)


def _field_kernel(qw_ref, rank_ref, me_ref, e_ref, leaf_ref, lr_ref, ll_ref, bl_ref, cp_ref, bpa_ref, out_ref, pj_ref, cu_ref):
    _, source_count, row_count = e_ref.shape
    levels = lr_ref.shape[0]
    rank_width = lr_ref.shape[2]
    blocks = bpa_ref.shape[0]
    coupling_rank = bpa_ref.shape[3]
    e_re = e_ref[0]
    e_im = e_ref[1]

    first_group = []
    slot = 0
    for j in range(levels):
        node = row_count // 2 ** (j + 1)
        first_group.append(slot)
        for g in range(2 ** (j + 1)):
            cols = slice(g * node, (g + 1) * node)
            a = e_re[:, cols]
            b = e_im[:, cols]
            r_re = lr_ref[j, 0, :, cols]
            r_im = lr_ref[j, 1, :, cols]
            pj_ref[slot, 0] = (_nt(a, r_re) - _nt(b, r_im)).astype(jnp.bfloat16)
            pj_ref[slot, 1] = (_nt(a, r_im) + _nt(b, r_re)).astype(jnp.bfloat16)
            slot += 1

    me = me_ref[0]
    c_re = jnp.zeros((source_count, rank_width), jnp.float32)
    c_im = jnp.zeros((source_count, rank_width), jnp.float32)
    for u in range(blocks):
        own = me == u
        zero = jnp.zeros((source_count, coupling_rank), jnp.bfloat16)
        b_re = jnp.where(own, zero, bpa_ref[u, 0])
        b_im = jnp.where(own, zero, bpa_ref[u, 1])
        k_re = cp_ref[0, :, u * coupling_rank:(u + 1) * coupling_rank]
        k_im = cp_ref[1, :, u * coupling_rank:(u + 1) * coupling_rank]
        c_re = c_re + (_nt(b_re, k_re) - _nt(b_im, k_im))
        c_im = c_im + (_nt(b_re, k_im) + _nt(b_im, k_re))
    cu_ref[0] = c_re.astype(jnp.bfloat16)
    cu_ref[1] = c_im.astype(jnp.bfloat16)
    coupled_re = cu_ref[0]
    coupled_im = cu_ref[1]

    w_re = qw_ref[0]
    w_im = qw_ref[1]
    for l in range(row_count // LEAF):
        cols = slice(l * LEAF, (l + 1) * LEAF)
        a = e_re[:, cols]
        b = e_im[:, cols]
        lf_re = leaf_ref[0, cols, :]
        lf_im = leaf_ref[1, cols, :]
        f_re = _nt(a, lf_re) - _nt(b, lf_im)
        f_im = _nt(a, lf_im) + _nt(b, lf_re)
        for j in range(levels):
            node = row_count // 2 ** (j + 1)
            g = (l * LEAF) // node
            p_re = pj_ref[first_group[j] + (g ^ 1), 0]
            p_im = pj_ref[first_group[j] + (g ^ 1), 1]
            m_re = ll_ref[j, 0, :, cols]
            m_im = ll_ref[j, 1, :, cols]
            f_re = f_re + (_nn(p_re, m_re) - _nn(p_im, m_im))
            f_im = f_im + (_nn(p_re, m_im) + _nn(p_im, m_re))
        keep = _rank_mask(rank_ref, (bl_ref.shape[1], LEAF))
        zero = jnp.zeros((bl_ref.shape[1], LEAF), jnp.bfloat16)
        q_re = jnp.where(keep, bl_ref[0, :, cols], zero)
        q_im = jnp.where(keep, bl_ref[1, :, cols], zero)
        f_re = f_re + (_nn(coupled_re, q_re) - _nn(coupled_im, q_im))
        f_im = f_im + (_nn(coupled_re, q_im) + _nn(coupled_im, q_re))
        out_ref[0, :, cols] = w_re * f_re - w_im * f_im
        out_ref[1, :, cols] = w_re * f_im + w_im * f_re


def shards(
    panels,
    panel_slot,
    panel_cell,
    bloch_k,
    leaf_inverse,
    level_left,
    level_right,
    block_left,
    block_right,
    block_coupling,
    rank_count,
    quad_weight,
):
    local_angles = leaf_inverse.shape[0]
    assert local_angles == 1
    row_count = leaf_inverse.shape[2]
    panel_count = panels.shape[1]
    local_sources = panels.shape[2]
    panel_width = panels.shape[4]
    slot_count = row_count // panel_width
    source_count = local_sources * lax.axis_size("ang")
    rank_width = block_right.shape[2]
    levels = level_right.shape[1]

    cell_float = panel_cell[0].astype(jnp.float32)
    own_wave = lax.dynamic_slice_in_dim(bloch_k, lax.axis_index("ang") * local_angles, local_angles, 0)
    theta = own_wave[0, 0] * cell_float[:, 0] + own_wave[0, 1] * cell_float[:, 1]
    own_cos = jnp.cos(theta).astype(jnp.bfloat16).astype(jnp.float32)
    own_sin = jnp.sin(theta).astype(jnp.bfloat16).astype(jnp.float32)

    local_panels = panels[0].reshape(panel_count, local_sources, 2 * panel_width)
    gathered = lax.all_gather(local_panels, "ang", axis=1, tiled=True)
    rank = rank_count[0].reshape(1)

    excitation, projected = pl.pallas_call(
        _excite_kernel,
        out_shape=(
            jax.ShapeDtypeStruct((2, source_count, row_count), jnp.bfloat16),
            jax.ShapeDtypeStruct((2, source_count, rank_width), jnp.bfloat16),
        ),
        in_specs=[_SMEM, _SMEM, _SMEM, _SMEM, _VMEM, _VMEM],
        out_specs=(_VMEM, _VMEM),
        scratch_shapes=[
            pltpu.VMEM((slot_count, source_count, panel_width), jnp.float32),
            pltpu.VMEM((slot_count, source_count, panel_width), jnp.float32),
        ],
    )(panel_slot[0], own_cos, own_sin, rank, gathered, block_right[0])

    all_projected = lax.all_gather(projected, "row", axis=0, tiled=False)
    me = lax.axis_index("row").astype(jnp.int32).reshape(1)

    field = pl.pallas_call(
        _field_kernel,
        out_shape=jax.ShapeDtypeStruct((2, source_count, row_count), jnp.float32),
        in_specs=[_SMEM, _SMEM, _SMEM] + [_VMEM] * 7,
        out_specs=_VMEM,
        scratch_shapes=[
            pltpu.VMEM((2 ** (levels + 1) - 2, 2, source_count, rank_width), jnp.bfloat16),
            pltpu.VMEM((2, source_count, rank_width), jnp.bfloat16),
        ],
    )(
        quad_weight[0],
        rank,
        me,
        excitation,
        leaf_inverse[0],
        level_right[0],
        level_left[0],
        block_left[0],
        block_coupling[0, 0],
        all_projected,
    )
    summed = lax.psum_scatter(field, "ang", scatter_dimension=1, tiled=True)
    return jnp.transpose(summed, (1, 0, 2))


def solution(mesh):
    placed = (
        P("row", None, "ang", None, None),
        P("row", None),
        P("row", None, None),
        P(),
        P("ang", None, "row", None),
        P("ang", None, None, None, "row"),
        P("ang", None, None, None, "row"),
        P("ang", None, None, "row"),
        P("ang", None, None, "row"),
        P("ang", "row", None, None, None),
        P("ang", "row"),
        P("ang", None),
    )
    return jax.shard_map(
        shards, mesh=mesh, in_specs=placed, out_specs=P("ang", None, "row"), check_vma=False
    )
```

```python
import jax
import jax.numpy as jnp
from jax import lax
from jax.experimental import pallas as pl
from jax.experimental.pallas import tpu as pltpu
from jax.sharding import PartitionSpec as P

LEAF = 256

_SMEM = pl.BlockSpec(memory_space=pltpu.MemorySpace.SMEM)
_VMEM = pl.BlockSpec(memory_space=pltpu.MemorySpace.VMEM)


def _nt(a, b):
    return lax.dot_general(a, b, (((1,), (1,)), ((), ())), preferred_element_type=jnp.float32)


def _nn(a, b):
    return lax.dot_general(a, b, (((1,), (0,)), ((), ())), preferred_element_type=jnp.float32)


def _rank_mask(rank_ref, shape):
    return lax.broadcasted_iota(jnp.int32, shape, 0) < rank_ref[0]


def _excite_kernel(slot_ref, cos_ref, sin_ref, rank_ref, g_ref, br_ref, e_ref, bp_ref, acc_re, acc_im):
    panel_count, _, width2 = g_ref.shape
    width = width2 // 2
    slots = acc_re.shape[0]
    acc_re[...] = jnp.zeros(acc_re.shape, jnp.float32)
    acc_im[...] = jnp.zeros(acc_im.shape, jnp.float32)

    def body(q, carry):
        k = slot_ref[q]
        c = cos_ref[q]
        s = sin_ref[q]
        p_re = g_ref[q, :, :width].astype(jnp.float32)
        p_im = g_ref[q, :, width:].astype(jnp.float32)
        acc_re[k] = acc_re[k] + (c * p_re + s * p_im)
        acc_im[k] = acc_im[k] + (c * p_im - s * p_re)
        return carry

    lax.fori_loop(0, panel_count, body, 0)
    for k in range(slots):
        e_ref[0, :, k * width:(k + 1) * width] = acc_re[k].astype(jnp.bfloat16)
        e_ref[1, :, k * width:(k + 1) * width] = acc_im[k].astype(jnp.bfloat16)
    e_re = e_ref[0]
    e_im = e_ref[1]
    keep = _rank_mask(rank_ref, br_ref.shape[1:])
    zero = jnp.zeros(br_ref.shape[1:], jnp.bfloat16)
    r_re = jnp.where(keep, br_ref[0], zero)
    r_im = jnp.where(keep, br_ref[1], zero)
    bp_ref[0] = (_nt(e_re, r_re) - _nt(e_im, r_im)).astype(jnp.bfloat16)
    bp_ref[1] = (_nt(e_re, r_im) + _nt(e_im, r_re)).astype(jnp.bfloat16)


def _field_kernel(qw_ref, rank_ref, me_ref, e_ref, leaf_ref, lr_ref, ll_ref, bl_ref, cp_ref, bpa_ref, out_ref, pj_ref, cu_ref):
    _, source_count, row_count = e_ref.shape
    levels = lr_ref.shape[0]
    rank_width = lr_ref.shape[2]
    blocks = bpa_ref.shape[0]
    coupling_rank = bpa_ref.shape[3]
    e_re = e_ref[0]
    e_im = e_ref[1]

    first_group = []
    slot = 0
    for j in range(levels):
        node = row_count // 2 ** (j + 1)
        first_group.append(slot)
        for g in range(2 ** (j + 1)):
            cols = slice(g * node, (g + 1) * node)
            a = e_re[:, cols]
            b = e_im[:, cols]
            r_re = lr_ref[j, 0, :, cols]
            r_im = lr_ref[j, 1, :, cols]
            pj_ref[slot, 0] = (_nt(a, r_re) - _nt(b, r_im)).astype(jnp.bfloat16)
            pj_ref[slot, 1] = (_nt(a, r_im) + _nt(b, r_re)).astype(jnp.bfloat16)
            slot += 1

    me = me_ref[0]
    c_re = jnp.zeros((source_count, rank_width), jnp.float32)
    c_im = jnp.zeros((source_count, rank_width), jnp.float32)
    for u in range(blocks):
        own = me == u
        zero = jnp.zeros((source_count, coupling_rank), jnp.bfloat16)
        b_re = jnp.where(own, zero, bpa_ref[u, 0])
        b_im = jnp.where(own, zero, bpa_ref[u, 1])
        k_re = cp_ref[0, :, u * coupling_rank:(u + 1) * coupling_rank]
        k_im = cp_ref[1, :, u * coupling_rank:(u + 1) * coupling_rank]
        c_re = c_re + (_nt(b_re, k_re) - _nt(b_im, k_im))
        c_im = c_im + (_nt(b_re, k_im) + _nt(b_im, k_re))
    cu_ref[0] = c_re.astype(jnp.bfloat16)
    cu_ref[1] = c_im.astype(jnp.bfloat16)
    coupled_re = cu_ref[0]
    coupled_im = cu_ref[1]

    w_re = qw_ref[0]
    w_im = qw_ref[1]
    for l in range(row_count // LEAF):
        cols = slice(l * LEAF, (l + 1) * LEAF)
        a = e_re[:, cols]
        b = e_im[:, cols]
        lf_re = leaf_ref[0, cols, :]
        lf_im = leaf_ref[1, cols, :]
        f_re = _nt(a, lf_re) - _nt(b, lf_im)
        f_im = _nt(a, lf_im) + _nt(b, lf_re)
        for j in range(levels):
            node = row_count // 2 ** (j + 1)
            g = (l * LEAF) // node
            p_re = pj_ref[first_group[j] + (g ^ 1), 0]
            p_im = pj_ref[first_group[j] + (g ^ 1), 1]
            m_re = ll_ref[j, 0, :, cols]
            m_im = ll_ref[j, 1, :, cols]
            f_re = f_re + (_nn(p_re, m_re) - _nn(p_im, m_im))
            f_im = f_im + (_nn(p_re, m_im) + _nn(p_im, m_re))
        keep = _rank_mask(rank_ref, (bl_ref.shape[1], LEAF))
        zero = jnp.zeros((bl_ref.shape[1], LEAF), jnp.bfloat16)
        q_re = jnp.where(keep, bl_ref[0, :, cols], zero)
        q_im = jnp.where(keep, bl_ref[1, :, cols], zero)
        f_re = f_re + (_nn(coupled_re, q_re) - _nn(coupled_im, q_im))
        f_im = f_im + (_nn(coupled_re, q_im) + _nn(coupled_im, q_re))
        out_ref[0, :, cols] = w_re * f_re - w_im * f_im
        out_ref[1, :, cols] = w_re * f_im + w_im * f_re


def shards(
    panels,
    panel_slot,
    panel_cell,
    bloch_k,
    leaf_inverse,
    level_left,
    level_right,
    block_left,
    block_right,
    block_coupling,
    rank_count,
    quad_weight,
):
    local_angles = leaf_inverse.shape[0]
    assert local_angles == 1
    row_count = leaf_inverse.shape[2]
    panel_count = panels.shape[1]
    local_sources = panels.shape[2]
    panel_width = panels.shape[4]
    slot_count = row_count // panel_width
    source_count = local_sources * lax.axis_size("ang")
    rank_width = block_right.shape[2]
    levels = level_right.shape[1]

    cell_float = panel_cell[0].astype(jnp.float32)
    own_wave = lax.dynamic_slice_in_dim(bloch_k, lax.axis_index("ang") * local_angles, local_angles, 0)
    theta = own_wave[0, 0] * cell_float[:, 0] + own_wave[0, 1] * cell_float[:, 1]
    own_cos = lax.reduce_precision(jnp.cos(theta), exponent_bits=8, mantissa_bits=7)
    own_sin = lax.reduce_precision(jnp.sin(theta), exponent_bits=8, mantissa_bits=7)

    local_panels = panels[0].reshape(panel_count, local_sources, 2 * panel_width)
    gathered = lax.all_gather(local_panels, "ang", axis=1, tiled=True)
    rank = rank_count[0].reshape(1)

    excitation, projected = pl.pallas_call(
        _excite_kernel,
        out_shape=(
            jax.ShapeDtypeStruct((2, source_count, row_count), jnp.bfloat16),
            jax.ShapeDtypeStruct((2, source_count, rank_width), jnp.bfloat16),
        ),
        in_specs=[_SMEM, _SMEM, _SMEM, _SMEM, _VMEM, _VMEM],
        out_specs=(_VMEM, _VMEM),
        scratch_shapes=[
            pltpu.VMEM((slot_count, source_count, panel_width), jnp.float32),
            pltpu.VMEM((slot_count, source_count, panel_width), jnp.float32),
        ],
    )(panel_slot[0], own_cos, own_sin, rank, gathered, block_right[0])

    all_projected = lax.all_gather(projected, "row", axis=0, tiled=False)
    me = lax.axis_index("row").astype(jnp.int32).reshape(1)

    field = pl.pallas_call(
        _field_kernel,
        out_shape=jax.ShapeDtypeStruct((2, source_count, row_count), jnp.float32),
        in_specs=[_SMEM, _SMEM, _SMEM] + [_VMEM] * 7,
        out_specs=_VMEM,
        scratch_shapes=[
            pltpu.VMEM((2 ** (levels + 1) - 2, 2, source_count, rank_width), jnp.bfloat16),
            pltpu.VMEM((2, source_count, rank_width), jnp.bfloat16),
        ],
    )(
        quad_weight[0],
        rank,
        me,
        excitation,
        leaf_inverse[0],
        level_right[0],
        level_left[0],
        block_left[0],
        block_coupling[0, 0],
        all_projected,
    )
    summed = lax.psum_scatter(field, "ang", scatter_dimension=1, tiled=True)
    return jnp.transpose(summed, (1, 0, 2))


def solution(mesh):
    placed = (
        P("row", None, "ang", None, None),
        P("row", None),
        P("row", None, None),
        P(),
        P("ang", None, "row", None),
        P("ang", None, None, None, "row"),
        P("ang", None, None, None, "row"),
        P("ang", None, None, "row"),
        P("ang", None, None, "row"),
        P("ang", "row", None, None, None),
        P("ang", "row"),
        P("ang", None),
    )
    return jax.shard_map(
        shards, mesh=mesh, in_specs=placed, out_specs=P("ang", None, "row"), check_vma=False
    )
```

```python
import jax
import jax.numpy as jnp
from jax import lax
from jax.experimental import pallas as pl
from jax.experimental.pallas import tpu as pltpu
from jax.sharding import PartitionSpec as P

LEAF = 256

_SMEM = pl.BlockSpec(memory_space=pltpu.MemorySpace.SMEM)
_VMEM = pl.BlockSpec(memory_space=pltpu.MemorySpace.VMEM)


def _nt(a, b):
    return lax.dot_general(a, b, (((1,), (1,)), ((), ())), preferred_element_type=jnp.float32)


def _nn(a, b):
    return lax.dot_general(a, b, (((1,), (0,)), ((), ())), preferred_element_type=jnp.float32)


def _rank_mask(rank_ref, shape):
    return lax.broadcasted_iota(jnp.int32, shape, 0) < rank_ref[0]


def _excite_kernel(slot_ref, cos_ref, sin_ref, rank_ref, g_ref, br_ref, e_ref, bp_ref, acc_re, acc_im):
    panel_count, _, width2 = g_ref.shape
    width = width2 // 2
    slots = acc_re.shape[0]
    acc_re[...] = jnp.zeros(acc_re.shape, jnp.float32)
    acc_im[...] = jnp.zeros(acc_im.shape, jnp.float32)

    def body(q, carry):
        k = slot_ref[q]
        c = cos_ref[q]
        s = sin_ref[q]
        p_re = g_ref[q, :, :width].astype(jnp.float32)
        p_im = g_ref[q, :, width:].astype(jnp.float32)
        acc_re[k] = acc_re[k] + (c * p_re + s * p_im)
        acc_im[k] = acc_im[k] + (c * p_im - s * p_re)
        return carry

    lax.fori_loop(0, panel_count, body, 0)
    for k in range(slots):
        e_ref[0, :, k * width:(k + 1) * width] = acc_re[k].astype(jnp.bfloat16)
        e_ref[1, :, k * width:(k + 1) * width] = acc_im[k].astype(jnp.bfloat16)
    e_re = e_ref[0]
    e_im = e_ref[1]
    keep = _rank_mask(rank_ref, br_ref.shape[1:])
    zero = jnp.zeros(br_ref.shape[1:], jnp.bfloat16)
    r_re = jnp.where(keep, br_ref[0], zero)
    r_im = jnp.where(keep, br_ref[1], zero)
    bp_ref[0] = (_nt(e_re, r_re) - _nt(e_im, r_im)).astype(jnp.bfloat16)
    bp_ref[1] = (_nt(e_re, r_im) + _nt(e_im, r_re)).astype(jnp.bfloat16)


def _field_kernel(qw_ref, rank_ref, me_ref, e_ref, leaf_ref, lr_ref, ll_ref, bl_ref, cp_ref, bpa_ref, out_ref, pj_ref, cu_ref):
    _, source_count, row_count = e_ref.shape
    levels = lr_ref.shape[0]
    rank_width = lr_ref.shape[2]
    blocks = bpa_ref.shape[0]
    coupling_rank = bpa_ref.shape[3]
    e_re = e_ref[0]
    e_im = e_ref[1]

    first_group = []
    slot = 0
    for j in range(levels):
        node = row_count // 2 ** (j + 1)
        first_group.append(slot)
        for g in range(2 ** (j + 1)):
            cols = slice(g * node, (g + 1) * node)
            a = e_re[:, cols]
            b = e_im[:, cols]
            r_re = lr_ref[j, 0, :, cols]
            r_im = lr_ref[j, 1, :, cols]
            pj_ref[slot, 0] = (_nt(a, r_re) - _nt(b, r_im)).astype(jnp.bfloat16)
            pj_ref[slot, 1] = (_nt(a, r_im) + _nt(b, r_re)).astype(jnp.bfloat16)
            slot += 1

    me = me_ref[0]
    c_re = jnp.zeros((source_count, rank_width), jnp.float32)
    c_im = jnp.zeros((source_count, rank_width), jnp.float32)
    for u in range(blocks):
        own = me == u
        zero = jnp.zeros((source_count, coupling_rank), jnp.bfloat16)
        b_re = jnp.where(own, zero, bpa_ref[u, 0])
        b_im = jnp.where(own, zero, bpa_ref[u, 1])
        k_re = cp_ref[0, :, u * coupling_rank:(u + 1) * coupling_rank]
        k_im = cp_ref[1, :, u * coupling_rank:(u + 1) * coupling_rank]
        c_re = c_re + (_nt(b_re, k_re) - _nt(b_im, k_im))
        c_im = c_im + (_nt(b_re, k_im) + _nt(b_im, k_re))
    cu_ref[0] = c_re.astype(jnp.bfloat16)
    cu_ref[1] = c_im.astype(jnp.bfloat16)
    coupled_re = cu_ref[0]
    coupled_im = cu_ref[1]

    w_re = qw_ref[0]
    w_im = qw_ref[1]
    for l in range(row_count // LEAF):
        cols = slice(l * LEAF, (l + 1) * LEAF)
        a = e_re[:, cols]
        b = e_im[:, cols]
        lf_re = leaf_ref[0, cols, :]
        lf_im = leaf_ref[1, cols, :]
        f_re = _nt(a, lf_re) - _nt(b, lf_im)
        f_im = _nt(a, lf_im) + _nt(b, lf_re)
        for j in range(levels):
            node = row_count // 2 ** (j + 1)
            g = (l * LEAF) // node
            p_re = pj_ref[first_group[j] + (g ^ 1), 0]
            p_im = pj_ref[first_group[j] + (g ^ 1), 1]
            m_re = ll_ref[j, 0, :, cols]
            m_im = ll_ref[j, 1, :, cols]
            f_re = f_re + (_nn(p_re, m_re) - _nn(p_im, m_im))
            f_im = f_im + (_nn(p_re, m_im) + _nn(p_im, m_re))
        keep = _rank_mask(rank_ref, (bl_ref.shape[1], LEAF))
        zero = jnp.zeros((bl_ref.shape[1], LEAF), jnp.bfloat16)
        q_re = jnp.where(keep, bl_ref[0, :, cols], zero)
        q_im = jnp.where(keep, bl_ref[1, :, cols], zero)
        f_re = f_re + (_nn(coupled_re, q_re) - _nn(coupled_im, q_im))
        f_im = f_im + (_nn(coupled_re, q_im) + _nn(coupled_im, q_re))
        out_ref[:, cols] = w_re * f_re - w_im * f_im
        out_ref[:, row_count + l * LEAF:row_count + (l + 1) * LEAF] = w_re * f_im + w_im * f_re


def _pair_perm(count, bit):
    return [(i, i ^ (1 << bit)) for i in range(count)]


def _reduce_scatter(x, axis_name):
    count = lax.axis_size(axis_name)
    index = lax.axis_index(axis_name)
    chunk = x.shape[0] // count
    current = x.reshape(count, chunk, *x.shape[1:])
    for bit in range(count.bit_length() - 1):
        current = current.reshape(current.shape[0] // 2, 2, *current.shape[1:])
        mine = (index >> bit) & 1
        keep = lax.dynamic_index_in_dim(current, mine, axis=1, keepdims=False)
        give = lax.dynamic_index_in_dim(current, 1 - mine, axis=1, keepdims=False)
        current = keep + lax.ppermute(give, axis_name, _pair_perm(count, bit))
    return current.reshape(chunk, *x.shape[1:])


def _all_gather(x, axis_name):
    count = lax.axis_size(axis_name)
    index = lax.axis_index(axis_name)
    current = x[None]
    for bit in range(count.bit_length() - 1):
        other = lax.ppermute(current, axis_name, _pair_perm(count, bit))
        low = ((index >> bit) & 1) == 0
        current = jnp.concatenate([jnp.where(low, current, other), jnp.where(low, other, current)], axis=0)
    return current


def shards(
    panels,
    panel_slot,
    panel_cell,
    bloch_k,
    leaf_inverse,
    level_left,
    level_right,
    block_left,
    block_right,
    block_coupling,
    rank_count,
    quad_weight,
):
    local_angles = leaf_inverse.shape[0]
    assert local_angles == 1
    row_count = leaf_inverse.shape[2]
    panel_count = panels.shape[1]
    local_sources = panels.shape[2]
    panel_width = panels.shape[4]
    slot_count = row_count // panel_width
    source_count = local_sources * lax.axis_size("ang")
    rank_width = block_right.shape[2]
    levels = level_right.shape[1]

    cell_float = panel_cell[0].astype(jnp.float32)
    own_wave = lax.dynamic_slice_in_dim(bloch_k, lax.axis_index("ang") * local_angles, local_angles, 0)
    theta = own_wave[0, 0] * cell_float[:, 0] + own_wave[0, 1] * cell_float[:, 1]
    own_cos = lax.reduce_precision(jnp.cos(theta), exponent_bits=8, mantissa_bits=7)
    own_sin = lax.reduce_precision(jnp.sin(theta), exponent_bits=8, mantissa_bits=7)

    local_panels = panels[0].reshape(panel_count, local_sources, 2 * panel_width)
    gathered = lax.all_gather(local_panels, "ang", axis=1, tiled=True)
    rank = rank_count[0].reshape(1)

    excitation, projected = pl.pallas_call(
        _excite_kernel,
        out_shape=(
            jax.ShapeDtypeStruct((2, source_count, row_count), jnp.bfloat16),
            jax.ShapeDtypeStruct((2, source_count, rank_width), jnp.bfloat16),
        ),
        in_specs=[_SMEM, _SMEM, _SMEM, _SMEM, _VMEM, _VMEM],
        out_specs=(_VMEM, _VMEM),
        scratch_shapes=[
            pltpu.VMEM((slot_count, source_count, panel_width), jnp.float32),
            pltpu.VMEM((slot_count, source_count, panel_width), jnp.float32),
        ],
    )(panel_slot[0], own_cos, own_sin, rank, gathered, block_right[0])

    all_projected = _all_gather(projected, "row")
    me = lax.axis_index("row").astype(jnp.int32).reshape(1)

    field = pl.pallas_call(
        _field_kernel,
        out_shape=jax.ShapeDtypeStruct((source_count, 2 * row_count), jnp.float32),
        in_specs=[_SMEM, _SMEM, _SMEM] + [_VMEM] * 7,
        out_specs=_VMEM,
        scratch_shapes=[
            pltpu.VMEM((2 ** (levels + 1) - 2, 2, source_count, rank_width), jnp.bfloat16),
            pltpu.VMEM((2, source_count, rank_width), jnp.bfloat16),
        ],
    )(
        quad_weight[0],
        rank,
        me,
        excitation,
        leaf_inverse[0],
        level_right[0],
        level_left[0],
        block_left[0],
        block_coupling[0, 0],
        all_projected,
    )
    summed = _reduce_scatter(field, "ang")
    return summed.reshape(summed.shape[0], 2, row_count)


def solution(mesh):
    placed = (
        P("row", None, "ang", None, None),
        P("row", None),
        P("row", None, None),
        P(),
        P("ang", None, "row", None),
        P("ang", None, None, None, "row"),
        P("ang", None, None, None, "row"),
        P("ang", None, None, "row"),
        P("ang", None, None, "row"),
        P("ang", "row", None, None, None),
        P("ang", "row"),
        P("ang", None),
    )
    return jax.shard_map(
        shards, mesh=mesh, in_specs=placed, out_specs=P("ang", None, "row"), check_vma=False
    )
```

```python
import jax
import jax.numpy as jnp
from jax import lax
from jax.experimental import pallas as pl
from jax.experimental.pallas import tpu as pltpu
from jax.sharding import PartitionSpec as P

LEAF = 256

_SMEM = pl.BlockSpec(memory_space=pltpu.MemorySpace.SMEM)
_VMEM = pl.BlockSpec(memory_space=pltpu.MemorySpace.VMEM)


def _nt(a, b):
    return lax.dot_general(a, b, (((1,), (1,)), ((), ())), preferred_element_type=jnp.float32)


def _nn(a, b):
    return lax.dot_general(a, b, (((1,), (0,)), ((), ())), preferred_element_type=jnp.float32)


def _rank_mask(rank_ref, shape):
    return lax.broadcasted_iota(jnp.int32, shape, 0) < rank_ref[0]


def _excite_kernel(slot_ref, cos_ref, sin_ref, rank_ref, g_ref, br_ref, e_ref, bp_ref, acc_re, acc_im):
    panel_count, _, width2 = g_ref.shape
    width = width2 // 2
    slots = acc_re.shape[0]
    acc_re[...] = jnp.zeros(acc_re.shape, jnp.float32)
    acc_im[...] = jnp.zeros(acc_im.shape, jnp.float32)

    def body(q, carry):
        k = slot_ref[q]
        c = cos_ref[q]
        s = sin_ref[q]
        p_re = g_ref[q, :, :width].astype(jnp.float32)
        p_im = g_ref[q, :, width:].astype(jnp.float32)
        acc_re[k] = acc_re[k] + (c * p_re + s * p_im)
        acc_im[k] = acc_im[k] + (c * p_im - s * p_re)
        return carry

    lax.fori_loop(0, panel_count, body, 0)
    for k in range(slots):
        e_ref[0, :, k * width:(k + 1) * width] = acc_re[k].astype(jnp.bfloat16)
        e_ref[1, :, k * width:(k + 1) * width] = acc_im[k].astype(jnp.bfloat16)
    e_re = e_ref[0]
    e_im = e_ref[1]
    keep = _rank_mask(rank_ref, br_ref.shape[1:])
    zero = jnp.zeros(br_ref.shape[1:], jnp.bfloat16)
    r_re = jnp.where(keep, br_ref[0], zero)
    r_im = jnp.where(keep, br_ref[1], zero)
    bp_ref[0] = (_nt(e_re, r_re) - _nt(e_im, r_im)).astype(jnp.bfloat16)
    bp_ref[1] = (_nt(e_re, r_im) + _nt(e_im, r_re)).astype(jnp.bfloat16)


def _field_kernel(qw_ref, rank_ref, e_ref, leaf_ref, lr_ref, ll_ref, bl_ref, cp_ref, bpa_ref, out_ref, pj_ref, cu_ref):
    _, source_count, row_count = e_ref.shape
    levels = lr_ref.shape[0]
    rank_width = lr_ref.shape[2]
    blocks = bpa_ref.shape[0]
    coupling_rank = bpa_ref.shape[3]
    e_re = e_ref[0]
    e_im = e_ref[1]

    first_group = []
    slot = 0
    for j in range(levels):
        node = row_count // 2 ** (j + 1)
        first_group.append(slot)
        for g in range(2 ** (j + 1)):
            cols = slice(g * node, (g + 1) * node)
            a = e_re[:, cols]
            b = e_im[:, cols]
            r_re = lr_ref[j, 0, :, cols]
            r_im = lr_ref[j, 1, :, cols]
            pj_ref[slot, 0] = (_nt(a, r_re) - _nt(b, r_im)).astype(jnp.bfloat16)
            pj_ref[slot, 1] = (_nt(a, r_im) + _nt(b, r_re)).astype(jnp.bfloat16)
            slot += 1

    c_re = jnp.zeros((source_count, rank_width), jnp.float32)
    c_im = jnp.zeros((source_count, rank_width), jnp.float32)
    for u in range(1, blocks):
        b_re = bpa_ref[u, 0]
        b_im = bpa_ref[u, 1]
        k_re = cp_ref[0, :, u * coupling_rank:(u + 1) * coupling_rank]
        k_im = cp_ref[1, :, u * coupling_rank:(u + 1) * coupling_rank]
        c_re = c_re + (_nt(b_re, k_re) - _nt(b_im, k_im))
        c_im = c_im + (_nt(b_re, k_im) + _nt(b_im, k_re))
    cu_ref[0] = c_re.astype(jnp.bfloat16)
    cu_ref[1] = c_im.astype(jnp.bfloat16)
    coupled_re = cu_ref[0]
    coupled_im = cu_ref[1]

    w_re = qw_ref[0]
    w_im = qw_ref[1]
    for l in range(row_count // LEAF):
        cols = slice(l * LEAF, (l + 1) * LEAF)
        a = e_re[:, cols]
        b = e_im[:, cols]
        lf_re = leaf_ref[0, cols, :]
        lf_im = leaf_ref[1, cols, :]
        f_re = _nt(a, lf_re) - _nt(b, lf_im)
        f_im = _nt(a, lf_im) + _nt(b, lf_re)
        for j in range(levels):
            node = row_count // 2 ** (j + 1)
            g = (l * LEAF) // node
            p_re = pj_ref[first_group[j] + (g ^ 1), 0]
            p_im = pj_ref[first_group[j] + (g ^ 1), 1]
            m_re = ll_ref[j, 0, :, cols]
            m_im = ll_ref[j, 1, :, cols]
            f_re = f_re + (_nn(p_re, m_re) - _nn(p_im, m_im))
            f_im = f_im + (_nn(p_re, m_im) + _nn(p_im, m_re))
        keep = _rank_mask(rank_ref, (bl_ref.shape[1], LEAF))
        zero = jnp.zeros((bl_ref.shape[1], LEAF), jnp.bfloat16)
        q_re = jnp.where(keep, bl_ref[0, :, cols], zero)
        q_im = jnp.where(keep, bl_ref[1, :, cols], zero)
        f_re = f_re + (_nn(coupled_re, q_re) - _nn(coupled_im, q_im))
        f_im = f_im + (_nn(coupled_re, q_im) + _nn(coupled_im, q_re))
        out_ref[:, cols] = w_re * f_re - w_im * f_im
        out_ref[:, row_count + l * LEAF:row_count + (l + 1) * LEAF] = w_re * f_im + w_im * f_re


def _pair_perm(count, bit):
    return [(i, i ^ (1 << bit)) for i in range(count)]


def _reduce_scatter(x, axis_name):
    count = lax.axis_size(axis_name)
    current = x
    for bit in range(count.bit_length() - 1):
        half = current.shape[0] // 2
        current = current[:half] + lax.ppermute(current[half:], axis_name, _pair_perm(count, bit))
    return current


def _all_gather(x, axis_name, axis, bits):
    count = lax.axis_size(axis_name)
    current = x
    for bit in bits:
        other = lax.ppermute(current, axis_name, _pair_perm(count, bit))
        current = jnp.concatenate([current, other], axis=axis)
    return current


def shards(
    panels,
    panel_slot,
    panel_cell,
    bloch_k,
    leaf_inverse,
    level_left,
    level_right,
    block_left,
    block_right,
    block_coupling,
    rank_count,
    quad_weight,
):
    local_angles = leaf_inverse.shape[0]
    assert local_angles == 1
    row_count = leaf_inverse.shape[2]
    panel_count = panels.shape[1]
    local_sources = panels.shape[2]
    panel_width = panels.shape[4]
    slot_count = row_count // panel_width
    source_count = local_sources * lax.axis_size("ang")
    rank_width = block_right.shape[2]
    levels = level_right.shape[1]

    cell_float = panel_cell[0].astype(jnp.float32)
    own_wave = lax.dynamic_slice_in_dim(bloch_k, lax.axis_index("ang") * local_angles, local_angles, 0)
    theta = own_wave[0, 0] * cell_float[:, 0] + own_wave[0, 1] * cell_float[:, 1]
    own_cos = lax.reduce_precision(jnp.cos(theta), exponent_bits=8, mantissa_bits=7)
    own_sin = lax.reduce_precision(jnp.sin(theta), exponent_bits=8, mantissa_bits=7)

    local_panels = panels[0].reshape(panel_count, local_sources, 2 * panel_width)
    ang_bits = lax.axis_size("ang").bit_length() - 1
    gathered = _all_gather(local_panels, "ang", 1, list(range(ang_bits))[::-1])
    rank = rank_count[0].reshape(1)

    excitation, projected = pl.pallas_call(
        _excite_kernel,
        out_shape=(
            jax.ShapeDtypeStruct((2, source_count, row_count), jnp.bfloat16),
            jax.ShapeDtypeStruct((2, source_count, rank_width), jnp.bfloat16),
        ),
        in_specs=[_SMEM, _SMEM, _SMEM, _SMEM, _VMEM, _VMEM],
        out_specs=(_VMEM, _VMEM),
        scratch_shapes=[
            pltpu.VMEM((slot_count, source_count, panel_width), jnp.float32),
            pltpu.VMEM((slot_count, source_count, panel_width), jnp.float32),
        ],
    )(panel_slot[0], own_cos, own_sin, rank, gathered, block_right[0])

    row_blocks = lax.axis_size("row")
    all_projected = _all_gather(projected[None], "row", 0, list(range(row_blocks.bit_length() - 1)))
    me = lax.axis_index("row")
    coupling = block_coupling[0, 0]
    coupling = coupling.reshape(2, rank_width, row_blocks, coupling.shape[2] // row_blocks)
    coupling = jnp.take(coupling, me ^ jnp.arange(row_blocks), axis=2).reshape(block_coupling.shape[2:])

    field = pl.pallas_call(
        _field_kernel,
        out_shape=jax.ShapeDtypeStruct((source_count, 2 * row_count), jnp.float32),
        in_specs=[_SMEM, _SMEM] + [_VMEM] * 7,
        out_specs=_VMEM,
        scratch_shapes=[
            pltpu.VMEM((2 ** (levels + 1) - 2, 2, source_count, rank_width), jnp.bfloat16),
            pltpu.VMEM((2, source_count, rank_width), jnp.bfloat16),
        ],
    )(
        quad_weight[0],
        rank,
        excitation,
        leaf_inverse[0],
        level_right[0],
        level_left[0],
        block_left[0],
        coupling,
        all_projected,
    )
    summed = _reduce_scatter(field, "ang")
    return summed.reshape(summed.shape[0], 2, row_count)


def solution(mesh):
    placed = (
        P("row", None, "ang", None, None),
        P("row", None),
        P("row", None, None),
        P(),
        P("ang", None, "row", None),
        P("ang", None, None, None, "row"),
        P("ang", None, None, None, "row"),
        P("ang", None, None, "row"),
        P("ang", None, None, "row"),
        P("ang", "row", None, None, None),
        P("ang", "row"),
        P("ang", None),
    )
    return jax.shard_map(
        shards, mesh=mesh, in_specs=placed, out_specs=P("ang", None, "row"), check_vma=False
    )
```

```python
import jax
import jax.numpy as jnp
from jax import lax
from jax.experimental import pallas as pl
from jax.experimental.pallas import tpu as pltpu
from jax.sharding import PartitionSpec as P

LEAF = 256

_SMEM = pl.BlockSpec(memory_space=pltpu.MemorySpace.SMEM)
_VMEM = pl.BlockSpec(memory_space=pltpu.MemorySpace.VMEM)


def _nt(a, b):
    return lax.dot_general(a, b, (((1,), (1,)), ((), ())), preferred_element_type=jnp.float32)


def _nn(a, b):
    return lax.dot_general(a, b, (((1,), (0,)), ((), ())), preferred_element_type=jnp.float32)


def _rank_mask(rank_ref, shape):
    return lax.broadcasted_iota(jnp.int32, shape, 0) < rank_ref[0]


def _excite_kernel(slot_ref, cos_ref, sin_ref, rank_ref, g_ref, br_ref, e_ref, bp_ref, acc_re, acc_im):
    panel_count, _, width2 = g_ref.shape
    width = width2 // 2
    slots = acc_re.shape[0]
    acc_re[...] = jnp.zeros(acc_re.shape, jnp.float32)
    acc_im[...] = jnp.zeros(acc_im.shape, jnp.float32)

    def body(q, carry):
        k = slot_ref[q]
        c = cos_ref[q]
        s = sin_ref[q]
        p_re = g_ref[q, :, :width].astype(jnp.float32)
        p_im = g_ref[q, :, width:].astype(jnp.float32)
        acc_re[k] = acc_re[k] + (c * p_re + s * p_im)
        acc_im[k] = acc_im[k] + (c * p_im - s * p_re)
        return carry

    lax.fori_loop(0, panel_count, body, 0)
    for k in range(slots):
        e_ref[0, :, k * width:(k + 1) * width] = acc_re[k].astype(jnp.bfloat16)
        e_ref[1, :, k * width:(k + 1) * width] = acc_im[k].astype(jnp.bfloat16)
    e_re = e_ref[0]
    e_im = e_ref[1]
    keep = _rank_mask(rank_ref, br_ref.shape[1:])
    zero = jnp.zeros(br_ref.shape[1:], jnp.bfloat16)
    r_re = jnp.where(keep, br_ref[0], zero)
    r_im = jnp.where(keep, br_ref[1], zero)
    bp_ref[0] = (_nt(e_re, r_re) - _nt(e_im, r_im)).astype(jnp.bfloat16)
    bp_ref[1] = (_nt(e_re, r_im) + _nt(e_im, r_re)).astype(jnp.bfloat16)


def _near_kernel(e_ref, leaf_ref, lr_ref, ll_ref, out_ref, pj_ref):
    _, source_count, row_count = e_ref.shape
    levels = lr_ref.shape[0]
    e_re = e_ref[0]
    e_im = e_ref[1]

    first_group = []
    slot = 0
    for j in range(levels):
        node = row_count // 2 ** (j + 1)
        first_group.append(slot)
        for g in range(2 ** (j + 1)):
            cols = slice(g * node, (g + 1) * node)
            a = e_re[:, cols]
            b = e_im[:, cols]
            r_re = lr_ref[j, 0, :, cols]
            r_im = lr_ref[j, 1, :, cols]
            pj_ref[slot, 0] = (_nt(a, r_re) - _nt(b, r_im)).astype(jnp.bfloat16)
            pj_ref[slot, 1] = (_nt(a, r_im) + _nt(b, r_re)).astype(jnp.bfloat16)
            slot += 1

    for l in range(row_count // LEAF):
        cols = slice(l * LEAF, (l + 1) * LEAF)
        a = e_re[:, cols]
        b = e_im[:, cols]
        lf_re = leaf_ref[0, cols, :]
        lf_im = leaf_ref[1, cols, :]
        f_re = _nt(a, lf_re) - _nt(b, lf_im)
        f_im = _nt(a, lf_im) + _nt(b, lf_re)
        for j in range(levels):
            node = row_count // 2 ** (j + 1)
            g = (l * LEAF) // node
            p_re = pj_ref[first_group[j] + (g ^ 1), 0]
            p_im = pj_ref[first_group[j] + (g ^ 1), 1]
            m_re = ll_ref[j, 0, :, cols]
            m_im = ll_ref[j, 1, :, cols]
            f_re = f_re + (_nn(p_re, m_re) - _nn(p_im, m_im))
            f_im = f_im + (_nn(p_re, m_im) + _nn(p_im, m_re))
        out_ref[:, cols] = f_re
        out_ref[:, row_count + l * LEAF:row_count + (l + 1) * LEAF] = f_im


def _far_kernel(qw_ref, rank_ref, near_ref, bl_ref, cp_ref, bpa_ref, out_ref, cu_ref):
    source_count = near_ref.shape[0]
    row_count = bl_ref.shape[2]
    rank_width = bl_ref.shape[1]
    blocks = bpa_ref.shape[0]
    coupling_rank = bpa_ref.shape[3]

    c_re = jnp.zeros((source_count, rank_width), jnp.float32)
    c_im = jnp.zeros((source_count, rank_width), jnp.float32)
    for u in range(1, blocks):
        b_re = bpa_ref[u, 0]
        b_im = bpa_ref[u, 1]
        k_re = cp_ref[0, :, u * coupling_rank:(u + 1) * coupling_rank]
        k_im = cp_ref[1, :, u * coupling_rank:(u + 1) * coupling_rank]
        c_re = c_re + (_nt(b_re, k_re) - _nt(b_im, k_im))
        c_im = c_im + (_nt(b_re, k_im) + _nt(b_im, k_re))
    cu_ref[0] = c_re.astype(jnp.bfloat16)
    cu_ref[1] = c_im.astype(jnp.bfloat16)
    coupled_re = cu_ref[0]
    coupled_im = cu_ref[1]

    w_re = qw_ref[0]
    w_im = qw_ref[1]
    for l in range(row_count // LEAF):
        cols = slice(l * LEAF, (l + 1) * LEAF)
        imag_cols = slice(row_count + l * LEAF, row_count + (l + 1) * LEAF)
        keep = _rank_mask(rank_ref, (rank_width, LEAF))
        zero = jnp.zeros((rank_width, LEAF), jnp.bfloat16)
        q_re = jnp.where(keep, bl_ref[0, :, cols], zero)
        q_im = jnp.where(keep, bl_ref[1, :, cols], zero)
        f_re = near_ref[:, cols] + (_nn(coupled_re, q_re) - _nn(coupled_im, q_im))
        f_im = near_ref[:, imag_cols] + (_nn(coupled_re, q_im) + _nn(coupled_im, q_re))
        out_ref[:, cols] = w_re * f_re - w_im * f_im
        out_ref[:, imag_cols] = w_re * f_im + w_im * f_re


def _pair_perm(count, bit):
    return [(i, i ^ (1 << bit)) for i in range(count)]


def _reduce_scatter(x, axis_name):
    count = lax.axis_size(axis_name)
    current = x
    for bit in range(count.bit_length() - 1):
        half = current.shape[0] // 2
        current = current[:half] + lax.ppermute(current[half:], axis_name, _pair_perm(count, bit))
    return current


def _all_gather(x, axis_name, axis, bits):
    count = lax.axis_size(axis_name)
    current = x
    for bit in bits:
        other = lax.ppermute(current, axis_name, _pair_perm(count, bit))
        current = jnp.concatenate([current, other], axis=axis)
    return current


def _exchange(x, axis_name):
    count = lax.axis_size(axis_name)
    if count > 4:
        return _all_gather(x[None], axis_name, 0, list(range(count.bit_length() - 1)))
    parts = [x] + [lax.ppermute(x, axis_name, [(i, i ^ p) for i in range(count)]) for p in range(1, count)]
    return jnp.stack(parts, axis=0)


def shards(
    panels,
    panel_slot,
    panel_cell,
    bloch_k,
    leaf_inverse,
    level_left,
    level_right,
    block_left,
    block_right,
    block_coupling,
    rank_count,
    quad_weight,
):
    local_angles = leaf_inverse.shape[0]
    assert local_angles == 1
    row_count = leaf_inverse.shape[2]
    panel_count = panels.shape[1]
    local_sources = panels.shape[2]
    panel_width = panels.shape[4]
    slot_count = row_count // panel_width
    source_count = local_sources * lax.axis_size("ang")
    rank_width = block_right.shape[2]
    levels = level_right.shape[1]

    cell_float = panel_cell[0].astype(jnp.float32)
    own_wave = lax.dynamic_slice_in_dim(bloch_k, lax.axis_index("ang") * local_angles, local_angles, 0)
    theta = own_wave[0, 0] * cell_float[:, 0] + own_wave[0, 1] * cell_float[:, 1]
    own_cos = lax.reduce_precision(jnp.cos(theta), exponent_bits=8, mantissa_bits=7)
    own_sin = lax.reduce_precision(jnp.sin(theta), exponent_bits=8, mantissa_bits=7)

    local_panels = panels[0].reshape(panel_count, local_sources, 2 * panel_width)
    ang_bits = lax.axis_size("ang").bit_length() - 1
    gathered = _all_gather(local_panels, "ang", 1, list(range(ang_bits))[::-1])
    rank = rank_count[0].reshape(1)

    excitation, projected = pl.pallas_call(
        _excite_kernel,
        out_shape=(
            jax.ShapeDtypeStruct((2, source_count, row_count), jnp.bfloat16),
            jax.ShapeDtypeStruct((2, source_count, rank_width), jnp.bfloat16),
        ),
        in_specs=[_SMEM, _SMEM, _SMEM, _SMEM, _VMEM, _VMEM],
        out_specs=(_VMEM, _VMEM),
        scratch_shapes=[
            pltpu.VMEM((slot_count, source_count, panel_width), jnp.float32),
            pltpu.VMEM((slot_count, source_count, panel_width), jnp.float32),
        ],
    )(panel_slot[0], own_cos, own_sin, rank, gathered, block_right[0])

    row_blocks = lax.axis_size("row")
    all_projected = _exchange(projected, "row")
    me = lax.axis_index("row")
    coupling = block_coupling[0, 0]
    coupling = coupling.reshape(2, rank_width, row_blocks, coupling.shape[2] // row_blocks)
    coupling = jnp.take(coupling, me ^ jnp.arange(row_blocks), axis=2).reshape(block_coupling.shape[2:])

    near = pl.pallas_call(
        _near_kernel,
        out_shape=jax.ShapeDtypeStruct((source_count, 2 * row_count), jnp.float32),
        in_specs=[_VMEM] * 4,
        out_specs=_VMEM,
        scratch_shapes=[pltpu.VMEM((2 ** (levels + 1) - 2, 2, source_count, rank_width), jnp.bfloat16)],
    )(excitation, leaf_inverse[0], level_right[0], level_left[0])

    field = pl.pallas_call(
        _far_kernel,
        out_shape=jax.ShapeDtypeStruct((source_count, 2 * row_count), jnp.float32),
        in_specs=[_SMEM, _SMEM] + [_VMEM] * 4,
        out_specs=_VMEM,
        scratch_shapes=[pltpu.VMEM((2, source_count, rank_width), jnp.bfloat16)],
        input_output_aliases={2: 0},
    )(quad_weight[0], rank, near, block_left[0], coupling, all_projected)
    summed = _reduce_scatter(field, "ang")
    return summed.reshape(summed.shape[0], 2, row_count)


def solution(mesh):
    placed = (
        P("row", None, "ang", None, None),
        P("row", None),
        P("row", None, None),
        P(),
        P("ang", None, "row", None),
        P("ang", None, None, None, "row"),
        P("ang", None, None, None, "row"),
        P("ang", None, None, "row"),
        P("ang", None, None, "row"),
        P("ang", "row", None, None, None),
        P("ang", "row"),
        P("ang", None),
    )
    return jax.shard_map(
        shards, mesh=mesh, in_specs=placed, out_specs=P("ang", None, "row"), check_vma=False
    )
```

```python
import jax
import jax.numpy as jnp
from jax import lax
from jax.experimental import pallas as pl
from jax.experimental.pallas import tpu as pltpu
from jax.sharding import PartitionSpec as P

LEAF = 256

_SMEM = pl.BlockSpec(memory_space=pltpu.MemorySpace.SMEM)
_VMEM = pl.BlockSpec(memory_space=pltpu.MemorySpace.VMEM)


def _nt(a, b):
    return lax.dot_general(a, b, (((1,), (1,)), ((), ())), preferred_element_type=jnp.float32)


def _nn(a, b):
    return lax.dot_general(a, b, (((1,), (0,)), ((), ())), preferred_element_type=jnp.float32)


def _rank_mask(rank_ref, shape):
    return lax.broadcasted_iota(jnp.int32, shape, 0) < rank_ref[0]


def _excite_kernel(slot_ref, cos_ref, sin_ref, rank_ref, g_ref, br_ref, e_ref, bp_ref, acc_re, acc_im):
    panel_count, _, width2 = g_ref.shape
    width = width2 // 2
    slots = acc_re.shape[0]
    acc_re[...] = jnp.zeros(acc_re.shape, jnp.float32)
    acc_im[...] = jnp.zeros(acc_im.shape, jnp.float32)

    def body(q, carry):
        k = slot_ref[q]
        c = cos_ref[q]
        s = sin_ref[q]
        p_re = g_ref[q, :, :width].astype(jnp.float32)
        p_im = g_ref[q, :, width:].astype(jnp.float32)
        acc_re[k] = acc_re[k] + (c * p_re + s * p_im)
        acc_im[k] = acc_im[k] + (c * p_im - s * p_re)
        return carry

    lax.fori_loop(0, panel_count, body, 0)
    for k in range(slots):
        e_ref[0, :, k * width:(k + 1) * width] = acc_re[k].astype(jnp.bfloat16)
        e_ref[1, :, k * width:(k + 1) * width] = acc_im[k].astype(jnp.bfloat16)
    e_re = e_ref[0]
    e_im = e_ref[1]
    keep = _rank_mask(rank_ref, br_ref.shape[1:])
    zero = jnp.zeros(br_ref.shape[1:], jnp.bfloat16)
    r_re = jnp.where(keep, br_ref[0], zero)
    r_im = jnp.where(keep, br_ref[1], zero)
    bp_ref[0] = (_nt(e_re, r_re) - _nt(e_im, r_im)).astype(jnp.bfloat16)
    bp_ref[1] = (_nt(e_re, r_im) + _nt(e_im, r_re)).astype(jnp.bfloat16)


def _near_kernel(e_ref, leaf_ref, lr_ref, ll_ref, out_ref, pj_ref):
    _, source_count, row_count = e_ref.shape
    levels = lr_ref.shape[0]
    e_re = e_ref[0]
    e_im = e_ref[1]

    first_group = []
    slot = 0
    for j in range(levels):
        node = row_count // 2 ** (j + 1)
        first_group.append(slot)
        for g in range(2 ** (j + 1)):
            cols = slice(g * node, (g + 1) * node)
            a = e_re[:, cols]
            b = e_im[:, cols]
            r_re = lr_ref[j, 0, :, cols]
            r_im = lr_ref[j, 1, :, cols]
            pj_ref[slot, 0] = (_nt(a, r_re) - _nt(b, r_im)).astype(jnp.bfloat16)
            pj_ref[slot, 1] = (_nt(a, r_im) + _nt(b, r_re)).astype(jnp.bfloat16)
            slot += 1

    for l in range(row_count // LEAF):
        cols = slice(l * LEAF, (l + 1) * LEAF)
        a = e_re[:, cols]
        b = e_im[:, cols]
        lf_re = leaf_ref[0, cols, :]
        lf_im = leaf_ref[1, cols, :]
        f_re = _nt(a, lf_re) - _nt(b, lf_im)
        f_im = _nt(a, lf_im) + _nt(b, lf_re)
        for j in range(levels):
            node = row_count // 2 ** (j + 1)
            g = (l * LEAF) // node
            p_re = pj_ref[first_group[j] + (g ^ 1), 0]
            p_im = pj_ref[first_group[j] + (g ^ 1), 1]
            m_re = ll_ref[j, 0, :, cols]
            m_im = ll_ref[j, 1, :, cols]
            f_re = f_re + (_nn(p_re, m_re) - _nn(p_im, m_im))
            f_im = f_im + (_nn(p_re, m_im) + _nn(p_im, m_re))
        out_ref[:, cols] = f_re
        out_ref[:, row_count + l * LEAF:row_count + (l + 1) * LEAF] = f_im


def _far_kernel(qw_ref, rank_ref, near_ref, bl_ref, cp_ref, bpa_ref, out_ref, cu_ref):
    source_count = near_ref.shape[0]
    row_count = bl_ref.shape[2]
    rank_width = bl_ref.shape[1]
    blocks = bpa_ref.shape[0]
    coupling_rank = bpa_ref.shape[3]

    c_re = jnp.zeros((source_count, rank_width), jnp.float32)
    c_im = jnp.zeros((source_count, rank_width), jnp.float32)
    for u in range(1, blocks):
        b_re = bpa_ref[u, 0]
        b_im = bpa_ref[u, 1]
        k_re = cp_ref[0, :, u * coupling_rank:(u + 1) * coupling_rank]
        k_im = cp_ref[1, :, u * coupling_rank:(u + 1) * coupling_rank]
        c_re = c_re + (_nt(b_re, k_re) - _nt(b_im, k_im))
        c_im = c_im + (_nt(b_re, k_im) + _nt(b_im, k_re))
    cu_ref[0] = c_re.astype(jnp.bfloat16)
    cu_ref[1] = c_im.astype(jnp.bfloat16)
    coupled_re = cu_ref[0]
    coupled_im = cu_ref[1]

    w_re = qw_ref[0]
    w_im = qw_ref[1]
    for l in range(row_count // LEAF):
        cols = slice(l * LEAF, (l + 1) * LEAF)
        imag_cols = slice(row_count + l * LEAF, row_count + (l + 1) * LEAF)
        keep = _rank_mask(rank_ref, (rank_width, LEAF))
        zero = jnp.zeros((rank_width, LEAF), jnp.bfloat16)
        q_re = jnp.where(keep, bl_ref[0, :, cols], zero)
        q_im = jnp.where(keep, bl_ref[1, :, cols], zero)
        f_re = near_ref[:, cols] + (_nn(coupled_re, q_re) - _nn(coupled_im, q_im))
        f_im = near_ref[:, imag_cols] + (_nn(coupled_re, q_im) + _nn(coupled_im, q_re))
        out_ref[:, cols] = w_re * f_re - w_im * f_im
        out_ref[:, imag_cols] = w_re * f_im + w_im * f_re


def _pair_perm(count, bit):
    return [(i, i ^ (1 << bit)) for i in range(count)]


def _reduce_scatter(keep, give, axis_name):
    count = lax.axis_size(axis_name)
    current = keep + lax.ppermute(give, axis_name, _pair_perm(count, 0))
    for bit in range(1, count.bit_length() - 1):
        half = current.shape[0] // 2
        current = current[:half] + lax.ppermute(current[half:], axis_name, _pair_perm(count, bit))
    return current


def _all_gather(x, axis_name, axis, bits):
    count = lax.axis_size(axis_name)
    current = x
    for bit in bits:
        other = lax.ppermute(current, axis_name, _pair_perm(count, bit))
        current = jnp.concatenate([current, other], axis=axis)
    return current


def _exchange(x, axis_name):
    count = lax.axis_size(axis_name)
    if count > 4:
        return _all_gather(x[None], axis_name, 0, list(range(count.bit_length() - 1)))
    parts = [x] + [lax.ppermute(x, axis_name, [(i, i ^ p) for i in range(count)]) for p in range(1, count)]
    return jnp.stack(parts, axis=0)


def shards(
    panels,
    panel_slot,
    panel_cell,
    bloch_k,
    leaf_inverse,
    level_left,
    level_right,
    block_left,
    block_right,
    block_coupling,
    rank_count,
    quad_weight,
):
    local_angles = leaf_inverse.shape[0]
    assert local_angles == 1
    row_count = leaf_inverse.shape[2]
    panel_count = panels.shape[1]
    local_sources = panels.shape[2]
    panel_width = panels.shape[4]
    slot_count = row_count // panel_width
    source_count = local_sources * lax.axis_size("ang")
    rank_width = block_right.shape[2]
    levels = level_right.shape[1]

    cell_float = panel_cell[0].astype(jnp.float32)
    own_wave = lax.dynamic_slice_in_dim(bloch_k, lax.axis_index("ang") * local_angles, local_angles, 0)
    theta = own_wave[0, 0] * cell_float[:, 0] + own_wave[0, 1] * cell_float[:, 1]
    own_cos = lax.reduce_precision(jnp.cos(theta), exponent_bits=8, mantissa_bits=7)
    own_sin = lax.reduce_precision(jnp.sin(theta), exponent_bits=8, mantissa_bits=7)

    local_panels = panels[0].reshape(panel_count, local_sources, 2 * panel_width)
    ang_bits = lax.axis_size("ang").bit_length() - 1
    gathered = _all_gather(local_panels, "ang", 1, list(range(ang_bits))[::-1])
    rank = rank_count[0].reshape(1)

    excitation, projected = pl.pallas_call(
        _excite_kernel,
        out_shape=(
            jax.ShapeDtypeStruct((2, source_count, row_count), jnp.bfloat16),
            jax.ShapeDtypeStruct((2, source_count, rank_width), jnp.bfloat16),
        ),
        in_specs=[_SMEM, _SMEM, _SMEM, _SMEM, _VMEM, _VMEM],
        out_specs=(_VMEM, _VMEM),
        scratch_shapes=[
            pltpu.VMEM((slot_count, source_count, panel_width), jnp.float32),
            pltpu.VMEM((slot_count, source_count, panel_width), jnp.float32),
        ],
    )(panel_slot[0], own_cos, own_sin, rank, gathered, block_right[0])

    row_blocks = lax.axis_size("row")
    all_projected = _exchange(projected, "row")
    me = lax.axis_index("row")
    coupling = block_coupling[0, 0]
    coupling = coupling.reshape(2, rank_width, row_blocks, coupling.shape[2] // row_blocks)
    coupling = jnp.take(coupling, me ^ jnp.arange(row_blocks), axis=2).reshape(block_coupling.shape[2:])

    near = pl.pallas_call(
        _near_kernel,
        out_shape=jax.ShapeDtypeStruct((source_count, 2 * row_count), jnp.float32),
        in_specs=[_VMEM] * 4,
        out_specs=_VMEM,
        scratch_shapes=[pltpu.VMEM((2 ** (levels + 1) - 2, 2, source_count, rank_width), jnp.bfloat16)],
    )(excitation, leaf_inverse[0], level_right[0], level_left[0])

    half = source_count // 2
    halves = []
    for h in (1, 0):
        halves.append(pl.pallas_call(
            _far_kernel,
            out_shape=jax.ShapeDtypeStruct((half, 2 * row_count), jnp.float32),
            grid=(1,),
            in_specs=[
                _SMEM,
                _SMEM,
                pl.BlockSpec((half, 2 * row_count), lambda i, h=h: (h, 0)),
                pl.BlockSpec(block_left.shape[1:], lambda i: (0, 0, 0)),
                pl.BlockSpec(coupling.shape, lambda i: (0, 0, 0)),
                pl.BlockSpec((row_blocks, 2, half, rank_width), lambda i, h=h: (0, 0, h, 0)),
            ],
            out_specs=pl.BlockSpec((half, 2 * row_count), lambda i: (0, 0)),
            scratch_shapes=[pltpu.VMEM((2, half, rank_width), jnp.bfloat16)],
        )(quad_weight[0], rank, near, block_left[0], coupling, all_projected))
    summed = _reduce_scatter(halves[1], halves[0], "ang")
    return summed.reshape(summed.shape[0], 2, row_count)


def solution(mesh):
    placed = (
        P("row", None, "ang", None, None),
        P("row", None),
        P("row", None, None),
        P(),
        P("ang", None, "row", None),
        P("ang", None, None, None, "row"),
        P("ang", None, None, None, "row"),
        P("ang", None, None, "row"),
        P("ang", None, None, "row"),
        P("ang", "row", None, None, None),
        P("ang", "row"),
        P("ang", None),
    )
    return jax.shard_map(
        shards, mesh=mesh, in_specs=placed, out_specs=P("ang", None, "row"), check_vma=False
    )
```

```python
import jax
import jax.numpy as jnp
from jax import lax
from jax.experimental import pallas as pl
from jax.experimental.pallas import tpu as pltpu
from jax.sharding import PartitionSpec as P

LEAF = 256

_SMEM = pl.BlockSpec(memory_space=pltpu.MemorySpace.SMEM)
_VMEM = pl.BlockSpec(memory_space=pltpu.MemorySpace.VMEM)


def _nt(a, b):
    return lax.dot_general(a, b, (((1,), (1,)), ((), ())), preferred_element_type=jnp.float32)


def _nn(a, b):
    return lax.dot_general(a, b, (((1,), (0,)), ((), ())), preferred_element_type=jnp.float32)


def _rank_mask(rank_ref, shape):
    return lax.broadcasted_iota(jnp.int32, shape, 0) < rank_ref[0]


def _excite_kernel(slot_ref, cos_ref, sin_ref, rank_ref, ga_ref, gb_ref, br_ref, e_ref, bp_ref, acc_re, acc_im):
    panel_count, part, width2 = ga_ref.shape
    width = width2 // 2
    slots = acc_re.shape[0]
    acc_re[...] = jnp.zeros(acc_re.shape, jnp.float32)
    acc_im[...] = jnp.zeros(acc_im.shape, jnp.float32)

    def body(q, carry):
        k = slot_ref[q]
        c = cos_ref[q]
        s = sin_ref[q]
        for rows, g_ref in ((slice(0, part), ga_ref), (slice(part, 2 * part), gb_ref)):
            p_re = g_ref[q, :, :width].astype(jnp.float32)
            p_im = g_ref[q, :, width:].astype(jnp.float32)
            acc_re[k, rows] = acc_re[k, rows] + (c * p_re + s * p_im)
            acc_im[k, rows] = acc_im[k, rows] + (c * p_im - s * p_re)
        return carry

    lax.fori_loop(0, panel_count, body, 0)
    for k in range(slots):
        e_ref[0, :, k * width:(k + 1) * width] = acc_re[k].astype(jnp.bfloat16)
        e_ref[1, :, k * width:(k + 1) * width] = acc_im[k].astype(jnp.bfloat16)
    e_re = e_ref[0]
    e_im = e_ref[1]
    keep = _rank_mask(rank_ref, br_ref.shape[1:])
    zero = jnp.zeros(br_ref.shape[1:], jnp.bfloat16)
    r_re = jnp.where(keep, br_ref[0], zero)
    r_im = jnp.where(keep, br_ref[1], zero)
    bp_ref[0] = (_nt(e_re, r_re) - _nt(e_im, r_im)).astype(jnp.bfloat16)
    bp_ref[1] = (_nt(e_re, r_im) + _nt(e_im, r_re)).astype(jnp.bfloat16)


def _near_kernel(e_ref, leaf_ref, lr_ref, ll_ref, out_ref, pj_ref):
    _, source_count, row_count = e_ref.shape
    levels = lr_ref.shape[0]
    e_re = e_ref[0]
    e_im = e_ref[1]

    first_group = []
    slot = 0
    for j in range(levels):
        node = row_count // 2 ** (j + 1)
        first_group.append(slot)
        for g in range(2 ** (j + 1)):
            cols = slice(g * node, (g + 1) * node)
            a = e_re[:, cols]
            b = e_im[:, cols]
            r_re = lr_ref[j, 0, :, cols]
            r_im = lr_ref[j, 1, :, cols]
            pj_ref[slot, 0] = (_nt(a, r_re) - _nt(b, r_im)).astype(jnp.bfloat16)
            pj_ref[slot, 1] = (_nt(a, r_im) + _nt(b, r_re)).astype(jnp.bfloat16)
            slot += 1

    for l in range(row_count // LEAF):
        cols = slice(l * LEAF, (l + 1) * LEAF)
        a = e_re[:, cols]
        b = e_im[:, cols]
        lf_re = leaf_ref[0, cols, :]
        lf_im = leaf_ref[1, cols, :]
        f_re = _nt(a, lf_re) - _nt(b, lf_im)
        f_im = _nt(a, lf_im) + _nt(b, lf_re)
        for j in range(levels):
            node = row_count // 2 ** (j + 1)
            g = (l * LEAF) // node
            p_re = pj_ref[first_group[j] + (g ^ 1), 0]
            p_im = pj_ref[first_group[j] + (g ^ 1), 1]
            m_re = ll_ref[j, 0, :, cols]
            m_im = ll_ref[j, 1, :, cols]
            f_re = f_re + (_nn(p_re, m_re) - _nn(p_im, m_im))
            f_im = f_im + (_nn(p_re, m_im) + _nn(p_im, m_re))
        out_ref[:, cols] = f_re
        out_ref[:, row_count + l * LEAF:row_count + (l + 1) * LEAF] = f_im


def _far_kernel(qw_ref, rank_ref, near_ref, bl_ref, cp_ref, bpa_ref, out_ref, cu_ref):
    source_count = near_ref.shape[0]
    row_count = bl_ref.shape[2]
    rank_width = bl_ref.shape[1]
    blocks = bpa_ref.shape[0]
    coupling_rank = bpa_ref.shape[3]

    c_re = jnp.zeros((source_count, rank_width), jnp.float32)
    c_im = jnp.zeros((source_count, rank_width), jnp.float32)
    for u in range(1, blocks):
        b_re = bpa_ref[u, 0]
        b_im = bpa_ref[u, 1]
        k_re = cp_ref[0, :, u * coupling_rank:(u + 1) * coupling_rank]
        k_im = cp_ref[1, :, u * coupling_rank:(u + 1) * coupling_rank]
        c_re = c_re + (_nt(b_re, k_re) - _nt(b_im, k_im))
        c_im = c_im + (_nt(b_re, k_im) + _nt(b_im, k_re))
    cu_ref[0] = c_re.astype(jnp.bfloat16)
    cu_ref[1] = c_im.astype(jnp.bfloat16)
    coupled_re = cu_ref[0]
    coupled_im = cu_ref[1]

    w_re = qw_ref[0]
    w_im = qw_ref[1]
    for l in range(row_count // LEAF):
        cols = slice(l * LEAF, (l + 1) * LEAF)
        imag_cols = slice(row_count + l * LEAF, row_count + (l + 1) * LEAF)
        keep = _rank_mask(rank_ref, (rank_width, LEAF))
        zero = jnp.zeros((rank_width, LEAF), jnp.bfloat16)
        q_re = jnp.where(keep, bl_ref[0, :, cols], zero)
        q_im = jnp.where(keep, bl_ref[1, :, cols], zero)
        f_re = near_ref[:, cols] + (_nn(coupled_re, q_re) - _nn(coupled_im, q_im))
        f_im = near_ref[:, imag_cols] + (_nn(coupled_re, q_im) + _nn(coupled_im, q_re))
        out_ref[:, cols] = w_re * f_re - w_im * f_im
        out_ref[:, imag_cols] = w_re * f_im + w_im * f_re


def _pair_perm(count, bit):
    return [(i, i ^ (1 << bit)) for i in range(count)]


def _reduce_scatter(keep, give, axis_name, shape):
    count = lax.axis_size(axis_name)
    bits = count.bit_length() - 1
    got = lax.ppermute(give, axis_name, _pair_perm(count, 0))
    for bit in range(1, bits):
        current = keep + got
        half = current.shape[0] // 2
        keep = current[:half]
        got = lax.ppermute(current[half:], axis_name, _pair_perm(count, bit))
    return keep.reshape(shape) + got.reshape(shape)


def _all_gather(x, axis_name, axis, bits, companions=()):
    count = lax.axis_size(axis_name)
    current = x
    for step, bit in enumerate(bits):
        if step == 1 and companions:
            current, companions = lax.optimization_barrier((current, companions))
        other = lax.ppermute(current, axis_name, _pair_perm(count, bit))
        if step == len(bits) - 1:
            return current, other, companions
        current = jnp.concatenate([current, other], axis=axis)


def _exchange(x, axis_name):
    count = lax.axis_size(axis_name)
    if count > 4:
        current, other, _ = _all_gather(x[None], axis_name, 0, list(range(count.bit_length() - 1)))
        return jnp.concatenate([current, other], axis=0)
    parts = [x] + [lax.ppermute(x, axis_name, [(i, i ^ p) for i in range(count)]) for p in range(1, count)]
    return jnp.stack(parts, axis=0)


def shards(
    panels,
    panel_slot,
    panel_cell,
    bloch_k,
    leaf_inverse,
    level_left,
    level_right,
    block_left,
    block_right,
    block_coupling,
    rank_count,
    quad_weight,
):
    local_angles = leaf_inverse.shape[0]
    assert local_angles == 1
    row_count = leaf_inverse.shape[2]
    panel_count = panels.shape[1]
    local_sources = panels.shape[2]
    panel_width = panels.shape[4]
    slot_count = row_count // panel_width
    source_count = local_sources * lax.axis_size("ang")
    rank_width = block_right.shape[2]
    levels = level_right.shape[1]

    cell_float = panel_cell[0].astype(jnp.float32)
    own_wave = lax.dynamic_slice_in_dim(bloch_k, lax.axis_index("ang") * local_angles, local_angles, 0)
    theta = own_wave[0, 0] * cell_float[:, 0] + own_wave[0, 1] * cell_float[:, 1]
    own_cos = lax.reduce_precision(jnp.cos(theta), exponent_bits=8, mantissa_bits=7)
    own_sin = lax.reduce_precision(jnp.sin(theta), exponent_bits=8, mantissa_bits=7)

    local_panels = panels[0].reshape(panel_count, local_sources, 2 * panel_width)
    ang_bits = lax.axis_size("ang").bit_length() - 1
    first, second, (own_cos, own_sin) = _all_gather(
        local_panels, "ang", 1, list(range(ang_bits))[::-1], (own_cos, own_sin))
    rank = rank_count[0].reshape(1)

    excitation, projected = pl.pallas_call(
        _excite_kernel,
        out_shape=(
            jax.ShapeDtypeStruct((2, source_count, row_count), jnp.bfloat16),
            jax.ShapeDtypeStruct((2, source_count, rank_width), jnp.bfloat16),
        ),
        in_specs=[_SMEM, _SMEM, _SMEM, _SMEM, _VMEM, _VMEM, _VMEM],
        out_specs=(_VMEM, _VMEM),
        scratch_shapes=[
            pltpu.VMEM((slot_count, source_count, panel_width), jnp.float32),
            pltpu.VMEM((slot_count, source_count, panel_width), jnp.float32),
        ],
    )(panel_slot[0], own_cos, own_sin, rank, first, second, block_right[0])

    row_blocks = lax.axis_size("row")
    all_projected = _exchange(projected, "row")
    me = lax.axis_index("row")
    coupling = block_coupling[0, 0]
    coupling = coupling.reshape(2, rank_width, row_blocks, coupling.shape[2] // row_blocks)
    coupling = jnp.take(coupling, me ^ jnp.arange(row_blocks), axis=2).reshape(block_coupling.shape[2:])

    near = pl.pallas_call(
        _near_kernel,
        out_shape=jax.ShapeDtypeStruct((source_count, 2 * row_count), jnp.float32),
        in_specs=[_VMEM] * 4,
        out_specs=_VMEM,
        scratch_shapes=[pltpu.VMEM((2 ** (levels + 1) - 2, 2, source_count, rank_width), jnp.bfloat16)],
    )(excitation, leaf_inverse[0], level_right[0], level_left[0])

    half = source_count // 2
    halves = []
    for h in (1, 0):
        halves.append(pl.pallas_call(
            _far_kernel,
            out_shape=jax.ShapeDtypeStruct((half, 2 * row_count), jnp.float32),
            grid=(1,),
            in_specs=[
                _SMEM,
                _SMEM,
                pl.BlockSpec((half, 2 * row_count), lambda i, h=h: (h, 0)),
                pl.BlockSpec(block_left.shape[1:], lambda i: (0, 0, 0)),
                pl.BlockSpec(coupling.shape, lambda i: (0, 0, 0)),
                pl.BlockSpec((row_blocks, 2, half, rank_width), lambda i, h=h: (0, 0, h, 0)),
            ],
            out_specs=pl.BlockSpec((half, 2 * row_count), lambda i: (0, 0)),
            scratch_shapes=[pltpu.VMEM((2, half, rank_width), jnp.bfloat16)],
        )(quad_weight[0], rank, near, block_left[0], coupling, all_projected))
    return _reduce_scatter(halves[1], halves[0], "ang", (local_sources, 2, row_count))


def solution(mesh):
    placed = (
        P("row", None, "ang", None, None),
        P("row", None),
        P("row", None, None),
        P(),
        P("ang", None, "row", None),
        P("ang", None, None, None, "row"),
        P("ang", None, None, None, "row"),
        P("ang", None, None, "row"),
        P("ang", None, None, "row"),
        P("ang", "row", None, None, None),
        P("ang", "row"),
        P("ang", None),
    )
    return jax.shard_map(
        shards, mesh=mesh, in_specs=placed, out_specs=P("ang", None, "row"), check_vma=False
    )
```

```python
import jax
import jax.numpy as jnp
from jax import lax
from jax.experimental import pallas as pl
from jax.experimental.pallas import tpu as pltpu
from jax.sharding import PartitionSpec as P

LEAF = 256

_SMEM = pl.BlockSpec(memory_space=pltpu.MemorySpace.SMEM)
_VMEM = pl.BlockSpec(memory_space=pltpu.MemorySpace.VMEM)


def _nt(a, b):
    return lax.dot_general(a, b, (((1,), (1,)), ((), ())), preferred_element_type=jnp.float32)


def _nn(a, b):
    return lax.dot_general(a, b, (((1,), (0,)), ((), ())), preferred_element_type=jnp.float32)


def _rank_mask(rank_ref, shape):
    return lax.broadcasted_iota(jnp.int32, shape, 0) < rank_ref[0]


def _excite_kernel(slot_ref, cos_ref, sin_ref, rank_ref, ga_ref, gb_ref, br_ref, e_ref, bp_ref, acc_re, acc_im):
    panel_count, part, width2 = ga_ref.shape
    width = width2 // 2
    slots = acc_re.shape[0]
    acc_re[...] = jnp.zeros(acc_re.shape, jnp.float32)
    acc_im[...] = jnp.zeros(acc_im.shape, jnp.float32)

    def body(q, carry):
        k = slot_ref[q]
        c = cos_ref[q]
        s = sin_ref[q]
        for rows, g_ref in ((slice(0, part), ga_ref), (slice(part, 2 * part), gb_ref)):
            p_re = g_ref[q, :, :width].astype(jnp.float32)
            p_im = g_ref[q, :, width:].astype(jnp.float32)
            acc_re[k, rows] = acc_re[k, rows] + (c * p_re + s * p_im)
            acc_im[k, rows] = acc_im[k, rows] + (c * p_im - s * p_re)
        return carry

    lax.fori_loop(0, panel_count, body, 0)
    for k in range(slots):
        e_ref[0, :, k * width:(k + 1) * width] = acc_re[k].astype(jnp.bfloat16)
        e_ref[1, :, k * width:(k + 1) * width] = acc_im[k].astype(jnp.bfloat16)
    e_re = e_ref[0]
    e_im = e_ref[1]
    keep = _rank_mask(rank_ref, br_ref.shape[1:])
    zero = jnp.zeros(br_ref.shape[1:], jnp.bfloat16)
    r_re = jnp.where(keep, br_ref[0], zero)
    r_im = jnp.where(keep, br_ref[1], zero)
    bp_ref[0] = (_nt(e_re, r_re) - _nt(e_im, r_im)).astype(jnp.bfloat16)
    bp_ref[1] = (_nt(e_re, r_im) + _nt(e_im, r_re)).astype(jnp.bfloat16)


def _near_kernel(e_ref, leaf_ref, lr_ref, ll_ref, out_ref, pj_ref):
    _, source_count, row_count = e_ref.shape
    levels = lr_ref.shape[0]
    e_re = e_ref[0]
    e_im = e_ref[1]

    first_group = []
    slot = 0
    for j in range(levels):
        node = row_count // 2 ** (j + 1)
        first_group.append(slot)
        for g in range(2 ** (j + 1)):
            cols = slice(g * node, (g + 1) * node)
            a = e_re[:, cols]
            b = e_im[:, cols]
            r_re = lr_ref[j, 0, :, cols]
            r_im = lr_ref[j, 1, :, cols]
            pj_ref[slot, 0] = (_nt(a, r_re) - _nt(b, r_im)).astype(jnp.bfloat16)
            pj_ref[slot, 1] = (_nt(a, r_im) + _nt(b, r_re)).astype(jnp.bfloat16)
            slot += 1

    for l in range(row_count // LEAF):
        cols = slice(l * LEAF, (l + 1) * LEAF)
        a = e_re[:, cols]
        b = e_im[:, cols]
        lf_re = leaf_ref[0, cols, :]
        lf_im = leaf_ref[1, cols, :]
        f_re = _nt(a, lf_re) - _nt(b, lf_im)
        f_im = _nt(a, lf_im) + _nt(b, lf_re)
        for j in range(levels):
            node = row_count // 2 ** (j + 1)
            g = (l * LEAF) // node
            p_re = pj_ref[first_group[j] + (g ^ 1), 0]
            p_im = pj_ref[first_group[j] + (g ^ 1), 1]
            m_re = ll_ref[j, 0, :, cols]
            m_im = ll_ref[j, 1, :, cols]
            f_re = f_re + (_nn(p_re, m_re) - _nn(p_im, m_im))
            f_im = f_im + (_nn(p_re, m_im) + _nn(p_im, m_re))
        out_ref[:, cols] = f_re
        out_ref[:, row_count + l * LEAF:row_count + (l + 1) * LEAF] = f_im


def _far_kernel(qw_ref, rank_ref, near_ref, bl_ref, cp_ref, bpa_ref, out_ref, cu_ref):
    source_count = near_ref.shape[0]
    row_count = bl_ref.shape[2]
    rank_width = bl_ref.shape[1]
    blocks = bpa_ref.shape[0]
    coupling_rank = bpa_ref.shape[3]

    c_re = jnp.zeros((source_count, rank_width), jnp.float32)
    c_im = jnp.zeros((source_count, rank_width), jnp.float32)
    for u in range(1, blocks):
        b_re = bpa_ref[u, 0]
        b_im = bpa_ref[u, 1]
        k_re = cp_ref[0, :, u * coupling_rank:(u + 1) * coupling_rank]
        k_im = cp_ref[1, :, u * coupling_rank:(u + 1) * coupling_rank]
        c_re = c_re + (_nt(b_re, k_re) - _nt(b_im, k_im))
        c_im = c_im + (_nt(b_re, k_im) + _nt(b_im, k_re))
    cu_ref[0] = c_re.astype(jnp.bfloat16)
    cu_ref[1] = c_im.astype(jnp.bfloat16)
    coupled_re = cu_ref[0]
    coupled_im = cu_ref[1]

    w_re = qw_ref[0]
    w_im = qw_ref[1]
    for l in range(row_count // LEAF):
        cols = slice(l * LEAF, (l + 1) * LEAF)
        imag_cols = slice(row_count + l * LEAF, row_count + (l + 1) * LEAF)
        keep = _rank_mask(rank_ref, (rank_width, LEAF))
        zero = jnp.zeros((rank_width, LEAF), jnp.bfloat16)
        q_re = jnp.where(keep, bl_ref[0, :, cols], zero)
        q_im = jnp.where(keep, bl_ref[1, :, cols], zero)
        f_re = near_ref[:, cols] + (_nn(coupled_re, q_re) - _nn(coupled_im, q_im))
        f_im = near_ref[:, imag_cols] + (_nn(coupled_re, q_im) + _nn(coupled_im, q_re))
        out_ref[:, cols] = w_re * f_re - w_im * f_im
        out_ref[:, imag_cols] = w_re * f_im + w_im * f_re


def _bit_groups(count):
    bits = count.bit_length() - 1
    groups = [[b, b - 1] for b in range(bits - 1, 1, -2)]
    rest = [b for b in range(bits) if all(b not in g for g in groups)]
    return groups + [[b] for b in rest[::-1]]


def _offset(value, group):
    return sum(1 << b for k, b in enumerate(group) if (value >> k) & 1)


def _permute(x, axis_name, count, offset):
    return lax.ppermute(x, axis_name, [(i, i ^ offset) for i in range(count)])


def _all_gather(x, axis_name, axis, companions=()):
    count = lax.axis_size(axis_name)
    groups = _bit_groups(count)
    current = x
    for step, group in enumerate(groups):
        if step == 1 and companions:
            current, companions = lax.optimization_barrier((current, companions))
        parts = [current] + [_permute(current, axis_name, count, _offset(j, group)) for j in range(1, 2 ** len(group))]
        if step == len(groups) - 1:
            return parts, companions
        current = jnp.concatenate(parts, axis=axis)


def _reduce_scatter(keep, give, axis_name, shape):
    count = lax.axis_size(axis_name)
    groups = _bit_groups(count)
    flat = sum(groups, [])

    def offset_of(position):
        return sum(1 << flat[k] for k in range(len(flat)) if (position >> k) & 1)

    chunks = 2 * keep.shape[0] // shape[0]
    current = keep + _permute(give, axis_name, count, offset_of(chunks // 2))
    chunks //= 2
    for group in groups[::-1][1:]:
        size = 2 ** len(group)
        block = chunks // size
        rows = block * shape[0]
        total = current[:rows]
        for t in range(1, size):
            part = current[t * rows:(t + 1) * rows]
            total = total + _permute(part, axis_name, count, offset_of(t * block))
        current = total
        chunks = block
    return current.reshape(shape)


def _position_offsets(count):
    if count <= 4:
        return list(range(count))
    flat = sum(_bit_groups(count), [])
    return [sum(1 << flat[k] for k in range(len(flat)) if (p >> k) & 1) for p in range(count)]


def _exchange(x, axis_name):
    count = lax.axis_size(axis_name)
    if count > 4:
        parts, _ = _all_gather(x[None], axis_name, 0)
        return jnp.concatenate(parts, axis=0)
    parts = [x] + [lax.ppermute(x, axis_name, [(i, i ^ p) for i in range(count)]) for p in range(1, count)]
    return jnp.stack(parts, axis=0)


def shards(
    panels,
    panel_slot,
    panel_cell,
    bloch_k,
    leaf_inverse,
    level_left,
    level_right,
    block_left,
    block_right,
    block_coupling,
    rank_count,
    quad_weight,
):
    local_angles = leaf_inverse.shape[0]
    assert local_angles == 1
    row_count = leaf_inverse.shape[2]
    panel_count = panels.shape[1]
    local_sources = panels.shape[2]
    panel_width = panels.shape[4]
    slot_count = row_count // panel_width
    source_count = local_sources * lax.axis_size("ang")
    rank_width = block_right.shape[2]
    levels = level_right.shape[1]

    cell_float = panel_cell[0].astype(jnp.float32)
    own_wave = lax.dynamic_slice_in_dim(bloch_k, lax.axis_index("ang") * local_angles, local_angles, 0)
    theta = own_wave[0, 0] * cell_float[:, 0] + own_wave[0, 1] * cell_float[:, 1]
    own_cos = lax.reduce_precision(jnp.cos(theta), exponent_bits=8, mantissa_bits=7)
    own_sin = lax.reduce_precision(jnp.sin(theta), exponent_bits=8, mantissa_bits=7)

    local_panels = panels[0].reshape(panel_count, local_sources, 2 * panel_width)
    (first, second), (own_cos, own_sin) = _all_gather(local_panels, "ang", 1, (own_cos, own_sin))
    rank = rank_count[0].reshape(1)

    excitation, projected = pl.pallas_call(
        _excite_kernel,
        out_shape=(
            jax.ShapeDtypeStruct((2, source_count, row_count), jnp.bfloat16),
            jax.ShapeDtypeStruct((2, source_count, rank_width), jnp.bfloat16),
        ),
        in_specs=[_SMEM, _SMEM, _SMEM, _SMEM, _VMEM, _VMEM, _VMEM],
        out_specs=(_VMEM, _VMEM),
        scratch_shapes=[
            pltpu.VMEM((slot_count, source_count, panel_width), jnp.float32),
            pltpu.VMEM((slot_count, source_count, panel_width), jnp.float32),
        ],
    )(panel_slot[0], own_cos, own_sin, rank, first, second, block_right[0])

    row_blocks = lax.axis_size("row")
    all_projected = _exchange(projected, "row")
    me = lax.axis_index("row")
    coupling = block_coupling[0, 0]
    coupling = coupling.reshape(2, rank_width, row_blocks, coupling.shape[2] // row_blocks)
    offsets = jnp.array(_position_offsets(row_blocks), jnp.int32)
    coupling = jnp.take(coupling, me ^ offsets, axis=2).reshape(block_coupling.shape[2:])

    near = pl.pallas_call(
        _near_kernel,
        out_shape=jax.ShapeDtypeStruct((source_count, 2 * row_count), jnp.float32),
        in_specs=[_VMEM] * 4,
        out_specs=_VMEM,
        scratch_shapes=[pltpu.VMEM((2 ** (levels + 1) - 2, 2, source_count, rank_width), jnp.bfloat16)],
    )(excitation, leaf_inverse[0], level_right[0], level_left[0])

    half = source_count // 2
    halves = []
    for h in (1, 0):
        halves.append(pl.pallas_call(
            _far_kernel,
            out_shape=jax.ShapeDtypeStruct((half, 2 * row_count), jnp.float32),
            grid=(1,),
            in_specs=[
                _SMEM,
                _SMEM,
                pl.BlockSpec((half, 2 * row_count), lambda i, h=h: (h, 0)),
                pl.BlockSpec(block_left.shape[1:], lambda i: (0, 0, 0)),
                pl.BlockSpec(coupling.shape, lambda i: (0, 0, 0)),
                pl.BlockSpec((row_blocks, 2, half, rank_width), lambda i, h=h: (0, 0, h, 0)),
            ],
            out_specs=pl.BlockSpec((half, 2 * row_count), lambda i: (0, 0)),
            scratch_shapes=[pltpu.VMEM((2, half, rank_width), jnp.bfloat16)],
        )(quad_weight[0], rank, near, block_left[0], coupling, all_projected))
    return _reduce_scatter(halves[1], halves[0], "ang", (local_sources, 2, row_count))


def solution(mesh):
    placed = (
        P("row", None, "ang", None, None),
        P("row", None),
        P("row", None, None),
        P(),
        P("ang", None, "row", None),
        P("ang", None, None, None, "row"),
        P("ang", None, None, None, "row"),
        P("ang", None, None, "row"),
        P("ang", None, None, "row"),
        P("ang", "row", None, None, None),
        P("ang", "row"),
        P("ang", None),
    )
    return jax.shard_map(
        shards, mesh=mesh, in_specs=placed, out_specs=P("ang", None, "row"), check_vma=False
    )
```

```python
import jax
import jax.numpy as jnp
from jax import lax
from jax.experimental import pallas as pl
from jax.experimental.pallas import tpu as pltpu
from jax.sharding import PartitionSpec as P

LEAF = 256

_SMEM = pl.BlockSpec(memory_space=pltpu.MemorySpace.SMEM)
_VMEM = pl.BlockSpec(memory_space=pltpu.MemorySpace.VMEM)


def _nt(a, b):
    return lax.dot_general(a, b, (((1,), (1,)), ((), ())), preferred_element_type=jnp.float32)


def _nn(a, b):
    return lax.dot_general(a, b, (((1,), (0,)), ((), ())), preferred_element_type=jnp.float32)


def _rank_mask(rank_ref, shape):
    return lax.broadcasted_iota(jnp.int32, shape, 0) < rank_ref[0]


def _excite_kernel(slot_ref, cos_ref, sin_ref, rank_ref, ga_ref, gb_ref, br_ref, e_ref, bp_ref, acc_re, acc_im):
    panel_count, part, width2 = ga_ref.shape
    width = width2 // 2
    slots = acc_re.shape[0]
    acc_re[...] = jnp.zeros(acc_re.shape, jnp.float32)
    acc_im[...] = jnp.zeros(acc_im.shape, jnp.float32)

    def body(q, carry):
        k = slot_ref[q]
        c = cos_ref[q]
        s = sin_ref[q]
        for rows, g_ref in ((slice(0, part), ga_ref), (slice(part, 2 * part), gb_ref)):
            p_re = g_ref[q, :, :width].astype(jnp.float32)
            p_im = g_ref[q, :, width:].astype(jnp.float32)
            acc_re[k, rows] = acc_re[k, rows] + (c * p_re + s * p_im)
            acc_im[k, rows] = acc_im[k, rows] + (c * p_im - s * p_re)
        return carry

    lax.fori_loop(0, panel_count, body, 0)
    for k in range(slots):
        e_ref[0, :, k * width:(k + 1) * width] = acc_re[k].astype(jnp.bfloat16)
        e_ref[1, :, k * width:(k + 1) * width] = acc_im[k].astype(jnp.bfloat16)
    e_re = e_ref[0]
    e_im = e_ref[1]
    keep = _rank_mask(rank_ref, br_ref.shape[1:])
    zero = jnp.zeros(br_ref.shape[1:], jnp.bfloat16)
    r_re = jnp.where(keep, br_ref[0], zero)
    r_im = jnp.where(keep, br_ref[1], zero)
    bp_ref[0] = (_nt(e_re, r_re) - _nt(e_im, r_im)).astype(jnp.bfloat16)
    bp_ref[1] = (_nt(e_re, r_im) + _nt(e_im, r_re)).astype(jnp.bfloat16)


def _near_kernel(e_ref, leaf_ref, lr_ref, ll_ref, out_ref, pj_ref):
    _, source_count, row_count = e_ref.shape
    levels = lr_ref.shape[0]
    e_re = e_ref[0]
    e_im = e_ref[1]

    first_group = []
    slot = 0
    for j in range(levels):
        node = row_count // 2 ** (j + 1)
        first_group.append(slot)
        for g in range(2 ** (j + 1)):
            cols = slice(g * node, (g + 1) * node)
            a = e_re[:, cols]
            b = e_im[:, cols]
            r_re = lr_ref[j, 0, :, cols]
            r_im = lr_ref[j, 1, :, cols]
            pj_ref[slot, 0] = (_nt(a, r_re) - _nt(b, r_im)).astype(jnp.bfloat16)
            pj_ref[slot, 1] = (_nt(a, r_im) + _nt(b, r_re)).astype(jnp.bfloat16)
            slot += 1

    for l in range(row_count // LEAF):
        cols = slice(l * LEAF, (l + 1) * LEAF)
        a = e_re[:, cols]
        b = e_im[:, cols]
        lf_re = leaf_ref[0, cols, :]
        lf_im = leaf_ref[1, cols, :]
        f_re = _nt(a, lf_re) - _nt(b, lf_im)
        f_im = _nt(a, lf_im) + _nt(b, lf_re)
        for j in range(levels):
            node = row_count // 2 ** (j + 1)
            g = (l * LEAF) // node
            p_re = pj_ref[first_group[j] + (g ^ 1), 0]
            p_im = pj_ref[first_group[j] + (g ^ 1), 1]
            m_re = ll_ref[j, 0, :, cols]
            m_im = ll_ref[j, 1, :, cols]
            f_re = f_re + (_nn(p_re, m_re) - _nn(p_im, m_im))
            f_im = f_im + (_nn(p_re, m_im) + _nn(p_im, m_re))
        out_ref[:, cols] = f_re
        out_ref[:, row_count + l * LEAF:row_count + (l + 1) * LEAF] = f_im


def _far_kernel(qw_ref, rank_ref, near_ref, bl_ref, cp_ref, *refs):
    part_refs = refs[:-2]
    out_ref, cu_ref = refs[-2:]
    source_count = near_ref.shape[0]
    row_count = bl_ref.shape[2]
    rank_width = bl_ref.shape[1]
    blocks = len(part_refs) + 1
    coupling_rank = part_refs[0].shape[2]

    c_re = jnp.zeros((source_count, rank_width), jnp.float32)
    c_im = jnp.zeros((source_count, rank_width), jnp.float32)
    for u in range(1, blocks):
        b_re = part_refs[u - 1][0]
        b_im = part_refs[u - 1][1]
        k_re = cp_ref[0, :, u * coupling_rank:(u + 1) * coupling_rank]
        k_im = cp_ref[1, :, u * coupling_rank:(u + 1) * coupling_rank]
        c_re = c_re + (_nt(b_re, k_re) - _nt(b_im, k_im))
        c_im = c_im + (_nt(b_re, k_im) + _nt(b_im, k_re))
    cu_ref[0] = c_re.astype(jnp.bfloat16)
    cu_ref[1] = c_im.astype(jnp.bfloat16)
    coupled_re = cu_ref[0]
    coupled_im = cu_ref[1]

    w_re = qw_ref[0]
    w_im = qw_ref[1]
    for l in range(row_count // LEAF):
        cols = slice(l * LEAF, (l + 1) * LEAF)
        imag_cols = slice(row_count + l * LEAF, row_count + (l + 1) * LEAF)
        keep = _rank_mask(rank_ref, (rank_width, LEAF))
        zero = jnp.zeros((rank_width, LEAF), jnp.bfloat16)
        q_re = jnp.where(keep, bl_ref[0, :, cols], zero)
        q_im = jnp.where(keep, bl_ref[1, :, cols], zero)
        f_re = near_ref[:, cols] + (_nn(coupled_re, q_re) - _nn(coupled_im, q_im))
        f_im = near_ref[:, imag_cols] + (_nn(coupled_re, q_im) + _nn(coupled_im, q_re))
        out_ref[:, cols] = w_re * f_re - w_im * f_im
        out_ref[:, imag_cols] = w_re * f_im + w_im * f_re


def _bit_groups(count):
    bits = count.bit_length() - 1
    groups = [[b, b - 1] for b in range(bits - 1, 1, -2)]
    rest = [b for b in range(bits) if all(b not in g for g in groups)]
    return groups + [[b] for b in rest[::-1]]


def _offset(value, group):
    return sum(1 << b for k, b in enumerate(group) if (value >> k) & 1)


def _permute(x, axis_name, count, offset):
    return lax.ppermute(x, axis_name, [(i, i ^ offset) for i in range(count)])


def _all_gather(x, axis_name, axis, companions=()):
    count = lax.axis_size(axis_name)
    groups = _bit_groups(count)
    current = x
    for step, group in enumerate(groups):
        if step == 1 and companions:
            current, companions = lax.optimization_barrier((current, companions))
        parts = [current] + [_permute(current, axis_name, count, _offset(j, group)) for j in range(1, 2 ** len(group))]
        if step == len(groups) - 1:
            return parts, companions
        current = jnp.concatenate(parts, axis=axis)


def _reduce_scatter(keep, give, axis_name, shape):
    count = lax.axis_size(axis_name)
    groups = _bit_groups(count)
    flat = sum(groups, [])

    def offset_of(position):
        return sum(1 << flat[k] for k in range(len(flat)) if (position >> k) & 1)

    chunks = 2 * keep.shape[0] // shape[0]
    current = keep + _permute(give, axis_name, count, offset_of(chunks // 2))
    chunks //= 2
    for group in groups[::-1][1:]:
        size = 2 ** len(group)
        block = chunks // size
        rows = block * shape[0]
        total = current[:rows]
        for t in range(1, size):
            part = current[t * rows:(t + 1) * rows]
            total = total + _permute(part, axis_name, count, offset_of(t * block))
        current = total
        chunks = block
    return current.reshape(shape)


def _position_offsets(count):
    if count <= 4:
        return list(range(count))
    flat = sum(_bit_groups(count), [])
    return [sum(1 << flat[k] for k in range(len(flat)) if (p >> k) & 1) for p in range(count)]


def _exchange(x, axis_name):
    count = lax.axis_size(axis_name)
    if count > 4:
        parts, _ = _all_gather(x[None], axis_name, 0)
        return list(jnp.concatenate(parts, axis=0)[1:])
    return [lax.ppermute(x, axis_name, [(i, i ^ p) for i in range(count)]) for p in range(1, count)]


def shards(
    panels,
    panel_slot,
    panel_cell,
    bloch_k,
    leaf_inverse,
    level_left,
    level_right,
    block_left,
    block_right,
    block_coupling,
    rank_count,
    quad_weight,
):
    local_angles = leaf_inverse.shape[0]
    assert local_angles == 1
    row_count = leaf_inverse.shape[2]
    panel_count = panels.shape[1]
    local_sources = panels.shape[2]
    panel_width = panels.shape[4]
    slot_count = row_count // panel_width
    source_count = local_sources * lax.axis_size("ang")
    rank_width = block_right.shape[2]
    levels = level_right.shape[1]

    cell_float = panel_cell[0].astype(jnp.float32)
    own_wave = lax.dynamic_slice_in_dim(bloch_k, lax.axis_index("ang") * local_angles, local_angles, 0)
    theta = own_wave[0, 0] * cell_float[:, 0] + own_wave[0, 1] * cell_float[:, 1]
    own_cos = lax.reduce_precision(jnp.cos(theta), exponent_bits=8, mantissa_bits=7)
    own_sin = lax.reduce_precision(jnp.sin(theta), exponent_bits=8, mantissa_bits=7)

    local_panels = panels[0].reshape(panel_count, local_sources, 2 * panel_width)
    row_blocks = lax.axis_size("row")
    me = lax.axis_index("row")
    coupling = block_coupling[0, 0]
    coupling = coupling.reshape(2, rank_width, row_blocks, coupling.shape[2] // row_blocks)
    offsets = jnp.array(_position_offsets(row_blocks), jnp.int32)
    coupling = jnp.take(coupling, me ^ offsets, axis=2).reshape(block_coupling.shape[2:])
    (first, second), (own_cos, own_sin, coupling) = _all_gather(local_panels, "ang", 1, (own_cos, own_sin, coupling))
    rank = rank_count[0].reshape(1)

    excitation, projected = pl.pallas_call(
        _excite_kernel,
        out_shape=(
            jax.ShapeDtypeStruct((2, source_count, row_count), jnp.bfloat16),
            jax.ShapeDtypeStruct((2, source_count, rank_width), jnp.bfloat16),
        ),
        in_specs=[_SMEM, _SMEM, _SMEM, _SMEM, _VMEM, _VMEM, _VMEM],
        out_specs=(_VMEM, _VMEM),
        scratch_shapes=[
            pltpu.VMEM((slot_count, source_count, panel_width), jnp.float32),
            pltpu.VMEM((slot_count, source_count, panel_width), jnp.float32),
        ],
    )(panel_slot[0], own_cos, own_sin, rank, first, second, block_right[0])
    all_projected = _exchange(projected, "row")

    near = pl.pallas_call(
        _near_kernel,
        out_shape=jax.ShapeDtypeStruct((source_count, 2 * row_count), jnp.float32),
        in_specs=[_VMEM] * 4,
        out_specs=_VMEM,
        scratch_shapes=[pltpu.VMEM((2 ** (levels + 1) - 2, 2, source_count, rank_width), jnp.bfloat16)],
    )(excitation, leaf_inverse[0], level_right[0], level_left[0])

    half = source_count // 2
    halves = []
    for h in (1, 0):
        halves.append(pl.pallas_call(
            _far_kernel,
            out_shape=jax.ShapeDtypeStruct((half, 2 * row_count), jnp.float32),
            grid=(1,),
            in_specs=[
                _SMEM,
                _SMEM,
                pl.BlockSpec((half, 2 * row_count), lambda i, h=h: (h, 0)),
                pl.BlockSpec(block_left.shape[1:], lambda i: (0, 0, 0)),
                pl.BlockSpec(coupling.shape, lambda i: (0, 0, 0)),
            ] + [pl.BlockSpec((2, half, rank_width), lambda i, h=h: (0, h, 0))] * (row_blocks - 1),
            out_specs=pl.BlockSpec((half, 2 * row_count), lambda i: (0, 0)),
            scratch_shapes=[pltpu.VMEM((2, half, rank_width), jnp.bfloat16)],
        )(quad_weight[0], rank, near, block_left[0], coupling, *all_projected))
    return _reduce_scatter(halves[1], halves[0], "ang", (local_sources, 2, row_count))


def solution(mesh):
    placed = (
        P("row", None, "ang", None, None),
        P("row", None),
        P("row", None, None),
        P(),
        P("ang", None, "row", None),
        P("ang", None, None, None, "row"),
        P("ang", None, None, None, "row"),
        P("ang", None, None, "row"),
        P("ang", None, None, "row"),
        P("ang", "row", None, None, None),
        P("ang", "row"),
        P("ang", None),
    )
    return jax.shard_map(
        shards, mesh=mesh, in_specs=placed, out_specs=P("ang", None, "row"), check_vma=False
    )
```

```python
import jax
import jax.numpy as jnp
from jax import lax
from jax.experimental import pallas as pl
from jax.experimental.pallas import tpu as pltpu
from jax.sharding import PartitionSpec as P

LEAF = 256

_SMEM = pl.BlockSpec(memory_space=pltpu.MemorySpace.SMEM)
_VMEM = pl.BlockSpec(memory_space=pltpu.MemorySpace.VMEM)


def _nt(a, b):
    return lax.dot_general(a, b, (((1,), (1,)), ((), ())), preferred_element_type=jnp.float32)


def _nn(a, b):
    return lax.dot_general(a, b, (((1,), (0,)), ((), ())), preferred_element_type=jnp.float32)


def _rank_mask(rank_ref, shape):
    return lax.broadcasted_iota(jnp.int32, shape, 0) < rank_ref[0]


def _excite_kernel(slot_ref, cos_ref, sin_ref, rank_ref, ga_ref, gb_ref, br_ref, e_ref, bp_ref, acc_re, acc_im):
    panel_count, part, width2 = ga_ref.shape
    width = width2 // 2
    slots = acc_re.shape[0]
    acc_re[...] = jnp.zeros(acc_re.shape, jnp.float32)
    acc_im[...] = jnp.zeros(acc_im.shape, jnp.float32)

    def body(q, carry):
        k = slot_ref[q]
        c = cos_ref[q]
        s = sin_ref[q]
        for rows, g_ref in ((slice(0, part), ga_ref), (slice(part, 2 * part), gb_ref)):
            p_re = g_ref[q, :, :width].astype(jnp.float32)
            p_im = g_ref[q, :, width:].astype(jnp.float32)
            acc_re[k, rows] = acc_re[k, rows] + (c * p_re + s * p_im)
            acc_im[k, rows] = acc_im[k, rows] + (c * p_im - s * p_re)
        return carry

    lax.fori_loop(0, panel_count, body, 0)
    for k in range(slots):
        e_ref[0, :, k * width:(k + 1) * width] = acc_re[k].astype(jnp.bfloat16)
        e_ref[1, :, k * width:(k + 1) * width] = acc_im[k].astype(jnp.bfloat16)
    e_re = e_ref[0]
    e_im = e_ref[1]
    keep = _rank_mask(rank_ref, br_ref.shape[1:])
    zero = jnp.zeros(br_ref.shape[1:], jnp.bfloat16)
    r_re = jnp.where(keep, br_ref[0], zero)
    r_im = jnp.where(keep, br_ref[1], zero)
    bp_ref[0] = (_nt(e_re, r_re) - _nt(e_im, r_im)).astype(jnp.bfloat16)
    bp_ref[1] = (_nt(e_re, r_im) + _nt(e_im, r_re)).astype(jnp.bfloat16)


def _near_kernel(e_ref, leaf_ref, lr_ref, ll_ref, out_re, out_im, pj_ref):
    _, source_count, row_count = e_ref.shape
    levels = lr_ref.shape[0]
    width = leaf_ref.shape[1]
    l = pl.program_id(0)

    group_starts = []
    slot = 0
    for j in range(levels):
        group_starts.append(slot)
        slot += 2 ** (j + 1)

    @pl.when(l == 0)
    def _():
        e_re = e_ref[0]
        e_im = e_ref[1]
        for j in range(levels):
            node = row_count // 2 ** (j + 1)
            for g in range(2 ** (j + 1)):
                cols = slice(g * node, (g + 1) * node)
                a = e_re[:, cols]
                b = e_im[:, cols]
                r_re = lr_ref[j, 0, :, cols]
                r_im = lr_ref[j, 1, :, cols]
                pj_ref[group_starts[j] + g, 0] = (_nt(a, r_re) - _nt(b, r_im)).astype(jnp.bfloat16)
                pj_ref[group_starts[j] + g, 1] = (_nt(a, r_im) + _nt(b, r_re)).astype(jnp.bfloat16)

    start = pl.multiple_of(l * width, width)
    a = e_ref[0, :, pl.ds(start, width)]
    b = e_ref[1, :, pl.ds(start, width)]
    lf_re = leaf_ref[0]
    lf_im = leaf_ref[1]
    f_re = _nt(a, lf_re) - _nt(b, lf_im)
    f_im = _nt(a, lf_im) + _nt(b, lf_re)
    for j in range(levels):
        node = row_count // 2 ** (j + 1)
        sibling = group_starts[j] + ((l * width) // node ^ 1)
        p_re = pj_ref[sibling, 0]
        p_im = pj_ref[sibling, 1]
        m_re = ll_ref[j, 0]
        m_im = ll_ref[j, 1]
        f_re = f_re + (_nn(p_re, m_re) - _nn(p_im, m_im))
        f_im = f_im + (_nn(p_re, m_im) + _nn(p_im, m_re))
    out_re[...] = f_re
    out_im[...] = f_im


def _far_kernel(qw_ref, rank_ref, near_re, near_im, bl_ref, cp_ref, *refs):
    part_refs = refs[:-2]
    out_ref, cu_ref = refs[-2:]
    source_count = near_re.shape[0]
    row_count = bl_ref.shape[2]
    rank_width = bl_ref.shape[1]
    blocks = len(part_refs) + 1
    coupling_rank = part_refs[0].shape[2]

    c_re = jnp.zeros((source_count, rank_width), jnp.float32)
    c_im = jnp.zeros((source_count, rank_width), jnp.float32)
    for u in range(1, blocks):
        b_re = part_refs[u - 1][0]
        b_im = part_refs[u - 1][1]
        k_re = cp_ref[0, :, u * coupling_rank:(u + 1) * coupling_rank]
        k_im = cp_ref[1, :, u * coupling_rank:(u + 1) * coupling_rank]
        c_re = c_re + (_nt(b_re, k_re) - _nt(b_im, k_im))
        c_im = c_im + (_nt(b_re, k_im) + _nt(b_im, k_re))
    cu_ref[0] = c_re.astype(jnp.bfloat16)
    cu_ref[1] = c_im.astype(jnp.bfloat16)
    coupled_re = cu_ref[0]
    coupled_im = cu_ref[1]

    w_re = qw_ref[0]
    w_im = qw_ref[1]
    for l in range(row_count // LEAF):
        cols = slice(l * LEAF, (l + 1) * LEAF)
        imag_cols = slice(row_count + l * LEAF, row_count + (l + 1) * LEAF)
        keep = _rank_mask(rank_ref, (rank_width, LEAF))
        zero = jnp.zeros((rank_width, LEAF), jnp.bfloat16)
        q_re = jnp.where(keep, bl_ref[0, :, cols], zero)
        q_im = jnp.where(keep, bl_ref[1, :, cols], zero)
        f_re = near_re[:, cols] + (_nn(coupled_re, q_re) - _nn(coupled_im, q_im))
        f_im = near_im[:, cols] + (_nn(coupled_re, q_im) + _nn(coupled_im, q_re))
        out_ref[:, cols] = w_re * f_re - w_im * f_im
        out_ref[:, imag_cols] = w_re * f_im + w_im * f_re


def _bit_groups(count):
    bits = count.bit_length() - 1
    groups = [[b, b - 1] for b in range(bits - 1, 1, -2)]
    rest = [b for b in range(bits) if all(b not in g for g in groups)]
    return groups + [[b] for b in rest[::-1]]


def _offset(value, group):
    return sum(1 << b for k, b in enumerate(group) if (value >> k) & 1)


def _permute(x, axis_name, count, offset):
    return lax.ppermute(x, axis_name, [(i, i ^ offset) for i in range(count)])


def _all_gather(x, axis_name, axis, companions=()):
    count = lax.axis_size(axis_name)
    groups = _bit_groups(count)
    current = x
    for step, group in enumerate(groups):
        if step == 1 and companions:
            current, companions = lax.optimization_barrier((current, companions))
        parts = [current] + [_permute(current, axis_name, count, _offset(j, group)) for j in range(1, 2 ** len(group))]
        if step == len(groups) - 1:
            return parts, companions
        current = jnp.concatenate(parts, axis=axis)


def _reduce_scatter(keep, give, axis_name, shape):
    count = lax.axis_size(axis_name)
    groups = _bit_groups(count)
    flat = sum(groups, [])

    def offset_of(position):
        return sum(1 << flat[k] for k in range(len(flat)) if (position >> k) & 1)

    chunks = 2 * keep.shape[0] // shape[0]
    current = keep + _permute(give, axis_name, count, offset_of(chunks // 2))
    chunks //= 2
    for group in groups[::-1][1:]:
        size = 2 ** len(group)
        block = chunks // size
        rows = block * shape[0]
        total = current[:rows]
        for t in range(1, size):
            part = current[t * rows:(t + 1) * rows]
            total = total + _permute(part, axis_name, count, offset_of(t * block))
        current = total
        chunks = block
    return current.reshape(shape)


def _position_offsets(count):
    if count <= 4:
        return list(range(count))
    flat = sum(_bit_groups(count), [])
    return [sum(1 << flat[k] for k in range(len(flat)) if (p >> k) & 1) for p in range(count)]


def _exchange(x, axis_name):
    count = lax.axis_size(axis_name)
    if count > 4:
        parts, _ = _all_gather(x[None], axis_name, 0)
        return list(jnp.concatenate(parts, axis=0)[1:])
    return [lax.ppermute(x, axis_name, [(i, i ^ p) for i in range(count)]) for p in range(1, count)]


def shards(
    panels,
    panel_slot,
    panel_cell,
    bloch_k,
    leaf_inverse,
    level_left,
    level_right,
    block_left,
    block_right,
    block_coupling,
    rank_count,
    quad_weight,
):
    local_angles = leaf_inverse.shape[0]
    assert local_angles == 1
    row_count = leaf_inverse.shape[2]
    panel_count = panels.shape[1]
    local_sources = panels.shape[2]
    panel_width = panels.shape[4]
    slot_count = row_count // panel_width
    source_count = local_sources * lax.axis_size("ang")
    rank_width = block_right.shape[2]
    levels = level_right.shape[1]

    cell_float = panel_cell[0].astype(jnp.float32)
    own_wave = lax.dynamic_slice_in_dim(bloch_k, lax.axis_index("ang") * local_angles, local_angles, 0)
    theta = own_wave[0, 0] * cell_float[:, 0] + own_wave[0, 1] * cell_float[:, 1]
    own_cos = lax.reduce_precision(jnp.cos(theta), exponent_bits=8, mantissa_bits=7)
    own_sin = lax.reduce_precision(jnp.sin(theta), exponent_bits=8, mantissa_bits=7)

    local_panels = panels[0].reshape(panel_count, local_sources, 2 * panel_width)
    row_blocks = lax.axis_size("row")
    me = lax.axis_index("row")
    coupling = block_coupling[0, 0]
    coupling = coupling.reshape(2, rank_width, row_blocks, coupling.shape[2] // row_blocks)
    offsets = jnp.array(_position_offsets(row_blocks), jnp.int32)
    coupling = jnp.take(coupling, me ^ offsets, axis=2).reshape(block_coupling.shape[2:])
    (first, second), (own_cos, own_sin, coupling) = _all_gather(local_panels, "ang", 1, (own_cos, own_sin, coupling))
    rank = rank_count[0].reshape(1)

    excitation, projected = pl.pallas_call(
        _excite_kernel,
        out_shape=(
            jax.ShapeDtypeStruct((2, source_count, row_count), jnp.bfloat16),
            jax.ShapeDtypeStruct((2, source_count, rank_width), jnp.bfloat16),
        ),
        in_specs=[_SMEM, _SMEM, _SMEM, _SMEM, _VMEM, _VMEM, _VMEM],
        out_specs=(_VMEM, _VMEM),
        scratch_shapes=[
            pltpu.VMEM((slot_count, source_count, panel_width), jnp.float32),
            pltpu.VMEM((slot_count, source_count, panel_width), jnp.float32),
        ],
    )(panel_slot[0], own_cos, own_sin, rank, first, second, block_right[0])
    all_projected = _exchange(projected, "row")

    leaf_width = leaf_inverse.shape[3]
    near_re, near_im = pl.pallas_call(
        _near_kernel,
        out_shape=(
            jax.ShapeDtypeStruct((source_count, row_count), jnp.float32),
            jax.ShapeDtypeStruct((source_count, row_count), jnp.float32),
        ),
        grid=(row_count // leaf_width,),
        in_specs=[
            pl.BlockSpec((2, source_count, row_count), lambda l: (0, 0, 0)),
            pl.BlockSpec((2, leaf_width, leaf_width), lambda l: (0, l, 0)),
            pl.BlockSpec(level_right.shape[1:], lambda l: (0, 0, 0, 0)),
            pl.BlockSpec((levels, 2, rank_width, leaf_width), lambda l: (0, 0, 0, l)),
        ],
        out_specs=(
            pl.BlockSpec((source_count, leaf_width), lambda l: (0, l)),
            pl.BlockSpec((source_count, leaf_width), lambda l: (0, l)),
        ),
        scratch_shapes=[pltpu.VMEM((2 ** (levels + 1) - 2, 2, source_count, rank_width), jnp.bfloat16)],
    )(excitation, leaf_inverse[0], level_right[0], level_left[0])

    half = source_count // 2
    halves = []
    for h in (1, 0):
        halves.append(pl.pallas_call(
            _far_kernel,
            out_shape=jax.ShapeDtypeStruct((half, 2 * row_count), jnp.float32),
            grid=(1,),
            in_specs=[
                _SMEM,
                _SMEM,
                pl.BlockSpec((half, row_count), lambda i, h=h: (h, 0)),
                pl.BlockSpec((half, row_count), lambda i, h=h: (h, 0)),
                pl.BlockSpec(block_left.shape[1:], lambda i: (0, 0, 0)),
                pl.BlockSpec(coupling.shape, lambda i: (0, 0, 0)),
            ] + [pl.BlockSpec((2, half, rank_width), lambda i, h=h: (0, h, 0))] * (row_blocks - 1),
            out_specs=pl.BlockSpec((half, 2 * row_count), lambda i: (0, 0)),
            scratch_shapes=[pltpu.VMEM((2, half, rank_width), jnp.bfloat16)],
        )(quad_weight[0], rank, near_re, near_im, block_left[0], coupling, *all_projected))
    return _reduce_scatter(halves[1], halves[0], "ang", (local_sources, 2, row_count))


def solution(mesh):
    placed = (
        P("row", None, "ang", None, None),
        P("row", None),
        P("row", None, None),
        P(),
        P("ang", None, "row", None),
        P("ang", None, None, None, "row"),
        P("ang", None, None, None, "row"),
        P("ang", None, None, "row"),
        P("ang", None, None, "row"),
        P("ang", "row", None, None, None),
        P("ang", "row"),
        P("ang", None),
    )
    return jax.shard_map(
        shards, mesh=mesh, in_specs=placed, out_specs=P("ang", None, "row"), check_vma=False
    )
```

```python
import jax
import jax.numpy as jnp
from jax import lax
from jax.experimental import pallas as pl
from jax.experimental.pallas import tpu as pltpu
from jax.sharding import PartitionSpec as P

LEAF = 256

_SMEM = pl.BlockSpec(memory_space=pltpu.MemorySpace.SMEM)
_VMEM = pl.BlockSpec(memory_space=pltpu.MemorySpace.VMEM)


def _nt(a, b):
    return lax.dot_general(a, b, (((1,), (1,)), ((), ())), preferred_element_type=jnp.float32)


def _nn(a, b):
    return lax.dot_general(a, b, (((1,), (0,)), ((), ())), preferred_element_type=jnp.float32)


def _rank_mask(rank_ref, shape):
    return lax.broadcasted_iota(jnp.int32, shape, 0) < rank_ref[0]


def _excite_kernel(slot_ref, cos_ref, sin_ref, rank_ref, ga_ref, gb_ref, br_ref, e_ref, bp_ref, acc_re, acc_im):
    panel_count, part, width2 = ga_ref.shape
    width = width2 // 2
    slots = acc_re.shape[0]
    acc_re[...] = jnp.zeros(acc_re.shape, jnp.float32)
    acc_im[...] = jnp.zeros(acc_im.shape, jnp.float32)

    def body(q, carry):
        k = slot_ref[q]
        c = cos_ref[q]
        s = sin_ref[q]
        for rows, g_ref in ((slice(0, part), ga_ref), (slice(part, 2 * part), gb_ref)):
            p_re = g_ref[q, :, :width].astype(jnp.float32)
            p_im = g_ref[q, :, width:].astype(jnp.float32)
            acc_re[k, rows] = acc_re[k, rows] + (c * p_re + s * p_im)
            acc_im[k, rows] = acc_im[k, rows] + (c * p_im - s * p_re)
        return carry

    lax.fori_loop(0, panel_count, body, 0)
    for k in range(slots):
        e_ref[0, :, k * width:(k + 1) * width] = acc_re[k].astype(jnp.bfloat16)
        e_ref[1, :, k * width:(k + 1) * width] = acc_im[k].astype(jnp.bfloat16)
    sources = e_ref.shape[1]
    stacked = e_ref[...].reshape(2 * sources, e_ref.shape[2])
    keep = _rank_mask(rank_ref, br_ref.shape[1:])
    zero = jnp.zeros(br_ref.shape[1:], jnp.bfloat16)
    t_re = _nt(stacked, jnp.where(keep, br_ref[0], zero))
    t_im = _nt(stacked, jnp.where(keep, br_ref[1], zero))
    bp_ref[0] = (t_re[:sources] - t_im[sources:]).astype(jnp.bfloat16)
    bp_ref[1] = (t_im[:sources] + t_re[sources:]).astype(jnp.bfloat16)


def _near_kernel(e_ref, leaf_ref, lr_ref, ll_ref, out_ref, pj_ref):
    _, source_count, row_count = e_ref.shape
    levels = lr_ref.shape[0]
    sc = source_count
    stacked = e_ref[...].reshape(2 * sc, row_count)

    first_group = []
    slot = 0
    for j in range(levels):
        node = row_count // 2 ** (j + 1)
        first_group.append(slot)
        for g in range(2 ** (j + 1)):
            cols = slice(g * node, (g + 1) * node)
            ab = stacked[:, cols]
            t_re = _nt(ab, lr_ref[j, 0, :, cols])
            t_im = _nt(ab, lr_ref[j, 1, :, cols])
            pj_ref[slot, 0] = (t_re[:sc] - t_im[sc:]).astype(jnp.bfloat16)
            pj_ref[slot, 1] = (t_im[:sc] + t_re[sc:]).astype(jnp.bfloat16)
            slot += 1

    for l in range(row_count // LEAF):
        cols = slice(l * LEAF, (l + 1) * LEAF)
        ab = stacked[:, cols]
        t_re = _nt(ab, leaf_ref[0, cols, :])
        t_im = _nt(ab, leaf_ref[1, cols, :])
        f_re = t_re[:sc] - t_im[sc:]
        f_im = t_im[:sc] + t_re[sc:]
        for j in range(levels):
            node = row_count // 2 ** (j + 1)
            g = (l * LEAF) // node
            pp = pj_ref[first_group[j] + (g ^ 1)].reshape(2 * sc, pj_ref.shape[3])
            v_re = _nn(pp, ll_ref[j, 0, :, cols])
            v_im = _nn(pp, ll_ref[j, 1, :, cols])
            f_re = f_re + (v_re[:sc] - v_im[sc:])
            f_im = f_im + (v_im[:sc] + v_re[sc:])
        out_ref[:, cols] = f_re
        out_ref[:, row_count + l * LEAF:row_count + (l + 1) * LEAF] = f_im


def _far_kernel(qw_ref, rank_ref, near_ref, bl_ref, cp_ref, *refs):
    part_refs = refs[:-2]
    out_ref, cu_ref = refs[-2:]
    source_count = near_ref.shape[0]
    row_count = bl_ref.shape[2]
    rank_width = bl_ref.shape[1]
    blocks = len(part_refs) + 1
    coupling_rank = part_refs[0].shape[2]

    c_re = jnp.zeros((source_count, rank_width), jnp.float32)
    c_im = jnp.zeros((source_count, rank_width), jnp.float32)
    sc = source_count
    for u in range(1, blocks):
        bb = part_refs[u - 1][...].reshape(2 * sc, coupling_rank)
        t_re = _nt(bb, cp_ref[0, :, u * coupling_rank:(u + 1) * coupling_rank])
        t_im = _nt(bb, cp_ref[1, :, u * coupling_rank:(u + 1) * coupling_rank])
        c_re = c_re + (t_re[:sc] - t_im[sc:])
        c_im = c_im + (t_im[:sc] + t_re[sc:])
    cu_ref[0] = c_re.astype(jnp.bfloat16)
    cu_ref[1] = c_im.astype(jnp.bfloat16)
    coupled = cu_ref[...].reshape(2 * sc, rank_width)

    w_re = qw_ref[0]
    w_im = qw_ref[1]
    for l in range(row_count // LEAF):
        cols = slice(l * LEAF, (l + 1) * LEAF)
        imag_cols = slice(row_count + l * LEAF, row_count + (l + 1) * LEAF)
        keep = _rank_mask(rank_ref, (rank_width, LEAF))
        zero = jnp.zeros((rank_width, LEAF), jnp.bfloat16)
        q_re = jnp.where(keep, bl_ref[0, :, cols], zero)
        q_im = jnp.where(keep, bl_ref[1, :, cols], zero)
        v_re = _nn(coupled, q_re)
        v_im = _nn(coupled, q_im)
        f_re = near_ref[:, cols] + (v_re[:sc] - v_im[sc:])
        f_im = near_ref[:, imag_cols] + (v_im[:sc] + v_re[sc:])
        out_ref[:, cols] = w_re * f_re - w_im * f_im
        out_ref[:, imag_cols] = w_re * f_im + w_im * f_re


def _bit_groups(count):
    bits = count.bit_length() - 1
    groups = [[b, b - 1] for b in range(bits - 1, 1, -2)]
    rest = [b for b in range(bits) if all(b not in g for g in groups)]
    return groups + [[b] for b in rest[::-1]]


def _offset(value, group):
    return sum(1 << b for k, b in enumerate(group) if (value >> k) & 1)


def _permute(x, axis_name, count, offset):
    return lax.ppermute(x, axis_name, [(i, i ^ offset) for i in range(count)])


def _all_gather(x, axis_name, axis, companions=()):
    count = lax.axis_size(axis_name)
    groups = _bit_groups(count)
    current = x
    for step, group in enumerate(groups):
        if step == 1 and companions:
            current, companions = lax.optimization_barrier((current, companions))
        parts = [current] + [_permute(current, axis_name, count, _offset(j, group)) for j in range(1, 2 ** len(group))]
        if step == len(groups) - 1:
            return parts, companions
        current = jnp.concatenate(parts, axis=axis)


def _reduce_scatter(keep, give, axis_name, shape):
    count = lax.axis_size(axis_name)
    groups = _bit_groups(count)
    flat = sum(groups, [])

    def offset_of(position):
        return sum(1 << flat[k] for k in range(len(flat)) if (position >> k) & 1)

    chunks = 2 * keep.shape[0] // shape[0]
    current = keep + _permute(give, axis_name, count, offset_of(chunks // 2))
    chunks //= 2
    for group in groups[::-1][1:]:
        size = 2 ** len(group)
        block = chunks // size
        rows = block * shape[0]
        total = current[:rows]
        for t in range(1, size):
            part = current[t * rows:(t + 1) * rows]
            total = total + _permute(part, axis_name, count, offset_of(t * block))
        current = total
        chunks = block
    return current.reshape(shape)


def _position_offsets(count):
    if count <= 4:
        return list(range(count))
    flat = sum(_bit_groups(count), [])
    return [sum(1 << flat[k] for k in range(len(flat)) if (p >> k) & 1) for p in range(count)]


def _exchange(x, axis_name):
    count = lax.axis_size(axis_name)
    if count > 4:
        parts, _ = _all_gather(x[None], axis_name, 0)
        return list(jnp.concatenate(parts, axis=0)[1:])
    return [lax.ppermute(x, axis_name, [(i, i ^ p) for i in range(count)]) for p in range(1, count)]


def shards(
    panels,
    panel_slot,
    panel_cell,
    bloch_k,
    leaf_inverse,
    level_left,
    level_right,
    block_left,
    block_right,
    block_coupling,
    rank_count,
    quad_weight,
):
    local_angles = leaf_inverse.shape[0]
    assert local_angles == 1
    row_count = leaf_inverse.shape[2]
    panel_count = panels.shape[1]
    local_sources = panels.shape[2]
    panel_width = panels.shape[4]
    slot_count = row_count // panel_width
    source_count = local_sources * lax.axis_size("ang")
    rank_width = block_right.shape[2]
    levels = level_right.shape[1]

    cell_float = panel_cell[0].astype(jnp.float32)
    own_wave = lax.dynamic_slice_in_dim(bloch_k, lax.axis_index("ang") * local_angles, local_angles, 0)
    theta = own_wave[0, 0] * cell_float[:, 0] + own_wave[0, 1] * cell_float[:, 1]
    own_cos = lax.reduce_precision(jnp.cos(theta), exponent_bits=8, mantissa_bits=7)
    own_sin = lax.reduce_precision(jnp.sin(theta), exponent_bits=8, mantissa_bits=7)

    local_panels = panels[0].reshape(panel_count, local_sources, 2 * panel_width)
    row_blocks = lax.axis_size("row")
    me = lax.axis_index("row")
    coupling = block_coupling[0, 0]
    coupling = coupling.reshape(2, rank_width, row_blocks, coupling.shape[2] // row_blocks)
    offsets = jnp.array(_position_offsets(row_blocks), jnp.int32)
    coupling = jnp.take(coupling, me ^ offsets, axis=2).reshape(block_coupling.shape[2:])
    (first, second), (own_cos, own_sin, coupling) = _all_gather(local_panels, "ang", 1, (own_cos, own_sin, coupling))
    rank = rank_count[0].reshape(1)

    excitation, projected = pl.pallas_call(
        _excite_kernel,
        out_shape=(
            jax.ShapeDtypeStruct((2, source_count, row_count), jnp.bfloat16),
            jax.ShapeDtypeStruct((2, source_count, rank_width), jnp.bfloat16),
        ),
        in_specs=[_SMEM, _SMEM, _SMEM, _SMEM, _VMEM, _VMEM, _VMEM],
        out_specs=(_VMEM, _VMEM),
        scratch_shapes=[
            pltpu.VMEM((slot_count, source_count, panel_width), jnp.float32),
            pltpu.VMEM((slot_count, source_count, panel_width), jnp.float32),
        ],
    )(panel_slot[0], own_cos, own_sin, rank, first, second, block_right[0])
    all_projected = _exchange(projected, "row")

    near = pl.pallas_call(
        _near_kernel,
        out_shape=jax.ShapeDtypeStruct((source_count, 2 * row_count), jnp.float32),
        in_specs=[_VMEM] * 4,
        out_specs=_VMEM,
        scratch_shapes=[pltpu.VMEM((2 ** (levels + 1) - 2, 2, source_count, rank_width), jnp.bfloat16)],
    )(excitation, leaf_inverse[0], level_right[0], level_left[0])

    half = source_count // 2
    halves = []
    for h in (1, 0):
        halves.append(pl.pallas_call(
            _far_kernel,
            out_shape=jax.ShapeDtypeStruct((half, 2 * row_count), jnp.float32),
            grid=(1,),
            in_specs=[
                _SMEM,
                _SMEM,
                pl.BlockSpec((half, 2 * row_count), lambda i, h=h: (h, 0)),
                pl.BlockSpec(block_left.shape[1:], lambda i: (0, 0, 0)),
                pl.BlockSpec(coupling.shape, lambda i: (0, 0, 0)),
            ] + [pl.BlockSpec((2, half, rank_width), lambda i, h=h: (0, h, 0))] * (row_blocks - 1),
            out_specs=pl.BlockSpec((half, 2 * row_count), lambda i: (0, 0)),
            scratch_shapes=[pltpu.VMEM((2, half, rank_width), jnp.bfloat16)],
        )(quad_weight[0], rank, near, block_left[0], coupling, *all_projected))
    return _reduce_scatter(halves[1], halves[0], "ang", (local_sources, 2, row_count))


def solution(mesh):
    placed = (
        P("row", None, "ang", None, None),
        P("row", None),
        P("row", None, None),
        P(),
        P("ang", None, "row", None),
        P("ang", None, None, None, "row"),
        P("ang", None, None, None, "row"),
        P("ang", None, None, "row"),
        P("ang", None, None, "row"),
        P("ang", "row", None, None, None),
        P("ang", "row"),
        P("ang", None),
    )
    return jax.shard_map(
        shards, mesh=mesh, in_specs=placed, out_specs=P("ang", None, "row"), check_vma=False
    )
```

```python
import jax
import jax.numpy as jnp
from jax import lax
from jax.experimental import pallas as pl
from jax.experimental.pallas import tpu as pltpu
from jax.sharding import PartitionSpec as P

LEAF = 256

_SMEM = pl.BlockSpec(memory_space=pltpu.MemorySpace.SMEM)
_VMEM = pl.BlockSpec(memory_space=pltpu.MemorySpace.VMEM)


def _nt(a, b):
    return lax.dot_general(a, b, (((1,), (1,)), ((), ())), preferred_element_type=jnp.float32)


def _nn(a, b):
    return lax.dot_general(a, b, (((1,), (0,)), ((), ())), preferred_element_type=jnp.float32)


def _rank_mask(rank_ref, shape):
    return lax.broadcasted_iota(jnp.int32, shape, 0) < rank_ref[0]


def _accumulate(slot_ref, cos_ref, sin_ref, g_ref, acc_re, acc_im):
    panel_count, _, width2 = g_ref.shape
    width = width2 // 2
    acc_re[...] = jnp.zeros(acc_re.shape, jnp.float32)
    acc_im[...] = jnp.zeros(acc_im.shape, jnp.float32)

    def body(q, carry):
        k = slot_ref[q]
        c = cos_ref[q]
        s = sin_ref[q]
        p_re = g_ref[q, :, :width].astype(jnp.float32)
        p_im = g_ref[q, :, width:].astype(jnp.float32)
        acc_re[k] = acc_re[k] + (c * p_re + s * p_im)
        acc_im[k] = acc_im[k] + (c * p_im - s * p_re)
        return carry

    lax.fori_loop(0, panel_count, body, 0)


def _store_excitation(acc_re, acc_im, e_ref):
    width = acc_re.shape[2]
    for k in range(acc_re.shape[0]):
        e_ref[0, :, k * width:(k + 1) * width] = acc_re[k].astype(jnp.bfloat16)
        e_ref[1, :, k * width:(k + 1) * width] = acc_im[k].astype(jnp.bfloat16)


def _excite_first_kernel(slot_ref, cos_ref, sin_ref, g_ref, e_ref, acc_re, acc_im):
    _accumulate(slot_ref, cos_ref, sin_ref, g_ref, acc_re, acc_im)
    _store_excitation(acc_re, acc_im, e_ref)


def _excite_second_kernel(slot_ref, cos_ref, sin_ref, rank_ref, g_ref, br_ref, e_in, e_ref, bp_ref, acc_re, acc_im):
    _accumulate(slot_ref, cos_ref, sin_ref, g_ref, acc_re, acc_im)
    _store_excitation(acc_re, acc_im, e_ref)
    part = e_ref.shape[1]
    keep = _rank_mask(rank_ref, br_ref.shape[1:])
    zero = jnp.zeros(br_ref.shape[1:], jnp.bfloat16)
    r_re = jnp.where(keep, br_ref[0], zero)
    r_im = jnp.where(keep, br_ref[1], zero)
    for rows, values in ((slice(0, part), e_in[:, :part, :]), (slice(part, 2 * part), e_ref[...])):
        stacked = values.reshape(2 * part, values.shape[2])
        t_re = _nt(stacked, r_re)
        t_im = _nt(stacked, r_im)
        bp_ref[0, rows, :] = (t_re[:part] - t_im[part:]).astype(jnp.bfloat16)
        bp_ref[1, rows, :] = (t_im[:part] + t_re[part:]).astype(jnp.bfloat16)


def _near_kernel(e_ref, leaf_ref, lr_ref, ll_ref, out_ref, pj_ref):
    _, source_count, row_count = e_ref.shape
    levels = lr_ref.shape[0]
    sc = source_count
    stacked = e_ref[...].reshape(2 * sc, row_count)

    first_group = []
    slot = 0
    for j in range(levels):
        node = row_count // 2 ** (j + 1)
        first_group.append(slot)
        for g in range(2 ** (j + 1)):
            cols = slice(g * node, (g + 1) * node)
            ab = stacked[:, cols]
            t_re = _nt(ab, lr_ref[j, 0, :, cols])
            t_im = _nt(ab, lr_ref[j, 1, :, cols])
            pj_ref[slot, 0] = (t_re[:sc] - t_im[sc:]).astype(jnp.bfloat16)
            pj_ref[slot, 1] = (t_im[:sc] + t_re[sc:]).astype(jnp.bfloat16)
            slot += 1

    for l in range(row_count // LEAF):
        cols = slice(l * LEAF, (l + 1) * LEAF)
        ab = stacked[:, cols]
        t_re = _nt(ab, leaf_ref[0, cols, :])
        t_im = _nt(ab, leaf_ref[1, cols, :])
        f_re = t_re[:sc] - t_im[sc:]
        f_im = t_im[:sc] + t_re[sc:]
        for j in range(levels):
            node = row_count // 2 ** (j + 1)
            g = (l * LEAF) // node
            pp = pj_ref[first_group[j] + (g ^ 1)].reshape(2 * sc, pj_ref.shape[3])
            v_re = _nn(pp, ll_ref[j, 0, :, cols])
            v_im = _nn(pp, ll_ref[j, 1, :, cols])
            f_re = f_re + (v_re[:sc] - v_im[sc:])
            f_im = f_im + (v_im[:sc] + v_re[sc:])
        out_ref[:, cols] = f_re
        out_ref[:, row_count + l * LEAF:row_count + (l + 1) * LEAF] = f_im


def _far_kernel(qw_ref, rank_ref, near_ref, bl_ref, cp_ref, *refs):
    part_refs = refs[:-2]
    out_ref, cu_ref = refs[-2:]
    source_count = near_ref.shape[0]
    row_count = bl_ref.shape[2]
    rank_width = bl_ref.shape[1]
    blocks = len(part_refs) + 1
    coupling_rank = part_refs[0].shape[2]

    c_re = jnp.zeros((source_count, rank_width), jnp.float32)
    c_im = jnp.zeros((source_count, rank_width), jnp.float32)
    sc = source_count
    for u in range(1, blocks):
        bb = part_refs[u - 1][...].reshape(2 * sc, coupling_rank)
        t_re = _nt(bb, cp_ref[0, :, u * coupling_rank:(u + 1) * coupling_rank])
        t_im = _nt(bb, cp_ref[1, :, u * coupling_rank:(u + 1) * coupling_rank])
        c_re = c_re + (t_re[:sc] - t_im[sc:])
        c_im = c_im + (t_im[:sc] + t_re[sc:])
    cu_ref[0] = c_re.astype(jnp.bfloat16)
    cu_ref[1] = c_im.astype(jnp.bfloat16)
    coupled = cu_ref[...].reshape(2 * sc, rank_width)

    w_re = qw_ref[0]
    w_im = qw_ref[1]
    for l in range(row_count // LEAF):
        cols = slice(l * LEAF, (l + 1) * LEAF)
        imag_cols = slice(row_count + l * LEAF, row_count + (l + 1) * LEAF)
        keep = _rank_mask(rank_ref, (rank_width, LEAF))
        zero = jnp.zeros((rank_width, LEAF), jnp.bfloat16)
        q_re = jnp.where(keep, bl_ref[0, :, cols], zero)
        q_im = jnp.where(keep, bl_ref[1, :, cols], zero)
        v_re = _nn(coupled, q_re)
        v_im = _nn(coupled, q_im)
        f_re = near_ref[:, cols] + (v_re[:sc] - v_im[sc:])
        f_im = near_ref[:, imag_cols] + (v_im[:sc] + v_re[sc:])
        out_ref[:, cols] = w_re * f_re - w_im * f_im
        out_ref[:, imag_cols] = w_re * f_im + w_im * f_re


def _bit_groups(count):
    bits = count.bit_length() - 1
    groups = [[b, b - 1] for b in range(bits - 1, 1, -2)]
    rest = [b for b in range(bits) if all(b not in g for g in groups)]
    return groups + [[b] for b in rest[::-1]]


def _offset(value, group):
    return sum(1 << b for k, b in enumerate(group) if (value >> k) & 1)


def _permute(x, axis_name, count, offset):
    return lax.ppermute(x, axis_name, [(i, i ^ offset) for i in range(count)])


def _all_gather(x, axis_name, axis, companions=()):
    count = lax.axis_size(axis_name)
    groups = _bit_groups(count)
    current = x
    for step, group in enumerate(groups):
        if step == 1 and companions:
            current, companions = lax.optimization_barrier((current, companions))
        parts = [current] + [_permute(current, axis_name, count, _offset(j, group)) for j in range(1, 2 ** len(group))]
        if step == len(groups) - 1:
            return parts, companions
        current = jnp.concatenate(parts, axis=axis)


def _reduce_scatter(keep, give, axis_name, shape):
    count = lax.axis_size(axis_name)
    groups = _bit_groups(count)
    flat = sum(groups, [])

    def offset_of(position):
        return sum(1 << flat[k] for k in range(len(flat)) if (position >> k) & 1)

    chunks = 2 * keep.shape[0] // shape[0]
    current = keep + _permute(give, axis_name, count, offset_of(chunks // 2))
    chunks //= 2
    for group in groups[::-1][1:]:
        size = 2 ** len(group)
        block = chunks // size
        rows = block * shape[0]
        total = current[:rows]
        for t in range(1, size):
            part = current[t * rows:(t + 1) * rows]
            total = total + _permute(part, axis_name, count, offset_of(t * block))
        current = total
        chunks = block
    return current.reshape(shape)


def _position_offsets(count):
    if count <= 4:
        return list(range(count))
    flat = sum(_bit_groups(count), [])
    return [sum(1 << flat[k] for k in range(len(flat)) if (p >> k) & 1) for p in range(count)]


def _exchange(x, axis_name):
    count = lax.axis_size(axis_name)
    if count > 4:
        parts, _ = _all_gather(x[None], axis_name, 0)
        return list(jnp.concatenate(parts, axis=0)[1:])
    return [lax.ppermute(x, axis_name, [(i, i ^ p) for i in range(count)]) for p in range(1, count)]


def shards(
    panels,
    panel_slot,
    panel_cell,
    bloch_k,
    leaf_inverse,
    level_left,
    level_right,
    block_left,
    block_right,
    block_coupling,
    rank_count,
    quad_weight,
):
    local_angles = leaf_inverse.shape[0]
    assert local_angles == 1
    row_count = leaf_inverse.shape[2]
    panel_count = panels.shape[1]
    local_sources = panels.shape[2]
    panel_width = panels.shape[4]
    slot_count = row_count // panel_width
    source_count = local_sources * lax.axis_size("ang")
    rank_width = block_right.shape[2]
    levels = level_right.shape[1]

    cell_float = panel_cell[0].astype(jnp.float32)
    own_wave = lax.dynamic_slice_in_dim(bloch_k, lax.axis_index("ang") * local_angles, local_angles, 0)
    theta = own_wave[0, 0] * cell_float[:, 0] + own_wave[0, 1] * cell_float[:, 1]
    own_cos = lax.reduce_precision(jnp.cos(theta), exponent_bits=8, mantissa_bits=7)
    own_sin = lax.reduce_precision(jnp.sin(theta), exponent_bits=8, mantissa_bits=7)

    local_panels = panels[0].reshape(panel_count, local_sources, 2 * panel_width)
    row_blocks = lax.axis_size("row")
    me = lax.axis_index("row")
    coupling = block_coupling[0, 0]
    coupling = coupling.reshape(2, rank_width, row_blocks, coupling.shape[2] // row_blocks)
    offsets = jnp.array(_position_offsets(row_blocks), jnp.int32)
    coupling = jnp.take(coupling, me ^ offsets, axis=2).reshape(block_coupling.shape[2:])
    (first, second), (own_cos, own_sin, coupling) = _all_gather(local_panels, "ang", 1, (own_cos, own_sin, coupling))
    rank = rank_count[0].reshape(1)

    part = source_count // 2
    acc = [pltpu.VMEM((slot_count, part, panel_width), jnp.float32)] * 2
    whole_e = jax.ShapeDtypeStruct((2, source_count, row_count), jnp.bfloat16)
    first_e = pl.pallas_call(
        _excite_first_kernel,
        out_shape=whole_e,
        grid=(1,),
        in_specs=[_SMEM, _SMEM, _SMEM, pl.BlockSpec(first.shape, lambda i: (0, 0, 0))],
        out_specs=pl.BlockSpec((2, part, row_count), lambda i: (0, 0, 0)),
        scratch_shapes=acc,
    )(panel_slot[0], own_cos, own_sin, first)
    excitation, projected = pl.pallas_call(
        _excite_second_kernel,
        out_shape=(whole_e, jax.ShapeDtypeStruct((2, source_count, rank_width), jnp.bfloat16)),
        grid=(1,),
        in_specs=[
            _SMEM,
            _SMEM,
            _SMEM,
            _SMEM,
            pl.BlockSpec(second.shape, lambda i: (0, 0, 0)),
            pl.BlockSpec(block_right.shape[1:], lambda i: (0, 0, 0)),
            pl.BlockSpec((2, source_count, row_count), lambda i: (0, 0, 0)),
        ],
        out_specs=(
            pl.BlockSpec((2, part, row_count), lambda i: (0, 1, 0)),
            pl.BlockSpec((2, source_count, rank_width), lambda i: (0, 0, 0)),
        ),
        scratch_shapes=acc,
        input_output_aliases={6: 0},
    )(panel_slot[0], own_cos, own_sin, rank, second, block_right[0], first_e)
    all_projected = _exchange(projected, "row")

    near = pl.pallas_call(
        _near_kernel,
        out_shape=jax.ShapeDtypeStruct((source_count, 2 * row_count), jnp.float32),
        in_specs=[_VMEM] * 4,
        out_specs=_VMEM,
        scratch_shapes=[pltpu.VMEM((2 ** (levels + 1) - 2, 2, source_count, rank_width), jnp.bfloat16)],
    )(excitation, leaf_inverse[0], level_right[0], level_left[0])

    half = source_count // 2
    halves = []
    for h in (1, 0):
        halves.append(pl.pallas_call(
            _far_kernel,
            out_shape=jax.ShapeDtypeStruct((half, 2 * row_count), jnp.float32),
            grid=(1,),
            in_specs=[
                _SMEM,
                _SMEM,
                pl.BlockSpec((half, 2 * row_count), lambda i, h=h: (h, 0)),
                pl.BlockSpec(block_left.shape[1:], lambda i: (0, 0, 0)),
                pl.BlockSpec(coupling.shape, lambda i: (0, 0, 0)),
            ] + [pl.BlockSpec((2, half, rank_width), lambda i, h=h: (0, h, 0))] * (row_blocks - 1),
            out_specs=pl.BlockSpec((half, 2 * row_count), lambda i: (0, 0)),
            scratch_shapes=[pltpu.VMEM((2, half, rank_width), jnp.bfloat16)],
        )(quad_weight[0], rank, near, block_left[0], coupling, *all_projected))
    return _reduce_scatter(halves[1], halves[0], "ang", (local_sources, 2, row_count))


def solution(mesh):
    placed = (
        P("row", None, "ang", None, None),
        P("row", None),
        P("row", None, None),
        P(),
        P("ang", None, "row", None),
        P("ang", None, None, None, "row"),
        P("ang", None, None, None, "row"),
        P("ang", None, None, "row"),
        P("ang", None, None, "row"),
        P("ang", "row", None, None, None),
        P("ang", "row"),
        P("ang", None),
    )
    return jax.shard_map(
        shards, mesh=mesh, in_specs=placed, out_specs=P("ang", None, "row"), check_vma=False
    )
```

```python
import jax
import jax.numpy as jnp
from jax import lax
from jax.experimental import pallas as pl
from jax.experimental.pallas import tpu as pltpu
from jax.sharding import PartitionSpec as P

LEAF = 256

_SMEM = pl.BlockSpec(memory_space=pltpu.MemorySpace.SMEM)
_VMEM = pl.BlockSpec(memory_space=pltpu.MemorySpace.VMEM)


def _nt(a, b):
    return lax.dot_general(a, b, (((1,), (1,)), ((), ())), preferred_element_type=jnp.float32)


def _nn(a, b):
    return lax.dot_general(a, b, (((1,), (0,)), ((), ())), preferred_element_type=jnp.float32)


def _rank_mask(rank_ref, shape):
    return lax.broadcasted_iota(jnp.int32, shape, 0) < rank_ref[0]


def _excite_kernel(slot_ref, cos_ref, sin_ref, rank_ref, ga_ref, gb_ref, br_ref, e_ref, bp_ref, acc_re, acc_im):
    panel_count, part, width2 = ga_ref.shape
    width = width2 // 2
    slots = acc_re.shape[0]
    acc_re[...] = jnp.zeros(acc_re.shape, jnp.float32)
    acc_im[...] = jnp.zeros(acc_im.shape, jnp.float32)

    def body(q, carry):
        k = slot_ref[q]
        c = cos_ref[q]
        s = sin_ref[q]
        for rows, g_ref in ((slice(0, part), ga_ref), (slice(part, 2 * part), gb_ref)):
            p_re = g_ref[q, :, :width].astype(jnp.float32)
            p_im = g_ref[q, :, width:].astype(jnp.float32)
            acc_re[k, rows] = acc_re[k, rows] + (c * p_re + s * p_im)
            acc_im[k, rows] = acc_im[k, rows] + (c * p_im - s * p_re)
        return carry

    lax.fori_loop(0, panel_count, body, 0)
    for k in range(slots):
        e_ref[0, :, k * width:(k + 1) * width] = acc_re[k].astype(jnp.bfloat16)
        e_ref[1, :, k * width:(k + 1) * width] = acc_im[k].astype(jnp.bfloat16)
    sources = e_ref.shape[1]
    stacked = e_ref[...].reshape(2 * sources, e_ref.shape[2])
    keep = _rank_mask(rank_ref, br_ref.shape[1:])
    zero = jnp.zeros(br_ref.shape[1:], jnp.bfloat16)
    t_re = _nt(stacked, jnp.where(keep, br_ref[0], zero))
    t_im = _nt(stacked, jnp.where(keep, br_ref[1], zero))
    bp_ref[0] = (t_re[:sources] - t_im[sources:]).astype(jnp.bfloat16)
    bp_ref[1] = (t_im[:sources] + t_re[sources:]).astype(jnp.bfloat16)


def _near_kernel(e_ref, leaf_ref, lr_ref, ll_ref, out_ref, pj_ref):
    _, source_count, row_count = e_ref.shape
    levels = lr_ref.shape[0]
    sc = source_count

    def stacked(cols, width):
        return e_ref[:, :, cols].reshape(2 * sc, width)

    first_group = []
    slot = 0
    for j in range(levels):
        node = row_count // 2 ** (j + 1)
        first_group.append(slot)
        for g in range(2 ** (j + 1)):
            cols = slice(g * node, (g + 1) * node)
            ab = stacked(cols, node)
            t_re = _nt(ab, lr_ref[j, 0, :, cols])
            t_im = _nt(ab, lr_ref[j, 1, :, cols])
            pj_ref[slot, 0] = (t_re[:sc] - t_im[sc:]).astype(jnp.bfloat16)
            pj_ref[slot, 1] = (t_im[:sc] + t_re[sc:]).astype(jnp.bfloat16)
            slot += 1

    for l in range(row_count // LEAF):
        cols = slice(l * LEAF, (l + 1) * LEAF)
        ab = stacked(cols, LEAF)
        t_re = _nt(ab, leaf_ref[0, cols, :])
        t_im = _nt(ab, leaf_ref[1, cols, :])
        f_re = t_re[:sc] - t_im[sc:]
        f_im = t_im[:sc] + t_re[sc:]
        for j in range(levels):
            node = row_count // 2 ** (j + 1)
            g = (l * LEAF) // node
            pp = pj_ref[first_group[j] + (g ^ 1)].reshape(2 * sc, pj_ref.shape[3])
            v_re = _nn(pp, ll_ref[j, 0, :, cols])
            v_im = _nn(pp, ll_ref[j, 1, :, cols])
            f_re = f_re + (v_re[:sc] - v_im[sc:])
            f_im = f_im + (v_im[:sc] + v_re[sc:])
        out_ref[:, cols] = f_re
        out_ref[:, row_count + l * LEAF:row_count + (l + 1) * LEAF] = f_im


def _far_kernel(qw_ref, rank_ref, near_ref, bl_ref, cp_ref, *refs):
    part_refs = refs[:-2]
    out_ref, cu_ref = refs[-2:]
    source_count = near_ref.shape[0]
    row_count = bl_ref.shape[2]
    rank_width = bl_ref.shape[1]
    blocks = len(part_refs) + 1
    coupling_rank = part_refs[0].shape[2]

    c_re = jnp.zeros((source_count, rank_width), jnp.float32)
    c_im = jnp.zeros((source_count, rank_width), jnp.float32)
    sc = source_count
    for u in range(1, blocks):
        bb = part_refs[u - 1][...].reshape(2 * sc, coupling_rank)
        t_re = _nt(bb, cp_ref[0, :, u * coupling_rank:(u + 1) * coupling_rank])
        t_im = _nt(bb, cp_ref[1, :, u * coupling_rank:(u + 1) * coupling_rank])
        c_re = c_re + (t_re[:sc] - t_im[sc:])
        c_im = c_im + (t_im[:sc] + t_re[sc:])
    cu_ref[0] = c_re.astype(jnp.bfloat16)
    cu_ref[1] = c_im.astype(jnp.bfloat16)
    coupled = cu_ref[...].reshape(2 * sc, rank_width)

    w_re = qw_ref[0]
    w_im = qw_ref[1]
    for l in range(row_count // LEAF):
        cols = slice(l * LEAF, (l + 1) * LEAF)
        imag_cols = slice(row_count + l * LEAF, row_count + (l + 1) * LEAF)
        keep = _rank_mask(rank_ref, (rank_width, LEAF))
        zero = jnp.zeros((rank_width, LEAF), jnp.bfloat16)
        q_re = jnp.where(keep, bl_ref[0, :, cols], zero)
        q_im = jnp.where(keep, bl_ref[1, :, cols], zero)
        v_re = _nn(coupled, q_re)
        v_im = _nn(coupled, q_im)
        f_re = near_ref[:, cols] + (v_re[:sc] - v_im[sc:])
        f_im = near_ref[:, imag_cols] + (v_im[:sc] + v_re[sc:])
        out_ref[:, cols] = w_re * f_re - w_im * f_im
        out_ref[:, imag_cols] = w_re * f_im + w_im * f_re


def _bit_groups(count):
    bits = count.bit_length() - 1
    groups = [[b, b - 1] for b in range(bits - 1, 1, -2)]
    rest = [b for b in range(bits) if all(b not in g for g in groups)]
    return groups + [[b] for b in rest[::-1]]


def _offset(value, group):
    return sum(1 << b for k, b in enumerate(group) if (value >> k) & 1)


def _permute(x, axis_name, count, offset):
    return lax.ppermute(x, axis_name, [(i, i ^ offset) for i in range(count)])


def _all_gather(x, axis_name, axis, companions=()):
    count = lax.axis_size(axis_name)
    groups = _bit_groups(count)
    current = x
    for step, group in enumerate(groups):
        if step == 1 and companions:
            current, companions = lax.optimization_barrier((current, companions))
        parts = [current] + [_permute(current, axis_name, count, _offset(j, group)) for j in range(1, 2 ** len(group))]
        if step == len(groups) - 1:
            return parts, companions
        current = jnp.concatenate(parts, axis=axis)


def _reduce_scatter(keep, give, axis_name, shape):
    count = lax.axis_size(axis_name)
    groups = _bit_groups(count)
    flat = sum(groups, [])

    def offset_of(position):
        return sum(1 << flat[k] for k in range(len(flat)) if (position >> k) & 1)

    chunks = 2 * keep.shape[0] // shape[0]
    current = keep + _permute(give, axis_name, count, offset_of(chunks // 2))
    chunks //= 2
    for group in groups[::-1][1:]:
        size = 2 ** len(group)
        block = chunks // size
        rows = block * shape[0]
        total = current[:rows]
        for t in range(1, size):
            part = current[t * rows:(t + 1) * rows]
            total = total + _permute(part, axis_name, count, offset_of(t * block))
        current = total
        chunks = block
    return current.reshape(shape)


def _position_offsets(count):
    if count <= 4:
        return list(range(count))
    flat = sum(_bit_groups(count), [])
    return [sum(1 << flat[k] for k in range(len(flat)) if (p >> k) & 1) for p in range(count)]


def _exchange(x, axis_name):
    count = lax.axis_size(axis_name)
    if count > 4:
        parts, _ = _all_gather(x[None], axis_name, 0)
        return list(jnp.concatenate(parts, axis=0)[1:])
    return [lax.ppermute(x, axis_name, [(i, i ^ p) for i in range(count)]) for p in range(1, count)]


def shards(
    panels,
    panel_slot,
    panel_cell,
    bloch_k,
    leaf_inverse,
    level_left,
    level_right,
    block_left,
    block_right,
    block_coupling,
    rank_count,
    quad_weight,
):
    local_angles = leaf_inverse.shape[0]
    assert local_angles == 1
    row_count = leaf_inverse.shape[2]
    panel_count = panels.shape[1]
    local_sources = panels.shape[2]
    panel_width = panels.shape[4]
    slot_count = row_count // panel_width
    source_count = local_sources * lax.axis_size("ang")
    rank_width = block_right.shape[2]
    levels = level_right.shape[1]

    cell_float = panel_cell[0].astype(jnp.float32)
    own_wave = lax.dynamic_slice_in_dim(bloch_k, lax.axis_index("ang") * local_angles, local_angles, 0)
    theta = own_wave[0, 0] * cell_float[:, 0] + own_wave[0, 1] * cell_float[:, 1]
    own_cos = lax.reduce_precision(jnp.cos(theta), exponent_bits=8, mantissa_bits=7)
    own_sin = lax.reduce_precision(jnp.sin(theta), exponent_bits=8, mantissa_bits=7)

    local_panels = panels[0].reshape(panel_count, local_sources, 2 * panel_width)
    row_blocks = lax.axis_size("row")
    me = lax.axis_index("row")
    coupling = block_coupling[0, 0]
    coupling = coupling.reshape(2, rank_width, row_blocks, coupling.shape[2] // row_blocks)
    offsets = jnp.array(_position_offsets(row_blocks), jnp.int32)
    coupling = jnp.take(coupling, me ^ offsets, axis=2).reshape(block_coupling.shape[2:])
    (first, second), (own_cos, own_sin, coupling) = _all_gather(local_panels, "ang", 1, (own_cos, own_sin, coupling))
    rank = rank_count[0].reshape(1)

    excitation, projected = pl.pallas_call(
        _excite_kernel,
        out_shape=(
            jax.ShapeDtypeStruct((2, source_count, row_count), jnp.bfloat16),
            jax.ShapeDtypeStruct((2, source_count, rank_width), jnp.bfloat16),
        ),
        in_specs=[_SMEM, _SMEM, _SMEM, _SMEM, _VMEM, _VMEM, _VMEM],
        out_specs=(_VMEM, _VMEM),
        scratch_shapes=[
            pltpu.VMEM((slot_count, source_count, panel_width), jnp.float32),
            pltpu.VMEM((slot_count, source_count, panel_width), jnp.float32),
        ],
    )(panel_slot[0], own_cos, own_sin, rank, first, second, block_right[0])
    all_projected = _exchange(projected, "row")

    near = pl.pallas_call(
        _near_kernel,
        out_shape=jax.ShapeDtypeStruct((source_count, 2 * row_count), jnp.float32),
        in_specs=[_VMEM] * 4,
        out_specs=_VMEM,
        scratch_shapes=[pltpu.VMEM((2 ** (levels + 1) - 2, 2, source_count, rank_width), jnp.bfloat16)],
    )(excitation, leaf_inverse[0], level_right[0], level_left[0])

    half = source_count // 2
    halves = []
    for h in (1, 0):
        halves.append(pl.pallas_call(
            _far_kernel,
            out_shape=jax.ShapeDtypeStruct((half, 2 * row_count), jnp.float32),
            grid=(1,),
            in_specs=[
                _SMEM,
                _SMEM,
                pl.BlockSpec((half, 2 * row_count), lambda i, h=h: (h, 0)),
                pl.BlockSpec(block_left.shape[1:], lambda i: (0, 0, 0)),
                pl.BlockSpec(coupling.shape, lambda i: (0, 0, 0)),
            ] + [pl.BlockSpec((2, half, rank_width), lambda i, h=h: (0, h, 0))] * (row_blocks - 1),
            out_specs=pl.BlockSpec((half, 2 * row_count), lambda i: (0, 0)),
            scratch_shapes=[pltpu.VMEM((2, half, rank_width), jnp.bfloat16)],
        )(quad_weight[0], rank, near, block_left[0], coupling, *all_projected))
    return _reduce_scatter(halves[1], halves[0], "ang", (local_sources, 2, row_count))


def solution(mesh):
    placed = (
        P("row", None, "ang", None, None),
        P("row", None),
        P("row", None, None),
        P(),
        P("ang", None, "row", None),
        P("ang", None, None, None, "row"),
        P("ang", None, None, None, "row"),
        P("ang", None, None, "row"),
        P("ang", None, None, "row"),
        P("ang", "row", None, None, None),
        P("ang", "row"),
        P("ang", None),
    )
    return jax.shard_map(
        shards, mesh=mesh, in_specs=placed, out_specs=P("ang", None, "row"), check_vma=False
    )
```

```python
import jax
import jax.numpy as jnp
from jax import lax
from jax.experimental import pallas as pl
from jax.experimental.pallas import tpu as pltpu
from jax.sharding import PartitionSpec as P

LEAF = 256

_SMEM = pl.BlockSpec(memory_space=pltpu.MemorySpace.SMEM)
_VMEM = pl.BlockSpec(memory_space=pltpu.MemorySpace.VMEM)


def _nt(a, b):
    return lax.dot_general(a, b, (((1,), (1,)), ((), ())), preferred_element_type=jnp.float32)


def _nn(a, b):
    return lax.dot_general(a, b, (((1,), (0,)), ((), ())), preferred_element_type=jnp.float32)


def _rank_mask(rank_ref, shape):
    return lax.broadcasted_iota(jnp.int32, shape, 0) < rank_ref[0]


def _excite_kernel(slot_ref, cos_ref, sin_ref, rank_ref, ga_ref, gb_ref, br_ref, e_ref, bp_ref, acc_re, acc_im):
    panel_count, part, width2 = ga_ref.shape
    width = width2 // 2
    slots = acc_re.shape[0]
    acc_re[...] = jnp.zeros(acc_re.shape, jnp.float32)
    acc_im[...] = jnp.zeros(acc_im.shape, jnp.float32)

    def body(q, carry):
        k = slot_ref[q]
        c = cos_ref[q]
        s = sin_ref[q]
        for rows, g_ref in ((slice(0, part), ga_ref), (slice(part, 2 * part), gb_ref)):
            p_re = g_ref[q, :, :width].astype(jnp.float32)
            p_im = g_ref[q, :, width:].astype(jnp.float32)
            acc_re[k, rows] = acc_re[k, rows] + (c * p_re + s * p_im)
            acc_im[k, rows] = acc_im[k, rows] + (c * p_im - s * p_re)
        return carry

    lax.fori_loop(0, panel_count, body, 0, unroll=8)
    for k in range(slots):
        e_ref[0, :, k * width:(k + 1) * width] = acc_re[k].astype(jnp.bfloat16)
        e_ref[1, :, k * width:(k + 1) * width] = acc_im[k].astype(jnp.bfloat16)
    sources = e_ref.shape[1]
    stacked = e_ref[...].reshape(2 * sources, e_ref.shape[2])
    keep = _rank_mask(rank_ref, br_ref.shape[1:])
    zero = jnp.zeros(br_ref.shape[1:], jnp.bfloat16)
    t_re = _nt(stacked, jnp.where(keep, br_ref[0], zero))
    t_im = _nt(stacked, jnp.where(keep, br_ref[1], zero))
    bp_ref[0] = (t_re[:sources] - t_im[sources:]).astype(jnp.bfloat16)
    bp_ref[1] = (t_im[:sources] + t_re[sources:]).astype(jnp.bfloat16)


def _near_kernel(e_ref, leaf_ref, lr_ref, ll_ref, out_ref, pj_ref):
    _, source_count, row_count = e_ref.shape
    levels = lr_ref.shape[0]
    sc = source_count
    stacked = e_ref[...].reshape(2 * sc, row_count)

    first_group = []
    slot = 0
    for j in range(levels):
        node = row_count // 2 ** (j + 1)
        first_group.append(slot)
        for g in range(2 ** (j + 1)):
            cols = slice(g * node, (g + 1) * node)
            ab = stacked[:, cols]
            t_re = _nt(ab, lr_ref[j, 0, :, cols])
            t_im = _nt(ab, lr_ref[j, 1, :, cols])
            pj_ref[slot, 0] = (t_re[:sc] - t_im[sc:]).astype(jnp.bfloat16)
            pj_ref[slot, 1] = (t_im[:sc] + t_re[sc:]).astype(jnp.bfloat16)
            slot += 1

    for l in range(row_count // LEAF):
        cols = slice(l * LEAF, (l + 1) * LEAF)
        ab = stacked[:, cols]
        t_re = _nt(ab, leaf_ref[0, cols, :])
        t_im = _nt(ab, leaf_ref[1, cols, :])
        f_re = t_re[:sc] - t_im[sc:]
        f_im = t_im[:sc] + t_re[sc:]
        for j in range(levels):
            node = row_count // 2 ** (j + 1)
            g = (l * LEAF) // node
            pp = pj_ref[first_group[j] + (g ^ 1)].reshape(2 * sc, pj_ref.shape[3])
            v_re = _nn(pp, ll_ref[j, 0, :, cols])
            v_im = _nn(pp, ll_ref[j, 1, :, cols])
            f_re = f_re + (v_re[:sc] - v_im[sc:])
            f_im = f_im + (v_im[:sc] + v_re[sc:])
        out_ref[:, cols] = f_re
        out_ref[:, row_count + l * LEAF:row_count + (l + 1) * LEAF] = f_im


def _far_kernel(qw_ref, rank_ref, near_ref, bl_ref, cp_ref, *refs):
    part_refs = refs[:-2]
    out_ref, cu_ref = refs[-2:]
    source_count = near_ref.shape[0]
    row_count = bl_ref.shape[2]
    rank_width = bl_ref.shape[1]
    blocks = len(part_refs) + 1
    coupling_rank = part_refs[0].shape[2]

    c_re = jnp.zeros((source_count, rank_width), jnp.float32)
    c_im = jnp.zeros((source_count, rank_width), jnp.float32)
    sc = source_count
    for u in range(1, blocks):
        bb = part_refs[u - 1][...].reshape(2 * sc, coupling_rank)
        t_re = _nt(bb, cp_ref[0, :, u * coupling_rank:(u + 1) * coupling_rank])
        t_im = _nt(bb, cp_ref[1, :, u * coupling_rank:(u + 1) * coupling_rank])
        c_re = c_re + (t_re[:sc] - t_im[sc:])
        c_im = c_im + (t_im[:sc] + t_re[sc:])
    cu_ref[0] = c_re.astype(jnp.bfloat16)
    cu_ref[1] = c_im.astype(jnp.bfloat16)
    coupled = cu_ref[...].reshape(2 * sc, rank_width)

    w_re = qw_ref[0]
    w_im = qw_ref[1]
    for l in range(row_count // LEAF):
        cols = slice(l * LEAF, (l + 1) * LEAF)
        imag_cols = slice(row_count + l * LEAF, row_count + (l + 1) * LEAF)
        keep = _rank_mask(rank_ref, (rank_width, LEAF))
        zero = jnp.zeros((rank_width, LEAF), jnp.bfloat16)
        q_re = jnp.where(keep, bl_ref[0, :, cols], zero)
        q_im = jnp.where(keep, bl_ref[1, :, cols], zero)
        v_re = _nn(coupled, q_re)
        v_im = _nn(coupled, q_im)
        f_re = near_ref[:, cols] + (v_re[:sc] - v_im[sc:])
        f_im = near_ref[:, imag_cols] + (v_im[:sc] + v_re[sc:])
        out_ref[:, cols] = w_re * f_re - w_im * f_im
        out_ref[:, imag_cols] = w_re * f_im + w_im * f_re


def _bit_groups(count):
    bits = count.bit_length() - 1
    groups = [[b, b - 1] for b in range(bits - 1, 1, -2)]
    rest = [b for b in range(bits) if all(b not in g for g in groups)]
    return groups + [[b] for b in rest[::-1]]


def _offset(value, group):
    return sum(1 << b for k, b in enumerate(group) if (value >> k) & 1)


def _permute(x, axis_name, count, offset):
    return lax.ppermute(x, axis_name, [(i, i ^ offset) for i in range(count)])


def _all_gather(x, axis_name, axis, companions=()):
    count = lax.axis_size(axis_name)
    groups = _bit_groups(count)
    current = x
    for step, group in enumerate(groups):
        if step == 1 and companions:
            current, companions = lax.optimization_barrier((current, companions))
        parts = [current] + [_permute(current, axis_name, count, _offset(j, group)) for j in range(1, 2 ** len(group))]
        if step == len(groups) - 1:
            return parts, companions
        current = jnp.concatenate(parts, axis=axis)


def _reduce_scatter(keep, give, axis_name, shape):
    count = lax.axis_size(axis_name)
    groups = _bit_groups(count)
    flat = sum(groups, [])

    def offset_of(position):
        return sum(1 << flat[k] for k in range(len(flat)) if (position >> k) & 1)

    chunks = 2 * keep.shape[0] // shape[0]
    current = keep + _permute(give, axis_name, count, offset_of(chunks // 2))
    chunks //= 2
    for group in groups[::-1][1:]:
        size = 2 ** len(group)
        block = chunks // size
        rows = block * shape[0]
        total = current[:rows]
        for t in range(1, size):
            part = current[t * rows:(t + 1) * rows]
            total = total + _permute(part, axis_name, count, offset_of(t * block))
        current = total
        chunks = block
    return current.reshape(shape)


def _position_offsets(count):
    if count <= 4:
        return list(range(count))
    flat = sum(_bit_groups(count), [])
    return [sum(1 << flat[k] for k in range(len(flat)) if (p >> k) & 1) for p in range(count)]


def _exchange(x, axis_name):
    count = lax.axis_size(axis_name)
    if count > 4:
        parts, _ = _all_gather(x[None], axis_name, 0)
        return list(jnp.concatenate(parts, axis=0)[1:])
    return [lax.ppermute(x, axis_name, [(i, i ^ p) for i in range(count)]) for p in range(1, count)]


def shards(
    panels,
    panel_slot,
    panel_cell,
    bloch_k,
    leaf_inverse,
    level_left,
    level_right,
    block_left,
    block_right,
    block_coupling,
    rank_count,
    quad_weight,
):
    local_angles = leaf_inverse.shape[0]
    assert local_angles == 1
    row_count = leaf_inverse.shape[2]
    panel_count = panels.shape[1]
    local_sources = panels.shape[2]
    panel_width = panels.shape[4]
    slot_count = row_count // panel_width
    source_count = local_sources * lax.axis_size("ang")
    rank_width = block_right.shape[2]
    levels = level_right.shape[1]

    cell_float = panel_cell[0].astype(jnp.float32)
    own_wave = lax.dynamic_slice_in_dim(bloch_k, lax.axis_index("ang") * local_angles, local_angles, 0)
    theta = own_wave[0, 0] * cell_float[:, 0] + own_wave[0, 1] * cell_float[:, 1]
    own_cos = lax.reduce_precision(jnp.cos(theta), exponent_bits=8, mantissa_bits=7)
    own_sin = lax.reduce_precision(jnp.sin(theta), exponent_bits=8, mantissa_bits=7)

    local_panels = panels[0].reshape(panel_count, local_sources, 2 * panel_width)
    row_blocks = lax.axis_size("row")
    me = lax.axis_index("row")
    coupling = block_coupling[0, 0]
    coupling = coupling.reshape(2, rank_width, row_blocks, coupling.shape[2] // row_blocks)
    offsets = jnp.array(_position_offsets(row_blocks), jnp.int32)
    coupling = jnp.take(coupling, me ^ offsets, axis=2).reshape(block_coupling.shape[2:])
    (first, second), (own_cos, own_sin, coupling) = _all_gather(local_panels, "ang", 1, (own_cos, own_sin, coupling))
    rank = rank_count[0].reshape(1)

    excitation, projected = pl.pallas_call(
        _excite_kernel,
        out_shape=(
            jax.ShapeDtypeStruct((2, source_count, row_count), jnp.bfloat16),
            jax.ShapeDtypeStruct((2, source_count, rank_width), jnp.bfloat16),
        ),
        in_specs=[_SMEM, _SMEM, _SMEM, _SMEM, _VMEM, _VMEM, _VMEM],
        out_specs=(_VMEM, _VMEM),
        scratch_shapes=[
            pltpu.VMEM((slot_count, source_count, panel_width), jnp.float32),
            pltpu.VMEM((slot_count, source_count, panel_width), jnp.float32),
        ],
    )(panel_slot[0], own_cos, own_sin, rank, first, second, block_right[0])
    all_projected = _exchange(projected, "row")

    near = pl.pallas_call(
        _near_kernel,
        out_shape=jax.ShapeDtypeStruct((source_count, 2 * row_count), jnp.float32),
        in_specs=[_VMEM] * 4,
        out_specs=_VMEM,
        scratch_shapes=[pltpu.VMEM((2 ** (levels + 1) - 2, 2, source_count, rank_width), jnp.bfloat16)],
    )(excitation, leaf_inverse[0], level_right[0], level_left[0])

    half = source_count // 2
    halves = []
    for h in (1, 0):
        halves.append(pl.pallas_call(
            _far_kernel,
            out_shape=jax.ShapeDtypeStruct((half, 2 * row_count), jnp.float32),
            grid=(1,),
            in_specs=[
                _SMEM,
                _SMEM,
                pl.BlockSpec((half, 2 * row_count), lambda i, h=h: (h, 0)),
                pl.BlockSpec(block_left.shape[1:], lambda i: (0, 0, 0)),
                pl.BlockSpec(coupling.shape, lambda i: (0, 0, 0)),
            ] + [pl.BlockSpec((2, half, rank_width), lambda i, h=h: (0, h, 0))] * (row_blocks - 1),
            out_specs=pl.BlockSpec((half, 2 * row_count), lambda i: (0, 0)),
            scratch_shapes=[pltpu.VMEM((2, half, rank_width), jnp.bfloat16)],
        )(quad_weight[0], rank, near, block_left[0], coupling, *all_projected))
    return _reduce_scatter(halves[1], halves[0], "ang", (local_sources, 2, row_count))


def solution(mesh):
    placed = (
        P("row", None, "ang", None, None),
        P("row", None),
        P("row", None, None),
        P(),
        P("ang", None, "row", None),
        P("ang", None, None, None, "row"),
        P("ang", None, None, None, "row"),
        P("ang", None, None, "row"),
        P("ang", None, None, "row"),
        P("ang", "row", None, None, None),
        P("ang", "row"),
        P("ang", None),
    )
    return jax.shard_map(
        shards, mesh=mesh, in_specs=placed, out_specs=P("ang", None, "row"), check_vma=False
    )
```

```python
import jax
import jax.numpy as jnp
from jax import lax
from jax.experimental import pallas as pl
from jax.experimental.pallas import tpu as pltpu
from jax.sharding import PartitionSpec as P

LEAF = 256

_SMEM = pl.BlockSpec(memory_space=pltpu.MemorySpace.SMEM)
_VMEM = pl.BlockSpec(memory_space=pltpu.MemorySpace.VMEM)


def _nt(a, b):
    return lax.dot_general(a, b, (((1,), (1,)), ((), ())), preferred_element_type=jnp.float32)


def _nn(a, b):
    return lax.dot_general(a, b, (((1,), (0,)), ((), ())), preferred_element_type=jnp.float32)


def _rank_mask(rank_ref, shape):
    return lax.broadcasted_iota(jnp.int32, shape, 0) < rank_ref[0]


def _excite_kernel(slot_ref, cos_ref, sin_ref, rank_ref, ga_ref, gb_ref, br_ref, e_ref, bp_ref, acc_re, acc_im):
    panel_count, part, width2 = ga_ref.shape
    width = width2 // 2
    slots = acc_re.shape[0]
    acc_re[...] = jnp.zeros(acc_re.shape, jnp.float32)
    acc_im[...] = jnp.zeros(acc_im.shape, jnp.float32)

    def body(q, carry):
        k = slot_ref[q]
        c = cos_ref[q]
        s = sin_ref[q]
        for rows, g_ref in ((slice(0, part), ga_ref), (slice(part, 2 * part), gb_ref)):
            p_re = g_ref[q, :, :width].astype(jnp.float32)
            p_im = g_ref[q, :, width:].astype(jnp.float32)
            acc_re[k, rows] = acc_re[k, rows] + (c * p_re + s * p_im)
            acc_im[k, rows] = acc_im[k, rows] + (c * p_im - s * p_re)
        return carry

    lax.fori_loop(0, panel_count, body, 0, unroll=8)
    for k in range(slots):
        e_ref[0, :, k * width:(k + 1) * width] = acc_re[k].astype(jnp.bfloat16)
        e_ref[1, :, k * width:(k + 1) * width] = acc_im[k].astype(jnp.bfloat16)
    sources = e_ref.shape[1]
    stacked = e_ref[...].reshape(2 * sources, e_ref.shape[2])
    keep = _rank_mask(rank_ref, br_ref.shape[1:])
    zero = jnp.zeros(br_ref.shape[1:], jnp.bfloat16)
    t_re = _nt(stacked, jnp.where(keep, br_ref[0], zero))
    t_im = _nt(stacked, jnp.where(keep, br_ref[1], zero))
    bp_ref[0] = (t_re[:sources] - t_im[sources:]).astype(jnp.bfloat16)
    bp_ref[1] = (t_im[:sources] + t_re[sources:]).astype(jnp.bfloat16)


def _near_kernel(e_ref, leaf_ref, lr_ref, ll_ref, out_ref, pj_ref, pc_ref):
    _, source_count, row_count = e_ref.shape
    levels = lr_ref.shape[0]
    sc = source_count
    stacked = e_ref[...].reshape(2 * sc, row_count)

    first_group = []
    slot = 0
    for j in range(levels):
        node = row_count // 2 ** (j + 1)
        first_group.append(slot)
        for g in range(2 ** (j + 1)):
            cols = slice(g * node, (g + 1) * node)
            ab = stacked[:, cols]
            t_re = _nt(ab, lr_ref[j, 0, :, cols])
            t_im = _nt(ab, lr_ref[j, 1, :, cols])
            pj_ref[slot, 0] = (t_re[:sc] - t_im[sc:]).astype(jnp.bfloat16)
            pj_ref[slot, 1] = (t_im[:sc] + t_re[sc:]).astype(jnp.bfloat16)
            slot += 1

    for l in range(row_count // LEAF):
        cols = slice(l * LEAF, (l + 1) * LEAF)
        ab = stacked[:, cols]
        t_re = _nt(ab, leaf_ref[0, cols, :])
        t_im = _nt(ab, leaf_ref[1, cols, :])
        f_re = t_re[:sc] - t_im[sc:]
        f_im = t_im[:sc] + t_re[sc:]
        rank = pj_ref.shape[3]
        for j in range(levels):
            node = row_count // 2 ** (j + 1)
            g = (l * LEAF) // node
            pc_ref[:, j * rank:(j + 1) * rank] = pj_ref[first_group[j] + (g ^ 1)].reshape(2 * sc, rank)
        pp = pc_ref[...]
        v_re = _nn(pp, ll_ref[:, 0, :, cols].reshape(levels * rank, LEAF))
        v_im = _nn(pp, ll_ref[:, 1, :, cols].reshape(levels * rank, LEAF))
        f_re = f_re + (v_re[:sc] - v_im[sc:])
        f_im = f_im + (v_im[:sc] + v_re[sc:])
        out_ref[:, cols] = f_re
        out_ref[:, row_count + l * LEAF:row_count + (l + 1) * LEAF] = f_im


def _far_kernel(qw_ref, rank_ref, near_ref, bl_ref, cp_ref, *refs):
    part_refs = refs[:-2]
    out_ref, cu_ref = refs[-2:]
    source_count = near_ref.shape[0]
    row_count = bl_ref.shape[2]
    rank_width = bl_ref.shape[1]
    blocks = len(part_refs) + 1
    coupling_rank = part_refs[0].shape[2]

    c_re = jnp.zeros((source_count, rank_width), jnp.float32)
    c_im = jnp.zeros((source_count, rank_width), jnp.float32)
    sc = source_count
    for u in range(1, blocks):
        bb = part_refs[u - 1][...].reshape(2 * sc, coupling_rank)
        t_re = _nt(bb, cp_ref[0, :, u * coupling_rank:(u + 1) * coupling_rank])
        t_im = _nt(bb, cp_ref[1, :, u * coupling_rank:(u + 1) * coupling_rank])
        c_re = c_re + (t_re[:sc] - t_im[sc:])
        c_im = c_im + (t_im[:sc] + t_re[sc:])
    cu_ref[0] = c_re.astype(jnp.bfloat16)
    cu_ref[1] = c_im.astype(jnp.bfloat16)
    coupled = cu_ref[...].reshape(2 * sc, rank_width)

    w_re = qw_ref[0]
    w_im = qw_ref[1]
    for l in range(row_count // LEAF):
        cols = slice(l * LEAF, (l + 1) * LEAF)
        imag_cols = slice(row_count + l * LEAF, row_count + (l + 1) * LEAF)
        keep = _rank_mask(rank_ref, (rank_width, LEAF))
        zero = jnp.zeros((rank_width, LEAF), jnp.bfloat16)
        q_re = jnp.where(keep, bl_ref[0, :, cols], zero)
        q_im = jnp.where(keep, bl_ref[1, :, cols], zero)
        v_re = _nn(coupled, q_re)
        v_im = _nn(coupled, q_im)
        f_re = near_ref[:, cols] + (v_re[:sc] - v_im[sc:])
        f_im = near_ref[:, imag_cols] + (v_im[:sc] + v_re[sc:])
        out_ref[:, cols] = w_re * f_re - w_im * f_im
        out_ref[:, imag_cols] = w_re * f_im + w_im * f_re


def _bit_groups(count):
    bits = count.bit_length() - 1
    groups = [[b, b - 1] for b in range(bits - 1, 1, -2)]
    rest = [b for b in range(bits) if all(b not in g for g in groups)]
    return groups + [[b] for b in rest[::-1]]


def _offset(value, group):
    return sum(1 << b for k, b in enumerate(group) if (value >> k) & 1)


def _permute(x, axis_name, count, offset):
    return lax.ppermute(x, axis_name, [(i, i ^ offset) for i in range(count)])


def _all_gather(x, axis_name, axis, companions=()):
    count = lax.axis_size(axis_name)
    groups = _bit_groups(count)
    current = x
    for step, group in enumerate(groups):
        if step == 1 and companions:
            current, companions = lax.optimization_barrier((current, companions))
        parts = [current] + [_permute(current, axis_name, count, _offset(j, group)) for j in range(1, 2 ** len(group))]
        if step == len(groups) - 1:
            return parts, companions
        current = jnp.concatenate(parts, axis=axis)


def _reduce_scatter(keep, give, axis_name, shape):
    count = lax.axis_size(axis_name)
    groups = _bit_groups(count)
    flat = sum(groups, [])

    def offset_of(position):
        return sum(1 << flat[k] for k in range(len(flat)) if (position >> k) & 1)

    chunks = 2 * keep.shape[0] // shape[0]
    current = keep + _permute(give, axis_name, count, offset_of(chunks // 2))
    chunks //= 2
    for group in groups[::-1][1:]:
        size = 2 ** len(group)
        block = chunks // size
        rows = block * shape[0]
        total = current[:rows]
        for t in range(1, size):
            part = current[t * rows:(t + 1) * rows]
            total = total + _permute(part, axis_name, count, offset_of(t * block))
        current = total
        chunks = block
    return current.reshape(shape)


def _position_offsets(count):
    if count <= 4:
        return list(range(count))
    flat = sum(_bit_groups(count), [])
    return [sum(1 << flat[k] for k in range(len(flat)) if (p >> k) & 1) for p in range(count)]


def _exchange(x, axis_name):
    count = lax.axis_size(axis_name)
    if count > 4:
        parts, _ = _all_gather(x[None], axis_name, 0)
        return list(jnp.concatenate(parts, axis=0)[1:])
    return [lax.ppermute(x, axis_name, [(i, i ^ p) for i in range(count)]) for p in range(1, count)]


def shards(
    panels,
    panel_slot,
    panel_cell,
    bloch_k,
    leaf_inverse,
    level_left,
    level_right,
    block_left,
    block_right,
    block_coupling,
    rank_count,
    quad_weight,
):
    local_angles = leaf_inverse.shape[0]
    assert local_angles == 1
    row_count = leaf_inverse.shape[2]
    panel_count = panels.shape[1]
    local_sources = panels.shape[2]
    panel_width = panels.shape[4]
    slot_count = row_count // panel_width
    source_count = local_sources * lax.axis_size("ang")
    rank_width = block_right.shape[2]
    levels = level_right.shape[1]

    cell_float = panel_cell[0].astype(jnp.float32)
    own_wave = lax.dynamic_slice_in_dim(bloch_k, lax.axis_index("ang") * local_angles, local_angles, 0)
    theta = own_wave[0, 0] * cell_float[:, 0] + own_wave[0, 1] * cell_float[:, 1]
    own_cos = lax.reduce_precision(jnp.cos(theta), exponent_bits=8, mantissa_bits=7)
    own_sin = lax.reduce_precision(jnp.sin(theta), exponent_bits=8, mantissa_bits=7)

    local_panels = panels[0].reshape(panel_count, local_sources, 2 * panel_width)
    row_blocks = lax.axis_size("row")
    me = lax.axis_index("row")
    coupling = block_coupling[0, 0]
    coupling = coupling.reshape(2, rank_width, row_blocks, coupling.shape[2] // row_blocks)
    offsets = jnp.array(_position_offsets(row_blocks), jnp.int32)
    coupling = jnp.take(coupling, me ^ offsets, axis=2).reshape(block_coupling.shape[2:])
    (first, second), (own_cos, own_sin, coupling) = _all_gather(local_panels, "ang", 1, (own_cos, own_sin, coupling))
    rank = rank_count[0].reshape(1)

    excitation, projected = pl.pallas_call(
        _excite_kernel,
        out_shape=(
            jax.ShapeDtypeStruct((2, source_count, row_count), jnp.bfloat16),
            jax.ShapeDtypeStruct((2, source_count, rank_width), jnp.bfloat16),
        ),
        in_specs=[_SMEM, _SMEM, _SMEM, _SMEM, _VMEM, _VMEM, _VMEM],
        out_specs=(_VMEM, _VMEM),
        scratch_shapes=[
            pltpu.VMEM((slot_count, source_count, panel_width), jnp.float32),
            pltpu.VMEM((slot_count, source_count, panel_width), jnp.float32),
        ],
    )(panel_slot[0], own_cos, own_sin, rank, first, second, block_right[0])
    all_projected = _exchange(projected, "row")

    near = pl.pallas_call(
        _near_kernel,
        out_shape=jax.ShapeDtypeStruct((source_count, 2 * row_count), jnp.float32),
        in_specs=[_VMEM] * 4,
        out_specs=_VMEM,
        scratch_shapes=[
            pltpu.VMEM((2 ** (levels + 1) - 2, 2, source_count, rank_width), jnp.bfloat16),
            pltpu.VMEM((2 * source_count, levels * rank_width), jnp.bfloat16),
        ],
    )(excitation, leaf_inverse[0], level_right[0], level_left[0])

    half = source_count // 2
    halves = []
    for h in (1, 0):
        halves.append(pl.pallas_call(
            _far_kernel,
            out_shape=jax.ShapeDtypeStruct((half, 2 * row_count), jnp.float32),
            grid=(1,),
            in_specs=[
                _SMEM,
                _SMEM,
                pl.BlockSpec((half, 2 * row_count), lambda i, h=h: (h, 0)),
                pl.BlockSpec(block_left.shape[1:], lambda i: (0, 0, 0)),
                pl.BlockSpec(coupling.shape, lambda i: (0, 0, 0)),
            ] + [pl.BlockSpec((2, half, rank_width), lambda i, h=h: (0, h, 0))] * (row_blocks - 1),
            out_specs=pl.BlockSpec((half, 2 * row_count), lambda i: (0, 0)),
            scratch_shapes=[pltpu.VMEM((2, half, rank_width), jnp.bfloat16)],
        )(quad_weight[0], rank, near, block_left[0], coupling, *all_projected))
    return _reduce_scatter(halves[1], halves[0], "ang", (local_sources, 2, row_count))


def solution(mesh):
    placed = (
        P("row", None, "ang", None, None),
        P("row", None),
        P("row", None, None),
        P(),
        P("ang", None, "row", None),
        P("ang", None, None, None, "row"),
        P("ang", None, None, None, "row"),
        P("ang", None, None, "row"),
        P("ang", None, None, "row"),
        P("ang", "row", None, None, None),
        P("ang", "row"),
        P("ang", None),
    )
    return jax.shard_map(
        shards, mesh=mesh, in_specs=placed, out_specs=P("ang", None, "row"), check_vma=False
    )
```

```python
import jax
import jax.numpy as jnp
from jax import lax
from jax.experimental import pallas as pl
from jax.experimental.pallas import tpu as pltpu
from jax.sharding import PartitionSpec as P

LEAF = 256

_SMEM = pl.BlockSpec(memory_space=pltpu.MemorySpace.SMEM)
_VMEM = pl.BlockSpec(memory_space=pltpu.MemorySpace.VMEM)


def _nt(a, b):
    return lax.dot_general(a, b, (((1,), (1,)), ((), ())), preferred_element_type=jnp.float32)


def _nn(a, b):
    return lax.dot_general(a, b, (((1,), (0,)), ((), ())), preferred_element_type=jnp.float32)


def _rank_mask(rank_ref, shape):
    return lax.broadcasted_iota(jnp.int32, shape, 0) < rank_ref[0]


def _excite_kernel(slot_ref, cos_ref, sin_ref, rank_ref, ga_ref, gb_ref, br_ref, e_ref, bp_ref, acc_re, acc_im):
    panel_count, part, width2 = ga_ref.shape
    width = width2 // 2
    slots = acc_re.shape[0]
    acc_re[...] = jnp.zeros(acc_re.shape, jnp.float32)
    acc_im[...] = jnp.zeros(acc_im.shape, jnp.float32)

    def body(q, carry):
        k = slot_ref[q]
        c = cos_ref[q]
        s = sin_ref[q]
        for rows, g_ref in ((slice(0, part), ga_ref), (slice(part, 2 * part), gb_ref)):
            p_re = g_ref[q, :, :width].astype(jnp.float32)
            p_im = g_ref[q, :, width:].astype(jnp.float32)
            acc_re[k, rows] = acc_re[k, rows] + (c * p_re + s * p_im)
            acc_im[k, rows] = acc_im[k, rows] + (c * p_im - s * p_re)
        return carry

    lax.fori_loop(0, panel_count, body, 0, unroll=8)
    for k in range(slots):
        e_ref[0, :, k * width:(k + 1) * width] = acc_re[k].astype(jnp.bfloat16)
        e_ref[1, :, k * width:(k + 1) * width] = acc_im[k].astype(jnp.bfloat16)
    sources = e_ref.shape[1]
    stacked = e_ref[...].reshape(2 * sources, e_ref.shape[2])
    keep = _rank_mask(rank_ref, br_ref.shape[1:])
    zero = jnp.zeros(br_ref.shape[1:], jnp.bfloat16)
    t_re = _nt(stacked, jnp.where(keep, br_ref[0], zero))
    t_im = _nt(stacked, jnp.where(keep, br_ref[1], zero))
    bp_ref[0] = (t_re[:sources] - t_im[sources:]).astype(jnp.bfloat16)
    bp_ref[1] = (t_im[:sources] + t_re[sources:]).astype(jnp.bfloat16)


def _near_kernel(e_ref, leaf_ref, lr_ref, ll_ref, out_ref, pj_ref, pc_ref):
    _, source_count, row_count = e_ref.shape
    levels = lr_ref.shape[0]
    sc = source_count
    stacked = e_ref[...].reshape(2 * sc, row_count)

    first_group = []
    slot = 0
    for j in range(levels):
        node = row_count // 2 ** (j + 1)
        first_group.append(slot)
        for g in range(2 ** (j + 1)):
            cols = slice(g * node, (g + 1) * node)
            ab = stacked[:, cols]
            t_re = _nt(ab, lr_ref[j, 0, :, cols])
            t_im = _nt(ab, lr_ref[j, 1, :, cols])
            pj_ref[slot, 0] = (t_re[:sc] - t_im[sc:]).astype(jnp.bfloat16)
            pj_ref[slot, 1] = (t_im[:sc] + t_re[sc:]).astype(jnp.bfloat16)
            slot += 1

    for l in range(row_count // LEAF):
        cols = slice(l * LEAF, (l + 1) * LEAF)
        ab = stacked[:, cols]
        t_re = _nt(ab, leaf_ref[0, cols, :])
        t_im = _nt(ab, leaf_ref[1, cols, :])
        f_re = t_re[:sc] - t_im[sc:]
        f_im = t_im[:sc] + t_re[sc:]
        rank = pj_ref.shape[3]
        for j in range(levels):
            node = row_count // 2 ** (j + 1)
            g = (l * LEAF) // node
            pc_ref[:, j * rank:(j + 1) * rank] = pj_ref[first_group[j] + (g ^ 1)].reshape(2 * sc, rank)
        pp = pc_ref[...]
        v_re = _nn(pp, ll_ref[:, 0, :, cols].reshape(levels * rank, LEAF))
        v_im = _nn(pp, ll_ref[:, 1, :, cols].reshape(levels * rank, LEAF))
        f_re = f_re + (v_re[:sc] - v_im[sc:])
        f_im = f_im + (v_im[:sc] + v_re[sc:])
        out_ref[:, cols] = f_re
        out_ref[:, row_count + l * LEAF:row_count + (l + 1) * LEAF] = f_im


def _far_kernel(qw_ref, rank_ref, near_ref, bl_ref, cp_ref, *refs):
    part_refs = refs[:-3]
    out_ref, cu_ref, bc_ref = refs[-3:]
    source_count = near_ref.shape[0]
    row_count = bl_ref.shape[2]
    rank_width = bl_ref.shape[1]
    blocks = len(part_refs) + 1
    coupling_rank = part_refs[0].shape[2]

    sc = source_count
    for u in range(1, blocks):
        bc_ref[:, (u - 1) * coupling_rank:u * coupling_rank] = part_refs[u - 1][...].reshape(2 * sc, coupling_rank)
    bb = bc_ref[...]
    t_re = _nt(bb, cp_ref[0, :, coupling_rank:])
    t_im = _nt(bb, cp_ref[1, :, coupling_rank:])
    c_re = t_re[:sc] - t_im[sc:]
    c_im = t_im[:sc] + t_re[sc:]
    cu_ref[0] = c_re.astype(jnp.bfloat16)
    cu_ref[1] = c_im.astype(jnp.bfloat16)
    coupled = cu_ref[...].reshape(2 * sc, rank_width)

    w_re = qw_ref[0]
    w_im = qw_ref[1]
    keep = _rank_mask(rank_ref, (rank_width, LEAF))
    zero = jnp.zeros((rank_width, LEAF), jnp.bfloat16)
    for l in range(row_count // LEAF):
        cols = slice(l * LEAF, (l + 1) * LEAF)
        imag_cols = slice(row_count + l * LEAF, row_count + (l + 1) * LEAF)
        q_re = jnp.where(keep, bl_ref[0, :, cols], zero)
        q_im = jnp.where(keep, bl_ref[1, :, cols], zero)
        v_re = _nn(coupled, q_re)
        v_im = _nn(coupled, q_im)
        f_re = near_ref[:, cols] + (v_re[:sc] - v_im[sc:])
        f_im = near_ref[:, imag_cols] + (v_im[:sc] + v_re[sc:])
        out_ref[:, cols] = w_re * f_re - w_im * f_im
        out_ref[:, imag_cols] = w_re * f_im + w_im * f_re


def _bit_groups(count):
    bits = count.bit_length() - 1
    groups = [[b, b - 1] for b in range(bits - 1, 1, -2)]
    rest = [b for b in range(bits) if all(b not in g for g in groups)]
    return groups + [[b] for b in rest[::-1]]


def _offset(value, group):
    return sum(1 << b for k, b in enumerate(group) if (value >> k) & 1)


def _permute(x, axis_name, count, offset):
    return lax.ppermute(x, axis_name, [(i, i ^ offset) for i in range(count)])


def _all_gather(x, axis_name, axis, companions=()):
    count = lax.axis_size(axis_name)
    groups = _bit_groups(count)
    current = x
    for step, group in enumerate(groups):
        if step == 1 and companions:
            current, companions = lax.optimization_barrier((current, companions))
        parts = [current] + [_permute(current, axis_name, count, _offset(j, group)) for j in range(1, 2 ** len(group))]
        if step == len(groups) - 1:
            return parts, companions
        current = jnp.concatenate(parts, axis=axis)


def _reduce_scatter(keep, give, axis_name, shape):
    count = lax.axis_size(axis_name)
    groups = _bit_groups(count)
    flat = sum(groups, [])

    def offset_of(position):
        return sum(1 << flat[k] for k in range(len(flat)) if (position >> k) & 1)

    chunks = 2 * keep.shape[0] // shape[0]
    current = keep + _permute(give, axis_name, count, offset_of(chunks // 2))
    chunks //= 2
    for group in groups[::-1][1:]:
        size = 2 ** len(group)
        block = chunks // size
        rows = block * shape[0]
        total = current[:rows]
        for t in range(1, size):
            part = current[t * rows:(t + 1) * rows]
            total = total + _permute(part, axis_name, count, offset_of(t * block))
        current = total
        chunks = block
    return current.reshape(shape)


def _position_offsets(count):
    if count <= 4:
        return list(range(count))
    flat = sum(_bit_groups(count), [])
    return [sum(1 << flat[k] for k in range(len(flat)) if (p >> k) & 1) for p in range(count)]


def _exchange(x, axis_name):
    count = lax.axis_size(axis_name)
    if count > 4:
        parts, _ = _all_gather(x[None], axis_name, 0)
        return list(jnp.concatenate(parts, axis=0)[1:])
    return [lax.ppermute(x, axis_name, [(i, i ^ p) for i in range(count)]) for p in range(1, count)]


def shards(
    panels,
    panel_slot,
    panel_cell,
    bloch_k,
    leaf_inverse,
    level_left,
    level_right,
    block_left,
    block_right,
    block_coupling,
    rank_count,
    quad_weight,
):
    local_angles = leaf_inverse.shape[0]
    assert local_angles == 1
    row_count = leaf_inverse.shape[2]
    panel_count = panels.shape[1]
    local_sources = panels.shape[2]
    panel_width = panels.shape[4]
    slot_count = row_count // panel_width
    source_count = local_sources * lax.axis_size("ang")
    rank_width = block_right.shape[2]
    levels = level_right.shape[1]

    cell_float = panel_cell[0].astype(jnp.float32)
    own_wave = lax.dynamic_slice_in_dim(bloch_k, lax.axis_index("ang") * local_angles, local_angles, 0)
    theta = own_wave[0, 0] * cell_float[:, 0] + own_wave[0, 1] * cell_float[:, 1]
    own_cos = lax.reduce_precision(jnp.cos(theta), exponent_bits=8, mantissa_bits=7)
    own_sin = lax.reduce_precision(jnp.sin(theta), exponent_bits=8, mantissa_bits=7)

    local_panels = panels[0].reshape(panel_count, local_sources, 2 * panel_width)
    row_blocks = lax.axis_size("row")
    me = lax.axis_index("row")
    coupling = block_coupling[0, 0]
    coupling = coupling.reshape(2, rank_width, row_blocks, coupling.shape[2] // row_blocks)
    offsets = jnp.array(_position_offsets(row_blocks), jnp.int32)
    coupling = jnp.take(coupling, me ^ offsets, axis=2).reshape(block_coupling.shape[2:])
    (first, second), (own_cos, own_sin, coupling) = _all_gather(local_panels, "ang", 1, (own_cos, own_sin, coupling))
    rank = rank_count[0].reshape(1)

    excitation, projected = pl.pallas_call(
        _excite_kernel,
        out_shape=(
            jax.ShapeDtypeStruct((2, source_count, row_count), jnp.bfloat16),
            jax.ShapeDtypeStruct((2, source_count, rank_width), jnp.bfloat16),
        ),
        in_specs=[_SMEM, _SMEM, _SMEM, _SMEM, _VMEM, _VMEM, _VMEM],
        out_specs=(_VMEM, _VMEM),
        scratch_shapes=[
            pltpu.VMEM((slot_count, source_count, panel_width), jnp.float32),
            pltpu.VMEM((slot_count, source_count, panel_width), jnp.float32),
        ],
    )(panel_slot[0], own_cos, own_sin, rank, first, second, block_right[0])
    all_projected = _exchange(projected, "row")

    near = pl.pallas_call(
        _near_kernel,
        out_shape=jax.ShapeDtypeStruct((source_count, 2 * row_count), jnp.float32),
        in_specs=[_VMEM] * 4,
        out_specs=_VMEM,
        scratch_shapes=[
            pltpu.VMEM((2 ** (levels + 1) - 2, 2, source_count, rank_width), jnp.bfloat16),
            pltpu.VMEM((2 * source_count, levels * rank_width), jnp.bfloat16),
        ],
    )(excitation, leaf_inverse[0], level_right[0], level_left[0])

    half = source_count // 2
    halves = []
    for h in (1, 0):
        halves.append(pl.pallas_call(
            _far_kernel,
            out_shape=jax.ShapeDtypeStruct((half, 2 * row_count), jnp.float32),
            grid=(1,),
            in_specs=[
                _SMEM,
                _SMEM,
                pl.BlockSpec((half, 2 * row_count), lambda i, h=h: (h, 0)),
                pl.BlockSpec(block_left.shape[1:], lambda i: (0, 0, 0)),
                pl.BlockSpec(coupling.shape, lambda i: (0, 0, 0)),
            ] + [pl.BlockSpec((2, half, rank_width), lambda i, h=h: (0, h, 0))] * (row_blocks - 1),
            out_specs=pl.BlockSpec((half, 2 * row_count), lambda i: (0, 0)),
            scratch_shapes=[
                pltpu.VMEM((2, half, rank_width), jnp.bfloat16),
                pltpu.VMEM((2 * half, (row_blocks - 1) * rank_width), jnp.bfloat16),
            ],
        )(quad_weight[0], rank, near, block_left[0], coupling, *all_projected))
    return _reduce_scatter(halves[1], halves[0], "ang", (local_sources, 2, row_count))


def solution(mesh):
    placed = (
        P("row", None, "ang", None, None),
        P("row", None),
        P("row", None, None),
        P(),
        P("ang", None, "row", None),
        P("ang", None, None, None, "row"),
        P("ang", None, None, None, "row"),
        P("ang", None, None, "row"),
        P("ang", None, None, "row"),
        P("ang", "row", None, None, None),
        P("ang", "row"),
        P("ang", None),
    )
    return jax.shard_map(
        shards, mesh=mesh, in_specs=placed, out_specs=P("ang", None, "row"), check_vma=False
    )
```

```python
import jax
import jax.numpy as jnp
from jax import lax
from jax.experimental import pallas as pl
from jax.experimental.pallas import tpu as pltpu
from jax.sharding import PartitionSpec as P

LEAF = 256

_SMEM = pl.BlockSpec(memory_space=pltpu.MemorySpace.SMEM)
_VMEM = pl.BlockSpec(memory_space=pltpu.MemorySpace.VMEM)


def _nt(a, b):
    return lax.dot_general(a, b, (((1,), (1,)), ((), ())), preferred_element_type=jnp.float32)


def _nn(a, b):
    return lax.dot_general(a, b, (((1,), (0,)), ((), ())), preferred_element_type=jnp.float32)


def _rank_mask(rank_ref, shape):
    return lax.broadcasted_iota(jnp.int32, shape, 0) < rank_ref[0]


def _excite_kernel(slot_ref, cos_ref, sin_ref, rank_ref, ga_ref, gb_ref, br_ref, e_ref, bp_ref, acc_re, acc_im):
    panel_count, part, width2 = ga_ref.shape
    width = width2 // 2
    slots = acc_re.shape[0]
    acc_re[...] = jnp.zeros(acc_re.shape, jnp.float32)
    acc_im[...] = jnp.zeros(acc_im.shape, jnp.float32)

    def body(q, carry):
        k = slot_ref[q]
        c = cos_ref[q]
        s = sin_ref[q]
        for rows, g_ref in ((slice(0, part), ga_ref), (slice(part, 2 * part), gb_ref)):
            p_re = g_ref[q, :, :width].astype(jnp.float32)
            p_im = g_ref[q, :, width:].astype(jnp.float32)
            acc_re[k, rows] = acc_re[k, rows] + (c * p_re + s * p_im)
            acc_im[k, rows] = acc_im[k, rows] + (c * p_im - s * p_re)
        return carry

    lax.fori_loop(0, panel_count, body, 0, unroll=8)
    for k in range(slots):
        e_ref[0, :, k * width:(k + 1) * width] = acc_re[k].astype(jnp.bfloat16)
        e_ref[1, :, k * width:(k + 1) * width] = acc_im[k].astype(jnp.bfloat16)
    sources = e_ref.shape[1]
    stacked = e_ref[...].reshape(2 * sources, e_ref.shape[2])
    keep = _rank_mask(rank_ref, br_ref.shape[1:])
    zero = jnp.zeros(br_ref.shape[1:], jnp.bfloat16)
    t_re = _nt(stacked, jnp.where(keep, br_ref[0], zero))
    t_im = _nt(stacked, jnp.where(keep, br_ref[1], zero))
    bp_ref[0] = (t_re[:sources] - t_im[sources:]).astype(jnp.bfloat16)
    bp_ref[1] = (t_im[:sources] + t_re[sources:]).astype(jnp.bfloat16)


def _near_kernel(e_ref, leaf_ref, lr_ref, ll_ref, out_ref, pj_ref, pc_ref):
    _, source_count, row_count = e_ref.shape
    levels = lr_ref.shape[0]
    sc = source_count
    stacked = e_ref[...].reshape(2 * sc, row_count)

    rank = lr_ref.shape[2]
    first_group = []
    slot = 0
    for j in range(levels):
        first_group.append(slot)
        slot += 2 ** (j + 1)
    sums = {}
    for l in range(row_count // LEAF):
        cols = slice(l * LEAF, (l + 1) * LEAF)
        ab = stacked[:, cols]
        t_re = _nt(ab, lr_ref[:, 0, :, cols].reshape(levels * rank, LEAF))
        t_im = _nt(ab, lr_ref[:, 1, :, cols].reshape(levels * rank, LEAF))
        for j in range(levels):
            key = first_group[j] + (l * LEAF) // (row_count // 2 ** (j + 1))
            pair = (t_re[:, j * rank:(j + 1) * rank], t_im[:, j * rank:(j + 1) * rank])
            sums[key] = pair if key not in sums else (sums[key][0] + pair[0], sums[key][1] + pair[1])
    for key, (u_re, u_im) in sums.items():
        pj_ref[key, 0] = (u_re[:sc] - u_im[sc:]).astype(jnp.bfloat16)
        pj_ref[key, 1] = (u_im[:sc] + u_re[sc:]).astype(jnp.bfloat16)

    for l in range(row_count // LEAF):
        cols = slice(l * LEAF, (l + 1) * LEAF)
        ab = stacked[:, cols]
        t_re = _nt(ab, leaf_ref[0, cols, :])
        t_im = _nt(ab, leaf_ref[1, cols, :])
        f_re = t_re[:sc] - t_im[sc:]
        f_im = t_im[:sc] + t_re[sc:]
        for j in range(levels):
            node = row_count // 2 ** (j + 1)
            g = (l * LEAF) // node
            pc_ref[:, j * rank:(j + 1) * rank] = pj_ref[first_group[j] + (g ^ 1)].reshape(2 * sc, rank)
        pp = pc_ref[...]
        v_re = _nn(pp, ll_ref[:, 0, :, cols].reshape(levels * rank, LEAF))
        v_im = _nn(pp, ll_ref[:, 1, :, cols].reshape(levels * rank, LEAF))
        f_re = f_re + (v_re[:sc] - v_im[sc:])
        f_im = f_im + (v_im[:sc] + v_re[sc:])
        out_ref[:, cols] = f_re
        out_ref[:, row_count + l * LEAF:row_count + (l + 1) * LEAF] = f_im


def _far_kernel(qw_ref, rank_ref, near_ref, bl_ref, cp_ref, *refs):
    part_refs = refs[:-2]
    out_ref, cu_ref = refs[-2:]
    source_count = near_ref.shape[0]
    row_count = bl_ref.shape[2]
    rank_width = bl_ref.shape[1]
    blocks = len(part_refs) + 1
    coupling_rank = part_refs[0].shape[2]

    c_re = jnp.zeros((source_count, rank_width), jnp.float32)
    c_im = jnp.zeros((source_count, rank_width), jnp.float32)
    sc = source_count
    for u in range(1, blocks):
        bb = part_refs[u - 1][...].reshape(2 * sc, coupling_rank)
        t_re = _nt(bb, cp_ref[0, :, u * coupling_rank:(u + 1) * coupling_rank])
        t_im = _nt(bb, cp_ref[1, :, u * coupling_rank:(u + 1) * coupling_rank])
        c_re = c_re + (t_re[:sc] - t_im[sc:])
        c_im = c_im + (t_im[:sc] + t_re[sc:])
    cu_ref[0] = c_re.astype(jnp.bfloat16)
    cu_ref[1] = c_im.astype(jnp.bfloat16)
    coupled = cu_ref[...].reshape(2 * sc, rank_width)

    w_re = qw_ref[0]
    w_im = qw_ref[1]
    for l in range(row_count // LEAF):
        cols = slice(l * LEAF, (l + 1) * LEAF)
        imag_cols = slice(row_count + l * LEAF, row_count + (l + 1) * LEAF)
        keep = _rank_mask(rank_ref, (rank_width, LEAF))
        zero = jnp.zeros((rank_width, LEAF), jnp.bfloat16)
        q_re = jnp.where(keep, bl_ref[0, :, cols], zero)
        q_im = jnp.where(keep, bl_ref[1, :, cols], zero)
        v_re = _nn(coupled, q_re)
        v_im = _nn(coupled, q_im)
        f_re = near_ref[:, cols] + (v_re[:sc] - v_im[sc:])
        f_im = near_ref[:, imag_cols] + (v_im[:sc] + v_re[sc:])
        out_ref[:, cols] = w_re * f_re - w_im * f_im
        out_ref[:, imag_cols] = w_re * f_im + w_im * f_re


def _bit_groups(count):
    bits = count.bit_length() - 1
    groups = [[b, b - 1] for b in range(bits - 1, 1, -2)]
    rest = [b for b in range(bits) if all(b not in g for g in groups)]
    return groups + [[b] for b in rest[::-1]]


def _offset(value, group):
    return sum(1 << b for k, b in enumerate(group) if (value >> k) & 1)


def _permute(x, axis_name, count, offset):
    return lax.ppermute(x, axis_name, [(i, i ^ offset) for i in range(count)])


def _all_gather(x, axis_name, axis, companions=()):
    count = lax.axis_size(axis_name)
    groups = _bit_groups(count)
    current = x
    for step, group in enumerate(groups):
        if step == 1 and companions:
            current, companions = lax.optimization_barrier((current, companions))
        parts = [current] + [_permute(current, axis_name, count, _offset(j, group)) for j in range(1, 2 ** len(group))]
        if step == len(groups) - 1:
            return parts, companions
        current = jnp.concatenate(parts, axis=axis)


def _reduce_scatter(keep, give, axis_name, shape):
    count = lax.axis_size(axis_name)
    groups = _bit_groups(count)
    flat = sum(groups, [])

    def offset_of(position):
        return sum(1 << flat[k] for k in range(len(flat)) if (position >> k) & 1)

    chunks = 2 * keep.shape[0] // shape[0]
    current = keep + _permute(give, axis_name, count, offset_of(chunks // 2))
    chunks //= 2
    for group in groups[::-1][1:]:
        size = 2 ** len(group)
        block = chunks // size
        rows = block * shape[0]
        total = current[:rows]
        for t in range(1, size):
            part = current[t * rows:(t + 1) * rows]
            total = total + _permute(part, axis_name, count, offset_of(t * block))
        current = total
        chunks = block
    return current.reshape(shape)


def _position_offsets(count):
    if count <= 4:
        return list(range(count))
    flat = sum(_bit_groups(count), [])
    return [sum(1 << flat[k] for k in range(len(flat)) if (p >> k) & 1) for p in range(count)]


def _exchange(x, axis_name):
    count = lax.axis_size(axis_name)
    if count > 4:
        parts, _ = _all_gather(x[None], axis_name, 0)
        return list(jnp.concatenate(parts, axis=0)[1:])
    return [lax.ppermute(x, axis_name, [(i, i ^ p) for i in range(count)]) for p in range(1, count)]


def shards(
    panels,
    panel_slot,
    panel_cell,
    bloch_k,
    leaf_inverse,
    level_left,
    level_right,
    block_left,
    block_right,
    block_coupling,
    rank_count,
    quad_weight,
):
    local_angles = leaf_inverse.shape[0]
    assert local_angles == 1
    row_count = leaf_inverse.shape[2]
    panel_count = panels.shape[1]
    local_sources = panels.shape[2]
    panel_width = panels.shape[4]
    slot_count = row_count // panel_width
    source_count = local_sources * lax.axis_size("ang")
    rank_width = block_right.shape[2]
    levels = level_right.shape[1]

    cell_float = panel_cell[0].astype(jnp.float32)
    own_wave = lax.dynamic_slice_in_dim(bloch_k, lax.axis_index("ang") * local_angles, local_angles, 0)
    theta = own_wave[0, 0] * cell_float[:, 0] + own_wave[0, 1] * cell_float[:, 1]
    own_cos = lax.reduce_precision(jnp.cos(theta), exponent_bits=8, mantissa_bits=7)
    own_sin = lax.reduce_precision(jnp.sin(theta), exponent_bits=8, mantissa_bits=7)

    local_panels = panels[0].reshape(panel_count, local_sources, 2 * panel_width)
    row_blocks = lax.axis_size("row")
    me = lax.axis_index("row")
    coupling = block_coupling[0, 0]
    coupling = coupling.reshape(2, rank_width, row_blocks, coupling.shape[2] // row_blocks)
    offsets = jnp.array(_position_offsets(row_blocks), jnp.int32)
    coupling = jnp.take(coupling, me ^ offsets, axis=2).reshape(block_coupling.shape[2:])
    (first, second), (own_cos, own_sin, coupling) = _all_gather(local_panels, "ang", 1, (own_cos, own_sin, coupling))
    rank = rank_count[0].reshape(1)

    excitation, projected = pl.pallas_call(
        _excite_kernel,
        out_shape=(
            jax.ShapeDtypeStruct((2, source_count, row_count), jnp.bfloat16),
            jax.ShapeDtypeStruct((2, source_count, rank_width), jnp.bfloat16),
        ),
        in_specs=[_SMEM, _SMEM, _SMEM, _SMEM, _VMEM, _VMEM, _VMEM],
        out_specs=(_VMEM, _VMEM),
        scratch_shapes=[
            pltpu.VMEM((slot_count, source_count, panel_width), jnp.float32),
            pltpu.VMEM((slot_count, source_count, panel_width), jnp.float32),
        ],
    )(panel_slot[0], own_cos, own_sin, rank, first, second, block_right[0])
    all_projected = _exchange(projected, "row")

    near = pl.pallas_call(
        _near_kernel,
        out_shape=jax.ShapeDtypeStruct((source_count, 2 * row_count), jnp.float32),
        in_specs=[_VMEM] * 4,
        out_specs=_VMEM,
        scratch_shapes=[
            pltpu.VMEM((2 ** (levels + 1) - 2, 2, source_count, rank_width), jnp.bfloat16),
            pltpu.VMEM((2 * source_count, levels * rank_width), jnp.bfloat16),
        ],
    )(excitation, leaf_inverse[0], level_right[0], level_left[0])

    half = source_count // 2
    halves = []
    for h in (1, 0):
        halves.append(pl.pallas_call(
            _far_kernel,
            out_shape=jax.ShapeDtypeStruct((half, 2 * row_count), jnp.float32),
            grid=(1,),
            in_specs=[
                _SMEM,
                _SMEM,
                pl.BlockSpec((half, 2 * row_count), lambda i, h=h: (h, 0)),
                pl.BlockSpec(block_left.shape[1:], lambda i: (0, 0, 0)),
                pl.BlockSpec(coupling.shape, lambda i: (0, 0, 0)),
            ] + [pl.BlockSpec((2, half, rank_width), lambda i, h=h: (0, h, 0))] * (row_blocks - 1),
            out_specs=pl.BlockSpec((half, 2 * row_count), lambda i: (0, 0)),
            scratch_shapes=[pltpu.VMEM((2, half, rank_width), jnp.bfloat16)],
        )(quad_weight[0], rank, near, block_left[0], coupling, *all_projected))
    return _reduce_scatter(halves[1], halves[0], "ang", (local_sources, 2, row_count))


def solution(mesh):
    placed = (
        P("row", None, "ang", None, None),
        P("row", None),
        P("row", None, None),
        P(),
        P("ang", None, "row", None),
        P("ang", None, None, None, "row"),
        P("ang", None, None, None, "row"),
        P("ang", None, None, "row"),
        P("ang", None, None, "row"),
        P("ang", "row", None, None, None),
        P("ang", "row"),
        P("ang", None),
    )
    return jax.shard_map(
        shards, mesh=mesh, in_specs=placed, out_specs=P("ang", None, "row"), check_vma=False
    )
```
